128 devices in a mesh: wide: 32 (over y, z, core), narrow: 4 (over x).
Axes of the slice: x: 4, y: 4, z: 4, core: 2. Of those that a mesh axis runs over, the one named last changes fastest.
Arguments:
- sources: bfloat16 [32768, 768], P('wide'), may hold values from -8 to 8
- targets: bfloat16 [262144, 768], P(('wide', 'narrow')), may hold values from -8 to 8
- pair_target: int32 [32, 12], replicated, may hold values from 0 to 255, as said below
- pair_count: int32 [32], replicated, may hold values from 8 to 12
Outputs:
- source_potential: float32 [32768], P('wide')
- target_potential: float32 [262144], P(('wide', 'narrow'))
- mapped: bfloat16 [32768, 768], P('wide')
The draws below stay inside these ranges and needn't reach their ends.
Inputs may be any that keep to these rules, and one draw needn't show every extreme that they name: `pair_target`: source block s lies in row group w = s. Its slots k < 8 hold w * 8 + k, so every target block is paired with some source block. Its other 4 slots hold distinct target blocks of groups w - 1 and w + 1 (taken modulo the number of groups); slot 8 + m holds a block whose position within its group, divided by 2 and rounded down, equals m modulo (4).
All inputs are finite; a program needn't handle non-finite values.
Results may differ from the reference program's by a relative error of at most 0.0044.
Values may be sent and summed in bfloat16 or wider, within the bound.
No kernel may reach another device: no remote copies, remote signals or barrier semaphores. Data moves between devices by JAX's collectives and lax.ppermute only.
A program may use at most 192 MiB of HBM per device.

```python
import math
import jax
import jax.numpy as jnp
from jax import lax

D = 768
BLK = 1024
TB_DEV = 2
SB_DEV = 1
EXTRA = 4
ITERS = 2
TBG = 8
COVER = 8
NSB = 32
NTB = 256
NS = 32768
NT = 262144


def target_values(key, row_ids):
    base_key = jax.random.fold_in(key, 11)

    def draw_row(row_index):
        row_key = jax.random.fold_in(base_key, row_index)
        return jnp.clip(jax.random.normal(row_key, (D,), jnp.float32), -6.0, 6.0)
    return jax.vmap(draw_row)(row_ids)


def draw_targets(key, part):
    row_ids = jnp.arange(NT, dtype=jnp.int32)
    return target_values(key, row_ids).astype(jnp.bfloat16)


def draw_sources(key, part):
    source_key = jax.random.fold_in(key, 23)
    return jnp.clip(jax.random.normal(source_key, (NS, D), jnp.float32), -6.0, 6.0).astype(jnp.bfloat16)


def draw_pair_count(key, part):
    first_key = jax.random.fold_in(key, 31)
    second_key = jax.random.fold_in(key, 32)
    chosen_key = jax.random.fold_in(key, 33)
    extra_count = jnp.minimum(jax.random.randint(first_key, (NSB,), 0, EXTRA + 1), jax.random.randint(second_key, (NSB,), 0, EXTRA + 1))
    chosen = jax.random.randint(chosen_key, (), 0, NSB)
    block_ids = jnp.arange(NSB, dtype=jnp.int32)
    counts = COVER + extra_count
    counts = jnp.where(block_ids == chosen, COVER + EXTRA, counts)
    counts = jnp.where(block_ids == (chosen + 1) % NSB, COVER, counts)
    return counts.astype(jnp.int32)


def draw_pair_target(key, part):
    block_ids = jnp.arange(NSB, dtype=jnp.int32)
    group_ids = block_ids // SB_DEV
    within = block_ids % SB_DEV
    cover_ids = group_ids[:, None] * TBG + within[:, None] * COVER + jnp.arange(COVER, dtype=jnp.int32)[None, :]
    columns = TBG // TB_DEV
    choices_count = 2 * TB_DEV
    scores = jax.random.randint(jax.random.fold_in(key, 41), (NSB, columns, choices_count), 0, 1 << 20) * choices_count + jnp.arange(choices_count, dtype=jnp.int32)[None, None, :]
    order = jnp.argsort(scores, axis=2).astype(jnp.int32)
    slot_ids = jnp.arange(EXTRA, dtype=jnp.int32)
    slot_column = slot_ids % columns
    slot_rank = slot_ids // columns
    picked = order[:, slot_column, slot_rank]
    group_count = NSB // SB_DEV
    side_shift = jnp.where(picked < TB_DEV, -1, 1)
    owner_group = (group_ids[:, None] + side_shift + group_count) % group_count
    extra_ids = owner_group * TBG + slot_column[None, :] * TB_DEV + picked % TB_DEV
    return jnp.concatenate([cover_ids, extra_ids], axis=1).astype(jnp.int32)


def setup_inputs(seed: int = 0) -> dict:
    keys = jax.random.split(jax.random.key(seed), 5)
    sources = draw_sources(jax.random.fold_in(keys[4], 71), 0)
    targets = draw_targets(jax.random.fold_in(keys[4], 71), 0)
    pair_target = draw_pair_target(jax.random.fold_in(keys[4], 71), 0)
    pair_count = draw_pair_count(jax.random.fold_in(keys[4], 71), 0)
    return dict(sources=sources, targets=targets, pair_target=pair_target, pair_count=pair_count)


epsilon = 0.25
sentinel = -1e+30

def block_products(sources, targets, pair_target):
    source_view = sources.reshape(NSB, BLK, D)
    target_view = targets.reshape(NTB, BLK, D)

    def per_block(block_index):
        row_block = source_view[block_index].astype(jnp.float32)
        col_blocks = target_view[pair_target[block_index]].astype(jnp.float32)
        return jnp.einsum('rd,pcd->prc', row_block, col_blocks)
    return lax.map(per_block, jnp.arange(NSB, dtype=jnp.int32))

def row_scores(product, potential, alive):
    inv_root = 1.0 / math.sqrt(D)
    scores = (potential[:, None, :] + product * inv_root) * (1.0 / epsilon)
    return jnp.where(alive[:, None, None], scores, sentinel)

def row_lse(products, pair_target, live_slots, target_pot):
    pot_blocks = target_pot.reshape(NTB, BLK)[pair_target]

    def per_block(inputs):
        product, potential, alive = inputs
        scores = row_scores(product, potential, alive)
        highest = lax.optimization_barrier(jnp.max(scores, axis=(0, 2)))
        return highest + jnp.log(lax.optimization_barrier(jnp.sum(jnp.exp(scores - highest[None, :, None]), axis=(0, 2))))
    return lax.map(per_block, (products, pot_blocks, live_slots)).reshape(-1)

def col_lse(products, pair_target, live_slots, source_pot):
    inv_root = 1.0 / math.sqrt(D)
    source_rows = source_pot.reshape(NSB, BLK)

    def per_block(inputs):
        product, potential, alive = inputs
        scores = (potential[None, :, None] + product * inv_root) * (1.0 / epsilon)
        highest = lax.optimization_barrier(jnp.max(scores, axis=1))
        partial_value = highest + jnp.log(lax.optimization_barrier(jnp.sum(jnp.exp(scores - highest[:, None, :]), axis=1)))
        return jnp.where(alive[:, None], partial_value, sentinel)
    partials = lax.map(per_block, (products, source_rows, live_slots))
    flat = partials.reshape(-1, BLK)
    block_ids = pair_target.reshape(-1)

    def per_target(target_index):
        member = block_ids == target_index
        highest = lax.optimization_barrier(jnp.max(jnp.where(member[:, None], flat, sentinel), axis=0))
        shifted = jnp.where(member[:, None], flat - highest[None, :], sentinel)
        return highest + jnp.log(lax.optimization_barrier(jnp.sum(jnp.exp(shifted), axis=0)))
    return lax.map(per_target, jnp.arange(NTB, dtype=jnp.int32)).reshape(-1)

def reference(sources, targets, pair_target, pair_count):
    slots = pair_target.shape[1]
    live_slots = jnp.arange(slots, dtype=jnp.int32)[None, :] < pair_count[:, None]
    products = block_products(sources, targets, pair_target)
    target_pot = jnp.zeros((NT,), jnp.float32)
    for iteration in range(ITERS):
        source_pot = epsilon * (-math.log(NS) - row_lse(products, pair_target, live_slots, target_pot))
        target_pot = epsilon * (-math.log(NT) - col_lse(products, pair_target, live_slots, source_pot))
    final_lse = row_lse(products, pair_target, live_slots, target_pot)
    source_pot = epsilon * (-math.log(NS) - final_lse)
    pot_blocks = target_pot.reshape(NTB, BLK)[pair_target]
    lse_blocks = final_lse.reshape(NSB, BLK)
    target_view = targets.reshape(NTB, BLK, D)

    def per_block(inputs):
        product, potential, alive, lse_rows, block_index = inputs
        scores = row_scores(product, potential, alive)
        weights = jnp.where(alive[:, None, None], jnp.exp(scores - lse_rows[None, :, None]), 0.0)
        weights = lax.optimization_barrier(weights.astype(jnp.bfloat16)).astype(jnp.float32)
        col_blocks = target_view[pair_target[block_index]].astype(jnp.float32)
        return jnp.einsum('prc,pcd->rd', weights, col_blocks)
    numer = lax.map(per_block, (products, pot_blocks, live_slots, lse_blocks, jnp.arange(NSB, dtype=jnp.int32)))
    mapped = numer.reshape(NS, D).astype(jnp.bfloat16)
    return (source_pot, target_pot, mapped)
```

```python
import math

import jax
import jax.numpy as jnp
from jax import lax
from jax.sharding import PartitionSpec as P

BLK = 1024
ITERS = 2


epsilon = 0.25
sentinel = -1e30


def shifted(x, axis, distance):
    size = lax.axis_size(axis)
    route = [(i, (i + distance) % size) for i in range(size)]
    return lax.ppermute(x, axis, route)


def lse_rows(scores):
    top = jnp.max(scores, axis=1)
    return top + jnp.log(jnp.sum(jnp.exp(scores - top[:, None]), axis=1))


def lse_cols(scores):
    top = jnp.max(scores, axis=0)
    return top + jnp.log(jnp.sum(jnp.exp(scores - top[None, :]), axis=0))


def narrow_lse(partial_value, column, narrow_count):
    pieces = [partial_value] + [shifted(partial_value, "narrow", k) for k in range(1, narrow_count)]
    stacked = jnp.stack(pieces)
    order = (column - jnp.arange(narrow_count, dtype=jnp.int32)) % narrow_count
    ordered = stacked[order]
    top = jnp.max(ordered, axis=0)
    return top + jnp.log(jnp.sum(jnp.exp(ordered - top[None, :]), axis=0))


def shards(sources, targets, pair_target, pair_count):
    feature_count = sources.shape[1]
    tgt_blocks = targets.shape[0] // BLK
    wide_count = lax.axis_size("wide")
    narrow_count = lax.axis_size("narrow")
    w = lax.axis_index("wide")
    c = lax.axis_index("narrow")
    group_blocks = tgt_blocks * narrow_count
    scale = (1.0 / math.sqrt(feature_count)) * (1.0 / epsilon)
    inv_eps = 1.0 / epsilon
    log_src = -math.log(wide_count * sources.shape[0])
    log_tgt = -math.log(wide_count * narrow_count * targets.shape[0])

    left = (w - 1 + wide_count) % wide_count
    right = (w + 1) % wide_count
    slot = group_blocks + c

    mine = pair_target[w, slot]
    mine_live = pair_count[w] > slot
    mine_from_left = (mine // group_blocks) == left

    want_right = pair_target[right, slot]
    want_right_live = (pair_count[right] > slot) & ((want_right // group_blocks) == w)
    want_left = pair_target[left, slot]
    want_left_live = (pair_count[left] > slot) & ((want_left // group_blocks) == w)

    blocks = targets.reshape(tgt_blocks, BLK, feature_count)
    to_right = blocks[want_right % tgt_blocks]
    to_left = blocks[want_left % tgt_blocks]
    from_left = shifted(to_right, "wide", 1)
    from_right = shifted(to_left, "wide", -1)

    own = lax.dot_general(
        sources, targets, (((1,), (1,)), ((), ())), preferred_element_type=jnp.float32
    ) * scale
    extra = jnp.where(mine_from_left, from_left, from_right)
    extra_dots = lax.dot_general(
        sources, extra, (((1,), (1,)), ((), ())), preferred_element_type=jnp.float32
    ) * scale
    z = jnp.concatenate([own, extra_dots], axis=1)

    extra_mask = jnp.where(mine_live, 0.0, sentinel).astype(jnp.float32)

    def row_lse(g_own, g_extra):
        gs = jnp.concatenate([g_own * inv_eps, g_extra * inv_eps + extra_mask])
        return narrow_lse(lse_rows(z + gs[None, :]), c, narrow_count)

    g_own = jnp.zeros((tgt_blocks * BLK,), jnp.float32)
    g_extra = jnp.zeros((BLK,), jnp.float32)
    for iteration in range(ITERS):
        row = row_lse(g_own, g_extra)
        f = epsilon * (log_src - row)
        cols = lse_cols(z + (f * inv_eps)[:, None])
        own_cols = cols[: tgt_blocks * BLK].reshape(tgt_blocks, BLK)
        extra_cols = jnp.where(mine_live, cols[tgt_blocks * BLK:], sentinel)
        back_from_right = shifted(extra_cols, "wide", -1)
        back_from_left = shifted(extra_cols, "wide", 1)
        ids = jnp.arange(tgt_blocks, dtype=jnp.int32)[:, None]
        add_right = jnp.where(want_right_live & (ids == want_right % tgt_blocks), back_from_right[None, :], sentinel)
        add_left = jnp.where(want_left_live & (ids == want_left % tgt_blocks), back_from_left[None, :], sentinel)
        top = jnp.maximum(own_cols, jnp.maximum(add_right, add_left))
        total = jnp.exp(own_cols - top) + jnp.exp(add_right - top) + jnp.exp(add_left - top)
        col = top + jnp.log(total)
        g_blocks = epsilon * (log_tgt - col)
        g_own = g_blocks.reshape(-1)
        send_right = g_blocks[want_right % tgt_blocks]
        send_left = g_blocks[want_left % tgt_blocks]
        g_extra = jnp.where(mine_from_left, shifted(send_right, "wide", 1), shifted(send_left, "wide", -1))

    row = row_lse(g_own, g_extra)
    source_pot = epsilon * (log_src - row)
    gs = jnp.concatenate([g_own * inv_eps, g_extra * inv_eps + extra_mask])
    weights = jnp.exp(z + gs[None, :] - row[:, None]).astype(jnp.bfloat16)
    numer = jnp.dot(weights[:, : tgt_blocks * BLK], targets, preferred_element_type=jnp.float32)
    numer = numer + jnp.dot(weights[:, tgt_blocks * BLK:], extra, preferred_element_type=jnp.float32)

    rows = sources.shape[0]
    part = rows // narrow_count
    mine_part = lax.dynamic_slice_in_dim(numer, c * part, part, 0)
    for k in range(1, narrow_count):
        dest = (c + k) % narrow_count
        piece = lax.dynamic_slice_in_dim(numer, dest * part, part, 0)
        mine_part = mine_part + shifted(piece, "narrow", k)
    done = mine_part.astype(jnp.bfloat16)
    pieces = jnp.stack([done] + [shifted(done, "narrow", k) for k in range(1, narrow_count)])
    order = (c - jnp.arange(narrow_count, dtype=jnp.int32)) % narrow_count
    mapped = pieces[order].reshape(rows, feature_count)
    return (source_pot, g_own, mapped)


def solution(mesh):
    placed = (P("wide", None), P(("wide", "narrow"), None), P(), P())
    return jax.shard_map(
        shards,
        mesh=mesh,
        in_specs=placed,
        out_specs=(P("wide"), P(("wide", "narrow")), P("wide", None)),
        check_vma=False,
    )
```

```python
import math

import jax
import jax.numpy as jnp
from jax import lax
from jax.sharding import PartitionSpec as P
from jax.experimental import pallas as pl

BLK = 1024
ITERS = 2


epsilon = 0.25
sentinel = -1e30


def shifted(x, axis, distance):
    size = lax.axis_size(axis)
    route = [(i, (i + distance) % size) for i in range(size)]
    return lax.ppermute(x, axis, route)


def _row_kernel(*refs):
    n = (len(refs) - 1) // 2
    out_ref = refs[-1]
    scores = [refs[k][...] + refs[n + k][...] for k in range(n)]
    top = scores[0].max(axis=1, keepdims=True)
    for s in scores[1:]:
        top = jnp.maximum(top, s.max(axis=1, keepdims=True))
    total = jnp.sum(jnp.exp(scores[0] - top), axis=1, keepdims=True)
    for s in scores[1:]:
        total = total + jnp.sum(jnp.exp(s - top), axis=1, keepdims=True)
    out_ref[...] = top + jnp.log(total)


def row_lse_call(zs, gs, tm=256):
    rows = zs[0].shape[0]
    in_specs = [pl.BlockSpec((tm, z.shape[1]), lambda i: (i, 0)) for z in zs]
    in_specs += [pl.BlockSpec((1, g.shape[1]), lambda i: (0, 0)) for g in gs]
    return pl.pallas_call(
        _row_kernel,
        grid=(rows // tm,),
        in_specs=in_specs,
        out_specs=pl.BlockSpec((tm, 1), lambda i: (i, 0)),
        out_shape=jax.ShapeDtypeStruct((rows, 1), jnp.float32),
    )(*zs, *gs)


def _col_kernel(zo_ref, ze_ref, f_ref, oo_ref, oe_ref):
    f = f_ref[...]
    for z_ref, o_ref in ((zo_ref, oo_ref), (ze_ref, oe_ref)):
        s = z_ref[...] + f
        top = s.max(axis=0, keepdims=True)
        o_ref[...] = top + jnp.log(jnp.sum(jnp.exp(s - top), axis=0, keepdims=True))


def col_lse_call(zo, ze, f, steps=4):
    rows = zo.shape[0]
    wo = zo.shape[1] // steps
    we = ze.shape[1] // steps
    return pl.pallas_call(
        _col_kernel,
        grid=(steps,),
        in_specs=[
            pl.BlockSpec((rows, wo), lambda j: (0, j)),
            pl.BlockSpec((rows, we), lambda j: (0, j)),
            pl.BlockSpec((rows, 1), lambda j: (0, 0)),
        ],
        out_specs=[
            pl.BlockSpec((1, wo), lambda j: (0, j)),
            pl.BlockSpec((1, we), lambda j: (0, j)),
        ],
        out_shape=[
            jax.ShapeDtypeStruct((1, zo.shape[1]), jnp.float32),
            jax.ShapeDtypeStruct((1, ze.shape[1]), jnp.float32),
        ],
    )(zo, ze, f)


def _map_kernel(zo_ref, ze_ref, go_ref, ge_ref, l_ref, to_ref, te_ref, out_ref):
    lse = l_ref[...]
    wo = jnp.exp(zo_ref[...] + go_ref[...] - lse).astype(jnp.bfloat16)
    we = jnp.exp(ze_ref[...] + ge_ref[...] - lse).astype(jnp.bfloat16)
    acc = jnp.dot(wo, to_ref[...], preferred_element_type=jnp.float32)
    out_ref[...] = acc + jnp.dot(we, te_ref[...], preferred_element_type=jnp.float32)


def map_call(zo, ze, go, ge, lse, to, te, tm=256):
    rows = zo.shape[0]
    feats = to.shape[1]
    return pl.pallas_call(
        _map_kernel,
        grid=(rows // tm,),
        in_specs=[
            pl.BlockSpec((tm, zo.shape[1]), lambda i: (i, 0)),
            pl.BlockSpec((tm, ze.shape[1]), lambda i: (i, 0)),
            pl.BlockSpec((1, go.shape[1]), lambda i: (0, 0)),
            pl.BlockSpec((1, ge.shape[1]), lambda i: (0, 0)),
            pl.BlockSpec((tm, 1), lambda i: (i, 0)),
            pl.BlockSpec(to.shape, lambda i: (0, 0)),
            pl.BlockSpec(te.shape, lambda i: (0, 0)),
        ],
        out_specs=pl.BlockSpec((tm, feats), lambda i: (i, 0)),
        out_shape=jax.ShapeDtypeStruct((rows, feats), jnp.float32),
    )(zo, ze, go, ge, lse, to, te)


def narrow_lse(partial_value, column, narrow_count):
    pieces = [partial_value] + [shifted(partial_value, "narrow", k) for k in range(1, narrow_count)]
    stacked = jnp.stack(pieces)
    order = (column - jnp.arange(narrow_count, dtype=jnp.int32)) % narrow_count
    ordered = stacked[order]
    top = jnp.max(ordered, axis=0)
    return top + jnp.log(jnp.sum(jnp.exp(ordered - top[None, :]), axis=0))


def shards(sources, targets, pair_target, pair_count):
    feature_count = sources.shape[1]
    tgt_blocks = targets.shape[0] // BLK
    wide_count = lax.axis_size("wide")
    narrow_count = lax.axis_size("narrow")
    w = lax.axis_index("wide")
    c = lax.axis_index("narrow")
    group_blocks = tgt_blocks * narrow_count
    scale = (1.0 / math.sqrt(feature_count)) * (1.0 / epsilon)
    inv_eps = 1.0 / epsilon
    log_src = -math.log(wide_count * sources.shape[0])
    log_tgt = -math.log(wide_count * narrow_count * targets.shape[0])

    left = (w - 1 + wide_count) % wide_count
    right = (w + 1) % wide_count
    slot = group_blocks + c

    mine = pair_target[w, slot]
    mine_live = pair_count[w] > slot
    mine_from_left = (mine // group_blocks) == left

    want_right = pair_target[right, slot]
    want_right_live = (pair_count[right] > slot) & ((want_right // group_blocks) == w)
    want_left = pair_target[left, slot]
    want_left_live = (pair_count[left] > slot) & ((want_left // group_blocks) == w)

    blocks = targets.reshape(tgt_blocks, BLK, feature_count)
    to_right = blocks[want_right % tgt_blocks]
    to_left = blocks[want_left % tgt_blocks]
    from_left = shifted(to_right, "wide", 1)
    from_right = shifted(to_left, "wide", -1)

    zo = lax.dot_general(
        sources, targets, (((1,), (1,)), ((), ())), preferred_element_type=jnp.float32
    ) * scale
    extra = jnp.where(mine_from_left, from_left, from_right)
    ze = lax.dot_general(
        sources, extra, (((1,), (1,)), ((), ())), preferred_element_type=jnp.float32
    ) * scale

    extra_mask = jnp.where(mine_live, 0.0, sentinel).astype(jnp.float32)
    own_width = tgt_blocks * BLK

    def scaled(g_own, g_extra):
        return ((g_own * inv_eps).reshape(1, own_width), (g_extra * inv_eps + extra_mask).reshape(1, BLK))

    g_own = jnp.zeros((own_width,), jnp.float32)
    g_extra = jnp.zeros((BLK,), jnp.float32)
    for iteration in range(ITERS):
        go, ge = scaled(g_own, g_extra)
        if iteration == 0:
            part_own = row_lse_call([zo], [go])
            part_ext = row_lse_call([ze], [ge])
            part = jnp.logaddexp(part_own, part_ext)
        else:
            part = row_lse_call([zo, ze], [go, ge])
        row = narrow_lse(part.reshape(-1), c, narrow_count)
        f = epsilon * (log_src - row)
        own_cols, extra_cols = col_lse_call(zo, ze, (f * inv_eps).reshape(-1, 1))
        own_cols = own_cols.reshape(tgt_blocks, BLK)
        extra_cols = jnp.where(mine_live, extra_cols.reshape(-1), sentinel)
        back_from_right = shifted(extra_cols, "wide", -1)
        back_from_left = shifted(extra_cols, "wide", 1)
        ids = jnp.arange(tgt_blocks, dtype=jnp.int32)[:, None]
        add_right = jnp.where(want_right_live & (ids == want_right % tgt_blocks), back_from_right[None, :], sentinel)
        add_left = jnp.where(want_left_live & (ids == want_left % tgt_blocks), back_from_left[None, :], sentinel)
        top = jnp.maximum(own_cols, jnp.maximum(add_right, add_left))
        total = jnp.exp(own_cols - top) + jnp.exp(add_right - top) + jnp.exp(add_left - top)
        col = top + jnp.log(total)
        g_blocks = epsilon * (log_tgt - col)
        g_own = g_blocks.reshape(-1)
        send_right = g_blocks[want_right % tgt_blocks]
        send_left = g_blocks[want_left % tgt_blocks]
        g_extra = jnp.where(mine_from_left, shifted(send_right, "wide", 1), shifted(send_left, "wide", -1))

    go, ge = scaled(g_own, g_extra)
    row = narrow_lse(row_lse_call([zo, ze], [go, ge]).reshape(-1), c, narrow_count)
    source_pot = epsilon * (log_src - row)
    numer = map_call(zo, ze, go, ge, row.reshape(-1, 1), targets, extra)

    rows = sources.shape[0]
    part = rows // narrow_count
    mine_part = lax.dynamic_slice_in_dim(numer, c * part, part, 0)
    for k in range(1, narrow_count):
        dest = (c + k) % narrow_count
        piece = lax.dynamic_slice_in_dim(numer, dest * part, part, 0)
        mine_part = mine_part + shifted(piece, "narrow", k)
    done = mine_part.astype(jnp.bfloat16)
    pieces = jnp.stack([done] + [shifted(done, "narrow", k) for k in range(1, narrow_count)])
    order = (c - jnp.arange(narrow_count, dtype=jnp.int32)) % narrow_count
    mapped = pieces[order].reshape(rows, feature_count)
    return (source_pot, g_own, mapped)


def solution(mesh):
    placed = (P("wide", None), P(("wide", "narrow"), None), P(), P())
    return jax.shard_map(
        shards,
        mesh=mesh,
        in_specs=placed,
        out_specs=(P("wide"), P(("wide", "narrow")), P("wide", None)),
        check_vma=False,
    )
```

```python
import math

import jax
import jax.numpy as jnp
from jax import lax
from jax.sharding import PartitionSpec as P
from jax.experimental import pallas as pl

BLK = 1024
ITERS = 2


epsilon = 0.25
sentinel = -1e30


def shifted(x, axis, distance):
    size = lax.axis_size(axis)
    route = [(i, (i + distance) % size) for i in range(size)]
    return lax.ppermute(x, axis, route)


def _row_kernel(*refs):
    n = (len(refs) - 1) // 2
    out_ref = refs[-1]
    scores = [refs[k][...] + refs[n + k][...] for k in range(n)]
    top = scores[0].max(axis=1, keepdims=True)
    for s in scores[1:]:
        top = jnp.maximum(top, s.max(axis=1, keepdims=True))
    total = jnp.sum(jnp.exp(scores[0] - top), axis=1, keepdims=True)
    for s in scores[1:]:
        total = total + jnp.sum(jnp.exp(s - top), axis=1, keepdims=True)
    out_ref[...] = top + jnp.log(total)


def row_lse_call(zs, gs, tm=256):
    rows = zs[0].shape[0]
    in_specs = [pl.BlockSpec((tm, z.shape[1]), lambda i: (i, 0)) for z in zs]
    in_specs += [pl.BlockSpec((1, g.shape[1]), lambda i: (0, 0)) for g in gs]
    return pl.pallas_call(
        _row_kernel,
        grid=(rows // tm,),
        in_specs=in_specs,
        out_specs=pl.BlockSpec((tm, 1), lambda i: (i, 0)),
        out_shape=jax.ShapeDtypeStruct((rows, 1), jnp.float32),
    )(*zs, *gs)


def _col_kernel(zo_ref, ze_ref, f_ref, oo_ref, oe_ref):
    f = f_ref[...]
    for z_ref, o_ref in ((zo_ref, oo_ref), (ze_ref, oe_ref)):
        s = z_ref[...] + f
        top = s.max(axis=0, keepdims=True)
        o_ref[...] = top + jnp.log(jnp.sum(jnp.exp(s - top), axis=0, keepdims=True))


def col_lse_call(zo, ze, f, steps=4):
    rows = zo.shape[0]
    wo = zo.shape[1] // steps
    we = ze.shape[1] // steps
    return pl.pallas_call(
        _col_kernel,
        grid=(steps,),
        in_specs=[
            pl.BlockSpec((rows, wo), lambda j: (0, j)),
            pl.BlockSpec((rows, we), lambda j: (0, j)),
            pl.BlockSpec((rows, 1), lambda j: (0, 0)),
        ],
        out_specs=[
            pl.BlockSpec((1, wo), lambda j: (0, j)),
            pl.BlockSpec((1, we), lambda j: (0, j)),
        ],
        out_shape=[
            jax.ShapeDtypeStruct((1, zo.shape[1]), jnp.float32),
            jax.ShapeDtypeStruct((1, ze.shape[1]), jnp.float32),
        ],
    )(zo, ze, f)


def _map_kernel(zo_ref, ze_ref, go_ref, ge_ref, l_ref, to_ref, te_ref, out_ref):
    lse = l_ref[...]
    wo = jnp.exp(zo_ref[...] + go_ref[...] - lse).astype(jnp.bfloat16)
    we = jnp.exp(ze_ref[...] + ge_ref[...] - lse).astype(jnp.bfloat16)
    acc = jnp.dot(wo, to_ref[...], preferred_element_type=jnp.float32)
    out_ref[...] = acc + jnp.dot(we, te_ref[...], preferred_element_type=jnp.float32)


def map_call(zo, ze, go, ge, lse, to, te, tm=256):
    rows = zo.shape[0]
    feats = to.shape[1]
    return pl.pallas_call(
        _map_kernel,
        grid=(rows // tm,),
        in_specs=[
            pl.BlockSpec((tm, zo.shape[1]), lambda i: (i, 0)),
            pl.BlockSpec((tm, ze.shape[1]), lambda i: (i, 0)),
            pl.BlockSpec((1, go.shape[1]), lambda i: (0, 0)),
            pl.BlockSpec((1, ge.shape[1]), lambda i: (0, 0)),
            pl.BlockSpec((tm, 1), lambda i: (i, 0)),
            pl.BlockSpec(to.shape, lambda i: (0, 0)),
            pl.BlockSpec(te.shape, lambda i: (0, 0)),
        ],
        out_specs=pl.BlockSpec((tm, feats), lambda i: (i, 0)),
        out_shape=jax.ShapeDtypeStruct((rows, feats), jnp.float32),
    )(zo, ze, go, ge, lse, to, te)


def narrow_lse(partial_value, column, narrow_count):
    pieces = [partial_value] + [shifted(partial_value, "narrow", k) for k in range(1, narrow_count)]
    stacked = jnp.stack(pieces)
    order = (column - jnp.arange(narrow_count, dtype=jnp.int32)) % narrow_count
    ordered = stacked[order]
    top = jnp.max(ordered, axis=0)
    return top + jnp.log(jnp.sum(jnp.exp(ordered - top[None, :]), axis=0))


def shards(sources, targets, pair_target, pair_count):
    feature_count = sources.shape[1]
    tgt_blocks = targets.shape[0] // BLK
    wide_count = lax.axis_size("wide")
    narrow_count = lax.axis_size("narrow")
    w = lax.axis_index("wide")
    c = lax.axis_index("narrow")
    group_blocks = tgt_blocks * narrow_count
    scale = (1.0 / math.sqrt(feature_count)) * (1.0 / epsilon)
    inv_eps = 1.0 / epsilon
    log_src = -math.log(wide_count * sources.shape[0])
    log_tgt = -math.log(wide_count * narrow_count * targets.shape[0])

    left = (w - 1 + wide_count) % wide_count
    right = (w + 1) % wide_count
    slot = group_blocks + c

    mine = pair_target[w, slot]
    mine_live = pair_count[w] > slot
    mine_from_left = (mine // group_blocks) == left

    want_right = pair_target[right, slot]
    want_right_live = (pair_count[right] > slot) & ((want_right // group_blocks) == w)
    want_left = pair_target[left, slot]
    want_left_live = (pair_count[left] > slot) & ((want_left // group_blocks) == w)

    blocks = targets.reshape(tgt_blocks, BLK, feature_count)
    to_right = blocks[want_right % tgt_blocks]
    to_left = blocks[want_left % tgt_blocks]
    from_left = shifted(to_right, "wide", 1)
    from_right = shifted(to_left, "wide", -1)

    zo = lax.dot_general(
        sources, targets, (((1,), (1,)), ((), ())), preferred_element_type=jnp.float32
    ) * scale
    extra = jnp.where(mine_from_left, from_left, from_right)
    ze = lax.dot_general(
        sources, extra, (((1,), (1,)), ((), ())), preferred_element_type=jnp.float32
    ) * scale

    extra_mask = jnp.where(mine_live, 0.0, sentinel).astype(jnp.float32)
    own_width = tgt_blocks * BLK

    def scaled(g_own, g_extra):
        return ((g_own * inv_eps).reshape(1, own_width), (g_extra * inv_eps + extra_mask).reshape(1, BLK))

    g_own = jnp.zeros((own_width,), jnp.float32)
    g_extra = jnp.zeros((BLK,), jnp.float32)
    for iteration in range(ITERS):
        go, ge = scaled(g_own, g_extra)
        if iteration == 0:
            part_own = row_lse_call([zo], [go])
            part_ext = row_lse_call([ze], [ge])
            part = jnp.logaddexp(part_own, part_ext)
        else:
            part = row_lse_call([zo, ze], [go, ge])
        row = narrow_lse(part.reshape(-1), c, narrow_count)
        f = epsilon * (log_src - row)
        own_cols, extra_cols = col_lse_call(zo, ze, (f * inv_eps).reshape(-1, 1))
        own_cols = own_cols.reshape(tgt_blocks, BLK)
        extra_cols = jnp.where(mine_live, extra_cols.reshape(-1), sentinel)
        back_from_right = shifted(extra_cols, "wide", -1)
        back_from_left = shifted(extra_cols, "wide", 1)
        ids = jnp.arange(tgt_blocks, dtype=jnp.int32)[:, None]
        add_right = jnp.where(want_right_live & (ids == want_right % tgt_blocks), back_from_right[None, :], sentinel)
        add_left = jnp.where(want_left_live & (ids == want_left % tgt_blocks), back_from_left[None, :], sentinel)
        top = jnp.maximum(own_cols, jnp.maximum(add_right, add_left))
        total = jnp.exp(own_cols - top) + jnp.exp(add_right - top) + jnp.exp(add_left - top)
        col = top + jnp.log(total)
        g_blocks = epsilon * (log_tgt - col)
        g_own = g_blocks.reshape(-1)
        send_right = g_blocks[want_right % tgt_blocks]
        send_left = g_blocks[want_left % tgt_blocks]
        g_extra = jnp.where(mine_from_left, shifted(send_right, "wide", 1), shifted(send_left, "wide", -1))

    go, ge = scaled(g_own, g_extra)
    row = narrow_lse(row_lse_call([zo, ze], [go, ge]).reshape(-1), c, narrow_count)
    source_pot = epsilon * (log_src - row)
    numer = map_call(zo, ze, go, ge, row.reshape(-1, 1), targets, extra)

    summed = lax.psum_scatter(numer, "narrow", scatter_dimension=0, tiled=True)
    mapped = lax.all_gather(summed.astype(jnp.bfloat16), "narrow", axis=0, tiled=True)
    return (source_pot, g_own, mapped)


def solution(mesh):
    placed = (P("wide", None), P(("wide", "narrow"), None), P(), P())
    return jax.shard_map(
        shards,
        mesh=mesh,
        in_specs=placed,
        out_specs=(P("wide"), P(("wide", "narrow")), P("wide", None)),
        check_vma=False,
    )
```

```python
import math

import jax
import jax.numpy as jnp
from jax import lax
from jax.sharding import PartitionSpec as P
from jax.experimental import pallas as pl

BLK = 1024
ITERS = 2


epsilon = 0.25
sentinel = -1e30


def shifted(x, axis, distance):
    size = lax.axis_size(axis)
    route = [(i, (i + distance) % size) for i in range(size)]
    return lax.ppermute(x, axis, route)


def _row_kernel(*refs):
    n = (len(refs) - 1) // 2
    out_ref = refs[-1]
    scores = [refs[k][...] + refs[n + k][...] for k in range(n)]
    top = scores[0].max(axis=1, keepdims=True)
    for s in scores[1:]:
        top = jnp.maximum(top, s.max(axis=1, keepdims=True))
    total = jnp.sum(jnp.exp(scores[0] - top), axis=1, keepdims=True)
    for s in scores[1:]:
        total = total + jnp.sum(jnp.exp(s - top), axis=1, keepdims=True)
    out_ref[...] = top + jnp.log(total)


def row_lse_call(zs, gs, tm=256):
    rows = zs[0].shape[0]
    in_specs = [pl.BlockSpec((tm, z.shape[1]), lambda i: (i, 0)) for z in zs]
    in_specs += [pl.BlockSpec((1, g.shape[1]), lambda i: (0, 0)) for g in gs]
    return pl.pallas_call(
        _row_kernel,
        grid=(rows // tm,),
        in_specs=in_specs,
        out_specs=pl.BlockSpec((tm, 1), lambda i: (i, 0)),
        out_shape=jax.ShapeDtypeStruct((rows, 1), jnp.float32),
    )(*zs, *gs)


def _col_kernel(zo_ref, ze_ref, f_ref, oo_ref, oe_ref):
    f = f_ref[...]
    for z_ref, o_ref in ((zo_ref, oo_ref), (ze_ref, oe_ref)):
        s = z_ref[...] + f
        top = s.max(axis=0, keepdims=True)
        o_ref[...] = top + jnp.log(jnp.sum(jnp.exp(s - top), axis=0, keepdims=True))


def col_lse_call(zo, ze, f, steps=4):
    rows = zo.shape[0]
    wo = zo.shape[1] // steps
    we = ze.shape[1] // steps
    return pl.pallas_call(
        _col_kernel,
        grid=(steps,),
        in_specs=[
            pl.BlockSpec((rows, wo), lambda j: (0, j)),
            pl.BlockSpec((rows, we), lambda j: (0, j)),
            pl.BlockSpec((rows, 1), lambda j: (0, 0)),
        ],
        out_specs=[
            pl.BlockSpec((1, wo), lambda j: (0, j)),
            pl.BlockSpec((1, we), lambda j: (0, j)),
        ],
        out_shape=[
            jax.ShapeDtypeStruct((1, zo.shape[1]), jnp.float32),
            jax.ShapeDtypeStruct((1, ze.shape[1]), jnp.float32),
        ],
    )(zo, ze, f)


def _map_kernel(zo_ref, ze_ref, go_ref, ge_ref, l_ref, to_ref, te_ref, out_ref):
    lse = l_ref[...]
    wo = jnp.exp(zo_ref[...] + go_ref[...] - lse).astype(jnp.bfloat16)
    we = jnp.exp(ze_ref[...] + ge_ref[...] - lse).astype(jnp.bfloat16)
    acc = jnp.dot(wo, to_ref[...], preferred_element_type=jnp.float32)
    out_ref[...] = acc + jnp.dot(we, te_ref[...], preferred_element_type=jnp.float32)


def map_call(zo, ze, go, ge, lse, to, te, tm=256):
    rows = zo.shape[0]
    feats = to.shape[1]
    return pl.pallas_call(
        _map_kernel,
        grid=(rows // tm,),
        in_specs=[
            pl.BlockSpec((tm, zo.shape[1]), lambda i: (i, 0)),
            pl.BlockSpec((tm, ze.shape[1]), lambda i: (i, 0)),
            pl.BlockSpec((1, go.shape[1]), lambda i: (0, 0)),
            pl.BlockSpec((1, ge.shape[1]), lambda i: (0, 0)),
            pl.BlockSpec((tm, 1), lambda i: (i, 0)),
            pl.BlockSpec(to.shape, lambda i: (0, 0)),
            pl.BlockSpec(te.shape, lambda i: (0, 0)),
        ],
        out_specs=pl.BlockSpec((tm, feats), lambda i: (i, 0)),
        out_shape=jax.ShapeDtypeStruct((rows, feats), jnp.float32),
    )(zo, ze, go, ge, lse, to, te)


def narrow_lse(partial_value, column, narrow_count):
    pieces = [partial_value] + [shifted(partial_value, "narrow", k) for k in range(1, narrow_count)]
    stacked = jnp.stack(pieces)
    order = (column - jnp.arange(narrow_count, dtype=jnp.int32)) % narrow_count
    ordered = stacked[order]
    top = jnp.max(ordered, axis=0)
    return top + jnp.log(jnp.sum(jnp.exp(ordered - top[None, :]), axis=0))


def shards(sources, targets, pair_target, pair_count):
    feature_count = sources.shape[1]
    tgt_blocks = targets.shape[0] // BLK
    wide_count = lax.axis_size("wide")
    narrow_count = lax.axis_size("narrow")
    w = lax.axis_index("wide")
    c = lax.axis_index("narrow")
    group_blocks = tgt_blocks * narrow_count
    scale = (1.0 / math.sqrt(feature_count)) * (1.0 / epsilon)
    inv_eps = 1.0 / epsilon
    log_src = -math.log(wide_count * sources.shape[0])
    log_tgt = -math.log(wide_count * narrow_count * targets.shape[0])

    left = (w - 1 + wide_count) % wide_count
    right = (w + 1) % wide_count
    slot = group_blocks + c

    mine = pair_target[w, slot]
    mine_live = pair_count[w] > slot
    mine_from_left = (mine // group_blocks) == left

    want_right = pair_target[right, slot]
    want_right_live = (pair_count[right] > slot) & ((want_right // group_blocks) == w)
    want_left = pair_target[left, slot]
    want_left_live = (pair_count[left] > slot) & ((want_left // group_blocks) == w)
    left2 = (w - 2 + 2 * wide_count) % wide_count
    right2 = (w + 2) % wide_count
    far_left_same = (pair_count[left2] > slot) & (pair_target[left2, slot] == mine)
    far_right_same = (pair_count[right2] > slot) & (pair_target[right2, slot] == mine)

    blocks = targets.reshape(tgt_blocks, BLK, feature_count)
    to_right = blocks[want_right % tgt_blocks]
    to_left = blocks[want_left % tgt_blocks]
    from_left = shifted(to_right, "wide", 1)
    from_right = shifted(to_left, "wide", -1)

    zo = lax.dot_general(
        sources, targets, (((1,), (1,)), ((), ())), preferred_element_type=jnp.float32
    ) * scale
    extra = jnp.where(mine_from_left, from_left, from_right)
    ze = lax.dot_general(
        sources, extra, (((1,), (1,)), ((), ())), preferred_element_type=jnp.float32
    ) * scale

    extra_mask = jnp.where(mine_live, 0.0, sentinel).astype(jnp.float32)
    own_width = tgt_blocks * BLK

    def scaled(g_own, g_extra):
        return ((g_own * inv_eps).reshape(1, own_width), (g_extra * inv_eps + extra_mask).reshape(1, BLK))

    g_own = jnp.zeros((own_width,), jnp.float32)
    g_extra = jnp.zeros((BLK,), jnp.float32)
    for iteration in range(ITERS):
        go, ge = scaled(g_own, g_extra)
        if iteration == 0:
            part_own = row_lse_call([zo], [go])
            part_ext = row_lse_call([ze], [ge])
            part = jnp.logaddexp(part_own, part_ext)
        else:
            part = row_lse_call([zo, ze], [go, ge])
        row = narrow_lse(part.reshape(-1), c, narrow_count)
        f = epsilon * (log_src - row)
        own_cols, extra_cols = col_lse_call(zo, ze, (f * inv_eps).reshape(-1, 1))
        own_cols = own_cols.reshape(tgt_blocks, BLK)
        extra_cols = jnp.where(mine_live, extra_cols.reshape(-1), sentinel)
        part_from_left = shifted(extra_cols, "wide", 1)
        part_from_right = shifted(extra_cols, "wide", -1)
        part_from_left2 = shifted(extra_cols, "wide", 2)
        part_from_right2 = shifted(extra_cols, "wide", -2)
        cover_from_left = shifted(own_cols[want_right % tgt_blocks], "wide", 1)
        cover_from_right = shifted(own_cols[want_left % tgt_blocks], "wide", -1)
        ids = jnp.arange(tgt_blocks, dtype=jnp.int32)[:, None]
        add_right = jnp.where(want_right_live & (ids == want_right % tgt_blocks), part_from_right[None, :], sentinel)
        add_left = jnp.where(want_left_live & (ids == want_left % tgt_blocks), part_from_left[None, :], sentinel)
        top = jnp.maximum(own_cols, jnp.maximum(add_right, add_left))
        total = jnp.exp(own_cols - top) + jnp.exp(add_right - top) + jnp.exp(add_left - top)
        g_blocks = epsilon * (log_tgt - (top + jnp.log(total)))
        g_own = g_blocks.reshape(-1)
        cover_e = jnp.where(mine_from_left, cover_from_left, cover_from_right)
        other = jnp.where(mine_from_left, part_from_left2, part_from_right2)
        other_live = jnp.where(mine_from_left, far_left_same, far_right_same)
        other = jnp.where(other_live, other, sentinel)
        first = jnp.where(mine_from_left, extra_cols, other)
        second = jnp.where(mine_from_left, other, extra_cols)
        top_e = jnp.maximum(cover_e, jnp.maximum(first, second))
        total_e = jnp.exp(cover_e - top_e) + jnp.exp(first - top_e) + jnp.exp(second - top_e)
        g_extra = epsilon * (log_tgt - (top_e + jnp.log(total_e)))

    go, ge = scaled(g_own, g_extra)
    row = narrow_lse(row_lse_call([zo, ze], [go, ge]).reshape(-1), c, narrow_count)
    source_pot = epsilon * (log_src - row)
    numer = map_call(zo, ze, go, ge, row.reshape(-1, 1), targets, extra)

    rows = sources.shape[0]
    quarter = rows // narrow_count
    half = quarter // 2
    chunks = numer.reshape(narrow_count, 2, half, feature_count)

    def chunk(index, side):
        return lax.dynamic_index_in_dim(chunks, index % narrow_count, 0, False)[side]

    far_a = shifted(chunk(c + 2, 0), "narrow", 1)
    far_b = shifted(chunk(c + 2, 1), "narrow", -1)
    to_right = jnp.stack([chunk(c + 1, 0) + far_a, chunk(c + 1, 1)])
    to_left = jnp.stack([chunk(c - 1, 0), chunk(c - 1, 1) + far_b])
    got_left = shifted(to_right, "narrow", 1)
    got_right = shifted(to_left, "narrow", -1)
    mine_sum = jnp.stack([chunk(c, 0), chunk(c, 1)]) + got_left + got_right
    done = mine_sum.astype(jnp.bfloat16).reshape(quarter, feature_count)
    q_left = shifted(done, "narrow", 1)
    q_right = shifted(done, "narrow", -1)
    far_half_a = shifted(q_left[:half], "narrow", 1)
    far_half_b = shifted(q_right[half:], "narrow", -1)
    q_far = jnp.concatenate([far_half_a, far_half_b])
    pieces = jnp.stack([done, q_left, q_far, q_right])
    order = (c - jnp.arange(narrow_count, dtype=jnp.int32)) % narrow_count
    mapped = pieces[order].reshape(rows, feature_count)
    return (source_pot, g_own, mapped)


def solution(mesh):
    placed = (P("wide", None), P(("wide", "narrow"), None), P(), P())
    return jax.shard_map(
        shards,
        mesh=mesh,
        in_specs=placed,
        out_specs=(P("wide"), P(("wide", "narrow")), P("wide", None)),
        check_vma=False,
    )
```

```python
import math

import jax
import jax.numpy as jnp
from jax import lax
from jax.sharding import PartitionSpec as P
from jax.experimental import pallas as pl

BLK = 1024
ITERS = 2


epsilon = 0.25
sentinel = -1e30


def shifted(x, axis, distance):
    size = lax.axis_size(axis)
    route = [(i, (i + distance) % size) for i in range(size)]
    return lax.ppermute(x, axis, route)


def _row_kernel(*refs):
    n = (len(refs) - 1) // 2
    out_ref = refs[-1]
    scores = [refs[k][...] + refs[n + k][...] for k in range(n)]
    top = scores[0].max(axis=1, keepdims=True)
    for s in scores[1:]:
        top = jnp.maximum(top, s.max(axis=1, keepdims=True))
    total = jnp.sum(jnp.exp(scores[0] - top), axis=1, keepdims=True)
    for s in scores[1:]:
        total = total + jnp.sum(jnp.exp(s - top), axis=1, keepdims=True)
    out_ref[...] = top + jnp.log(total)


def row_lse_call(zs, gs, tm=256):
    rows = zs[0].shape[0]
    in_specs = [pl.BlockSpec((tm, z.shape[1]), lambda i: (i, 0)) for z in zs]
    in_specs += [pl.BlockSpec((1, g.shape[1]), lambda i: (0, 0)) for g in gs]
    return pl.pallas_call(
        _row_kernel,
        grid=(rows // tm,),
        in_specs=in_specs,
        out_specs=pl.BlockSpec((tm, 1), lambda i: (i, 0)),
        out_shape=jax.ShapeDtypeStruct((rows, 1), jnp.float32),
    )(*zs, *gs)


def _col_kernel(zo_ref, ze_ref, f_ref, oo_ref, oe_ref):
    f = f_ref[...]
    for z_ref, o_ref in ((zo_ref, oo_ref), (ze_ref, oe_ref)):
        s = z_ref[...] + f
        top = s.max(axis=0, keepdims=True)
        o_ref[...] = top + jnp.log(jnp.sum(jnp.exp(s - top), axis=0, keepdims=True))


def col_lse_call(zo, ze, f, steps=4):
    rows = zo.shape[0]
    wo = zo.shape[1] // steps
    we = ze.shape[1] // steps
    return pl.pallas_call(
        _col_kernel,
        grid=(steps,),
        in_specs=[
            pl.BlockSpec((rows, wo), lambda j: (0, j)),
            pl.BlockSpec((rows, we), lambda j: (0, j)),
            pl.BlockSpec((rows, 1), lambda j: (0, 0)),
        ],
        out_specs=[
            pl.BlockSpec((1, wo), lambda j: (0, j)),
            pl.BlockSpec((1, we), lambda j: (0, j)),
        ],
        out_shape=[
            jax.ShapeDtypeStruct((1, zo.shape[1]), jnp.float32),
            jax.ShapeDtypeStruct((1, ze.shape[1]), jnp.float32),
        ],
    )(zo, ze, f)


def _map_kernel(zo_ref, ze_ref, go_ref, ge_ref, l_ref, to_ref, te_ref, out_ref):
    lse = l_ref[...]
    wo = jnp.exp(zo_ref[...] + go_ref[...] - lse).astype(jnp.bfloat16)
    we = jnp.exp(ze_ref[...] + ge_ref[...] - lse).astype(jnp.bfloat16)
    acc = jnp.dot(wo, to_ref[...], preferred_element_type=jnp.float32)
    out_ref[...] = acc + jnp.dot(we, te_ref[...], preferred_element_type=jnp.float32)


def map_call(zo, ze, go, ge, lse, to, te, tm=256):
    rows = zo.shape[0]
    feats = to.shape[1]
    return pl.pallas_call(
        _map_kernel,
        grid=(rows // tm,),
        in_specs=[
            pl.BlockSpec((tm, zo.shape[1]), lambda i: (i, 0)),
            pl.BlockSpec((tm, ze.shape[1]), lambda i: (i, 0)),
            pl.BlockSpec((1, go.shape[1]), lambda i: (0, 0)),
            pl.BlockSpec((1, ge.shape[1]), lambda i: (0, 0)),
            pl.BlockSpec((tm, 1), lambda i: (i, 0)),
            pl.BlockSpec(to.shape, lambda i: (0, 0)),
            pl.BlockSpec(te.shape, lambda i: (0, 0)),
        ],
        out_specs=pl.BlockSpec((tm, feats), lambda i: (i, 0)),
        out_shape=jax.ShapeDtypeStruct((rows, feats), jnp.float32),
    )(zo, ze, go, ge, lse, to, te)


def narrow_lse(partial_value, column, narrow_count):
    pieces = [partial_value] + [shifted(partial_value, "narrow", k) for k in range(1, narrow_count)]
    stacked = jnp.stack(pieces)
    order = (column - jnp.arange(narrow_count, dtype=jnp.int32)) % narrow_count
    ordered = stacked[order]
    top = jnp.max(ordered, axis=0)
    return top + jnp.log(jnp.sum(jnp.exp(ordered - top[None, :]), axis=0))


def shards(sources, targets, pair_target, pair_count):
    feature_count = sources.shape[1]
    tgt_blocks = targets.shape[0] // BLK
    wide_count = lax.axis_size("wide")
    narrow_count = lax.axis_size("narrow")
    w = lax.axis_index("wide")
    c = lax.axis_index("narrow")
    group_blocks = tgt_blocks * narrow_count
    scale = (1.0 / math.sqrt(feature_count)) * (1.0 / epsilon)
    inv_eps = 1.0 / epsilon
    log_src = -math.log(wide_count * sources.shape[0])
    log_tgt = -math.log(wide_count * narrow_count * targets.shape[0])

    left = (w - 1 + wide_count) % wide_count
    right = (w + 1) % wide_count
    slot = group_blocks + c

    mine = pair_target[w, slot]
    mine_live = pair_count[w] > slot
    mine_from_left = (mine // group_blocks) == left

    want_right = pair_target[right, slot]
    want_right_live = (pair_count[right] > slot) & ((want_right // group_blocks) == w)
    want_left = pair_target[left, slot]
    want_left_live = (pair_count[left] > slot) & ((want_left // group_blocks) == w)
    left2 = (w - 2 + 2 * wide_count) % wide_count
    right2 = (w + 2) % wide_count
    far_left_same = (pair_count[left2] > slot) & (pair_target[left2, slot] == mine)
    far_right_same = (pair_count[right2] > slot) & (pair_target[right2, slot] == mine)

    blocks = targets.reshape(tgt_blocks, BLK, feature_count)
    to_right = blocks[want_right % tgt_blocks]
    to_left = blocks[want_left % tgt_blocks]
    from_left = shifted(to_right, "wide", 1)
    from_right = shifted(to_left, "wide", -1)

    zo = lax.dot_general(
        sources, targets, (((1,), (1,)), ((), ())), preferred_element_type=jnp.float32
    ) * scale
    extra = jnp.where(mine_from_left, from_left, from_right)
    ze = lax.dot_general(
        sources, extra, (((1,), (1,)), ((), ())), preferred_element_type=jnp.float32
    ) * scale

    extra_mask = jnp.where(mine_live, 0.0, sentinel).astype(jnp.float32)
    own_width = tgt_blocks * BLK

    def scaled(g_own, g_extra):
        return ((g_own * inv_eps).reshape(1, own_width), (g_extra * inv_eps + extra_mask).reshape(1, BLK))

    g_own = jnp.zeros((own_width,), jnp.float32)
    g_extra = jnp.zeros((BLK,), jnp.float32)
    for iteration in range(ITERS):
        go, ge = scaled(g_own, g_extra)
        if iteration == 0:
            part_own = row_lse_call([zo], [go])
            part_ext = row_lse_call([ze], [ge])
            part = jnp.logaddexp(part_own, part_ext)
        else:
            part = row_lse_call([zo, ze], [go, ge])
        row = narrow_lse(part.reshape(-1), c, narrow_count)
        f = epsilon * (log_src - row)
        own_cols, extra_cols = col_lse_call(zo, ze, (f * inv_eps).reshape(-1, 1))
        own_cols = own_cols.reshape(tgt_blocks, BLK)
        extra_cols = jnp.where(mine_live, extra_cols.reshape(-1), sentinel)
        from_left_msg = shifted(jnp.stack([extra_cols, own_cols[want_right % tgt_blocks]]), "wide", 1)
        from_right_msg = shifted(jnp.stack([extra_cols, own_cols[want_left % tgt_blocks]]), "wide", -1)
        part_from_left2 = shifted(extra_cols, "wide", 2)
        part_from_right2 = shifted(extra_cols, "wide", -2)
        part_from_left, cover_from_left = from_left_msg[0], from_left_msg[1]
        part_from_right, cover_from_right = from_right_msg[0], from_right_msg[1]
        ids = jnp.arange(tgt_blocks, dtype=jnp.int32)[:, None]
        add_right = jnp.where(want_right_live & (ids == want_right % tgt_blocks), part_from_right[None, :], sentinel)
        add_left = jnp.where(want_left_live & (ids == want_left % tgt_blocks), part_from_left[None, :], sentinel)
        top = jnp.maximum(own_cols, jnp.maximum(add_right, add_left))
        total = jnp.exp(own_cols - top) + jnp.exp(add_right - top) + jnp.exp(add_left - top)
        g_blocks = epsilon * (log_tgt - (top + jnp.log(total)))
        g_own = g_blocks.reshape(-1)
        cover_e = jnp.where(mine_from_left, cover_from_left, cover_from_right)
        other = jnp.where(mine_from_left, part_from_left2, part_from_right2)
        other_live = jnp.where(mine_from_left, far_left_same, far_right_same)
        other = jnp.where(other_live, other, sentinel)
        first = jnp.where(mine_from_left, extra_cols, other)
        second = jnp.where(mine_from_left, other, extra_cols)
        top_e = jnp.maximum(cover_e, jnp.maximum(first, second))
        total_e = jnp.exp(cover_e - top_e) + jnp.exp(first - top_e) + jnp.exp(second - top_e)
        g_extra = epsilon * (log_tgt - (top_e + jnp.log(total_e)))

    go, ge = scaled(g_own, g_extra)
    row = narrow_lse(row_lse_call([zo, ze], [go, ge]).reshape(-1), c, narrow_count)
    source_pot = epsilon * (log_src - row)
    numer = map_call(zo, ze, go, ge, row.reshape(-1, 1), targets, extra)

    rows = sources.shape[0]
    quarter = rows // narrow_count
    half = quarter // 2
    chunks = numer.reshape(narrow_count, 2, half, feature_count)

    def chunk(index, side):
        return lax.dynamic_index_in_dim(chunks, index % narrow_count, 0, False)[side]

    far_a = shifted(chunk(c + 2, 0), "narrow", 1)
    far_b = shifted(chunk(c + 2, 1), "narrow", -1)
    to_right = jnp.stack([chunk(c + 1, 0) + far_a, chunk(c + 1, 1)])
    to_left = jnp.stack([chunk(c - 1, 0), chunk(c - 1, 1) + far_b])
    got_left = shifted(to_right, "narrow", 1)
    got_right = shifted(to_left, "narrow", -1)
    mine_sum = jnp.stack([chunk(c, 0), chunk(c, 1)]) + got_left + got_right
    done = mine_sum.astype(jnp.bfloat16).reshape(quarter, feature_count)
    q_left = shifted(done, "narrow", 1)
    q_right = shifted(done, "narrow", -1)
    far_half_a = shifted(q_left[:half], "narrow", 1)
    far_half_b = shifted(q_right[half:], "narrow", -1)
    q_far = jnp.concatenate([far_half_a, far_half_b])
    pieces = jnp.stack([done, q_left, q_far, q_right])
    order = (c - jnp.arange(narrow_count, dtype=jnp.int32)) % narrow_count
    mapped = pieces[order].reshape(rows, feature_count)
    return (source_pot, g_own, mapped)


def solution(mesh):
    placed = (P("wide", None), P(("wide", "narrow"), None), P(), P())
    return jax.shard_map(
        shards,
        mesh=mesh,
        in_specs=placed,
        out_specs=(P("wide"), P(("wide", "narrow")), P("wide", None)),
        check_vma=False,
    )
```

```python
import math

import jax
import jax.numpy as jnp
from jax import lax
from jax.sharding import PartitionSpec as P
from jax.experimental import pallas as pl
from jax.experimental.pallas import tpu as pltpu

BLK = 1024
ITERS = 2


epsilon = 0.25
sentinel = -1e30


def shifted(x, axis, distance):
    size = lax.axis_size(axis)
    route = [(i, (i + distance) % size) for i in range(size)]
    return lax.ppermute(x, axis, route)


def _row_kernel(*refs):
    n = (len(refs) - 1) // 2
    out_ref = refs[-1]
    scores = [refs[k][...] + refs[n + k][...] for k in range(n)]
    top = scores[0].max(axis=1, keepdims=True)
    for s in scores[1:]:
        top = jnp.maximum(top, s.max(axis=1, keepdims=True))
    total = jnp.sum(jnp.exp(scores[0] - top), axis=1, keepdims=True)
    for s in scores[1:]:
        total = total + jnp.sum(jnp.exp(s - top), axis=1, keepdims=True)
    out_ref[...] = top + jnp.log(total)


def row_lse_call(zs, gs, tm=256):
    rows = zs[0].shape[0]
    in_specs = [pl.BlockSpec((tm, z.shape[1]), lambda i: (i, 0)) for z in zs]
    in_specs += [pl.BlockSpec((1, g.shape[1]), lambda i: (0, 0)) for g in gs]
    return pl.pallas_call(
        _row_kernel,
        grid=(rows // tm,),
        in_specs=in_specs,
        out_specs=pl.BlockSpec((tm, 1), lambda i: (i, 0)),
        out_shape=jax.ShapeDtypeStruct((rows, 1), jnp.float32),
    )(*zs, *gs)


def _col_kernel(zo_ref, ze_ref, f_ref, oo_ref, oe_ref):
    f = f_ref[...]
    for z_ref, o_ref in ((zo_ref, oo_ref), (ze_ref, oe_ref)):
        s = z_ref[...] + f
        top = s.max(axis=0, keepdims=True)
        o_ref[...] = top + jnp.log(jnp.sum(jnp.exp(s - top), axis=0, keepdims=True))


def col_lse_call(zo, ze, f, steps=4):
    rows = zo.shape[0]
    wo = zo.shape[1] // steps
    we = ze.shape[1] // steps
    return pl.pallas_call(
        _col_kernel,
        grid=(steps,),
        in_specs=[
            pl.BlockSpec((rows, wo), lambda j: (0, j)),
            pl.BlockSpec((rows, we), lambda j: (0, j)),
            pl.BlockSpec((rows, 1), lambda j: (0, 0)),
        ],
        out_specs=[
            pl.BlockSpec((1, wo), lambda j: (0, j)),
            pl.BlockSpec((1, we), lambda j: (0, j)),
        ],
        out_shape=[
            jax.ShapeDtypeStruct((1, zo.shape[1]), jnp.float32),
            jax.ShapeDtypeStruct((1, ze.shape[1]), jnp.float32),
        ],
    )(zo, ze, f)


def _map_kernel(q_ref, zo_ref, ze_ref, go_ref, ge_ref, l_ref, to_ref, te_ref, out_ref):
    lse = l_ref[...]
    wo = jnp.exp(zo_ref[...] + go_ref[...] - lse).astype(jnp.bfloat16)
    we = jnp.exp(ze_ref[...] + ge_ref[...] - lse).astype(jnp.bfloat16)
    acc = jnp.dot(wo, to_ref[...], preferred_element_type=jnp.float32)
    out_ref[...] = acc + jnp.dot(we, te_ref[...], preferred_element_type=jnp.float32)


def map_call(zo, ze, go, ge, lse, to, te, quarters, tm):
    feats = to.shape[1]
    count = quarters.shape[0]
    grid_spec = pltpu.PrefetchScalarGridSpec(
        num_scalar_prefetch=1,
        grid=(count,),
        in_specs=[
            pl.BlockSpec((tm, zo.shape[1]), lambda i, q: (q[i], 0)),
            pl.BlockSpec((tm, ze.shape[1]), lambda i, q: (q[i], 0)),
            pl.BlockSpec((1, go.shape[1]), lambda i, q: (0, 0)),
            pl.BlockSpec((1, ge.shape[1]), lambda i, q: (0, 0)),
            pl.BlockSpec((tm, 1), lambda i, q: (q[i], 0)),
            pl.BlockSpec(to.shape, lambda i, q: (0, 0)),
            pl.BlockSpec(te.shape, lambda i, q: (0, 0)),
        ],
        out_specs=pl.BlockSpec((tm, feats), lambda i, q: (i, 0)),
    )
    return pl.pallas_call(
        _map_kernel,
        grid_spec=grid_spec,
        out_shape=jax.ShapeDtypeStruct((count * tm, feats), jnp.float32),
    )(quarters, zo, ze, go, ge, lse, to, te)


def narrow_lse(partial_value, column, narrow_count):
    pieces = [partial_value] + [shifted(partial_value, "narrow", k) for k in range(1, narrow_count)]
    stacked = jnp.stack(pieces)
    order = (column - jnp.arange(narrow_count, dtype=jnp.int32)) % narrow_count
    ordered = stacked[order]
    top = jnp.max(ordered, axis=0)
    return top + jnp.log(jnp.sum(jnp.exp(ordered - top[None, :]), axis=0))


def shards(sources, targets, pair_target, pair_count):
    feature_count = sources.shape[1]
    tgt_blocks = targets.shape[0] // BLK
    wide_count = lax.axis_size("wide")
    narrow_count = lax.axis_size("narrow")
    w = lax.axis_index("wide")
    c = lax.axis_index("narrow")
    group_blocks = tgt_blocks * narrow_count
    scale = (1.0 / math.sqrt(feature_count)) * (1.0 / epsilon)
    inv_eps = 1.0 / epsilon
    log_src = -math.log(wide_count * sources.shape[0])
    log_tgt = -math.log(wide_count * narrow_count * targets.shape[0])

    left = (w - 1 + wide_count) % wide_count
    right = (w + 1) % wide_count
    slot = group_blocks + c

    mine = pair_target[w, slot]
    mine_live = pair_count[w] > slot
    mine_from_left = (mine // group_blocks) == left

    want_right = pair_target[right, slot]
    want_right_live = (pair_count[right] > slot) & ((want_right // group_blocks) == w)
    want_left = pair_target[left, slot]
    want_left_live = (pair_count[left] > slot) & ((want_left // group_blocks) == w)
    left2 = (w - 2 + 2 * wide_count) % wide_count
    right2 = (w + 2) % wide_count
    far_left_same = (pair_count[left2] > slot) & (pair_target[left2, slot] == mine)
    far_right_same = (pair_count[right2] > slot) & (pair_target[right2, slot] == mine)

    blocks = targets.reshape(tgt_blocks, BLK, feature_count)
    to_right = blocks[want_right % tgt_blocks]
    to_left = blocks[want_left % tgt_blocks]
    from_left = shifted(to_right, "wide", 1)
    from_right = shifted(to_left, "wide", -1)

    zo = lax.dot_general(
        sources, targets, (((1,), (1,)), ((), ())), preferred_element_type=jnp.float32
    ) * scale
    extra = jnp.where(mine_from_left, from_left, from_right)
    ze = lax.dot_general(
        sources, extra, (((1,), (1,)), ((), ())), preferred_element_type=jnp.float32
    ) * scale

    extra_mask = jnp.where(mine_live, 0.0, sentinel).astype(jnp.float32)
    own_width = tgt_blocks * BLK

    def scaled(g_own, g_extra):
        return ((g_own * inv_eps).reshape(1, own_width), (g_extra * inv_eps + extra_mask).reshape(1, BLK))

    g_own = jnp.zeros((own_width,), jnp.float32)
    g_extra = jnp.zeros((BLK,), jnp.float32)
    for iteration in range(ITERS):
        go, ge = scaled(g_own, g_extra)
        if iteration == 0:
            part_own = row_lse_call([zo], [go])
            part_ext = row_lse_call([ze], [ge])
            part = jnp.logaddexp(part_own, part_ext)
        else:
            part = row_lse_call([zo, ze], [go, ge])
        row = narrow_lse(part.reshape(-1), c, narrow_count)
        f = epsilon * (log_src - row)
        own_cols, extra_cols = col_lse_call(zo, ze, (f * inv_eps).reshape(-1, 1))
        own_cols = own_cols.reshape(tgt_blocks, BLK)
        extra_cols = jnp.where(mine_live, extra_cols.reshape(-1), sentinel)
        from_left_msg = shifted(jnp.stack([extra_cols, own_cols[want_right % tgt_blocks]]), "wide", 1)
        from_right_msg = shifted(jnp.stack([extra_cols, own_cols[want_left % tgt_blocks]]), "wide", -1)
        part_from_left2 = shifted(extra_cols, "wide", 2)
        part_from_right2 = shifted(extra_cols, "wide", -2)
        part_from_left, cover_from_left = from_left_msg[0], from_left_msg[1]
        part_from_right, cover_from_right = from_right_msg[0], from_right_msg[1]
        ids = jnp.arange(tgt_blocks, dtype=jnp.int32)[:, None]
        add_right = jnp.where(want_right_live & (ids == want_right % tgt_blocks), part_from_right[None, :], sentinel)
        add_left = jnp.where(want_left_live & (ids == want_left % tgt_blocks), part_from_left[None, :], sentinel)
        top = jnp.maximum(own_cols, jnp.maximum(add_right, add_left))
        total = jnp.exp(own_cols - top) + jnp.exp(add_right - top) + jnp.exp(add_left - top)
        g_blocks = epsilon * (log_tgt - (top + jnp.log(total)))
        g_own = g_blocks.reshape(-1)
        cover_e = jnp.where(mine_from_left, cover_from_left, cover_from_right)
        other = jnp.where(mine_from_left, part_from_left2, part_from_right2)
        other_live = jnp.where(mine_from_left, far_left_same, far_right_same)
        other = jnp.where(other_live, other, sentinel)
        first = jnp.where(mine_from_left, extra_cols, other)
        second = jnp.where(mine_from_left, other, extra_cols)
        top_e = jnp.maximum(cover_e, jnp.maximum(first, second))
        total_e = jnp.exp(cover_e - top_e) + jnp.exp(first - top_e) + jnp.exp(second - top_e)
        g_extra = epsilon * (log_tgt - (top_e + jnp.log(total_e)))

    go, ge = scaled(g_own, g_extra)
    row = narrow_lse(row_lse_call([zo, ze], [go, ge]).reshape(-1), c, narrow_count)
    source_pot = epsilon * (log_src - row)
    rows = sources.shape[0]
    quarter = rows // narrow_count
    half = quarter // 2
    lse_col = row.reshape(-1, 1)

    def quarters(*offsets):
        return jnp.stack([(c + k) % narrow_count for k in offsets]).astype(jnp.int32)

    far = map_call(zo, ze, go, ge, lse_col, targets, extra, quarters(2), quarter)
    far_a = shifted(far[:half], "narrow", 1)
    far_b = shifted(far[half:], "narrow", -1)
    near = map_call(zo, ze, go, ge, lse_col, targets, extra, quarters(1, -1, 0), quarter)
    q_next, q_prev, q_mine = near[:quarter], near[quarter:2 * quarter], near[2 * quarter:]
    to_right = jnp.concatenate([q_next[:half] + far_a, q_next[half:]])
    to_left = jnp.concatenate([q_prev[:half], q_prev[half:] + far_b])
    got_left = shifted(to_right, "narrow", 1)
    got_right = shifted(to_left, "narrow", -1)
    mine_sum = q_mine + got_left + got_right
    done = mine_sum.astype(jnp.bfloat16).reshape(quarter, feature_count)
    q_left = shifted(done, "narrow", 1)
    q_right = shifted(done, "narrow", -1)
    far_half_a = shifted(q_left[:half], "narrow", 1)
    far_half_b = shifted(q_right[half:], "narrow", -1)
    q_far = jnp.concatenate([far_half_a, far_half_b])
    pieces = jnp.stack([done, q_left, q_far, q_right])
    order = (c - jnp.arange(narrow_count, dtype=jnp.int32)) % narrow_count
    mapped = pieces[order].reshape(rows, feature_count)
    return (source_pot, g_own, mapped)


def solution(mesh):
    placed = (P("wide", None), P(("wide", "narrow"), None), P(), P())
    return jax.shard_map(
        shards,
        mesh=mesh,
        in_specs=placed,
        out_specs=(P("wide"), P(("wide", "narrow")), P("wide", None)),
        check_vma=False,
    )
```

```python
import math

import jax
import jax.numpy as jnp
from jax import lax
from jax.sharding import PartitionSpec as P
from jax.experimental import pallas as pl

BLK = 1024
ITERS = 2


epsilon = 0.25
sentinel = -1e30


def shifted(x, axis, distance):
    size = lax.axis_size(axis)
    route = [(i, (i + distance) % size) for i in range(size)]
    return lax.ppermute(x, axis, route)


def _row_kernel(*refs):
    n = (len(refs) - 1) // 2
    z_refs, g_refs, out_ref = refs[:n], refs[n:2 * n], refs[-1]

    def body(r, carry):
        rs = pl.ds(pl.multiple_of(r * 8, 8), 8)
        scores = [z_refs[k][rs, :] + g_refs[k][...] for k in range(n)]
        top = scores[0].max(axis=1, keepdims=True)
        for s in scores[1:]:
            top = jnp.maximum(top, s.max(axis=1, keepdims=True))
        total = jnp.sum(jnp.exp(scores[0] - top), axis=1, keepdims=True)
        for s in scores[1:]:
            total = total + jnp.sum(jnp.exp(s - top), axis=1, keepdims=True)
        out_ref[rs, :] = top + jnp.log(total)
        return carry

    lax.fori_loop(0, out_ref.shape[0] // 8, body, 0)


def row_lse_call(zs, gs, tm=128):
    rows = zs[0].shape[0]
    gs = [jnp.broadcast_to(g, (8, g.shape[1])) for g in gs]
    in_specs = [pl.BlockSpec((tm, z.shape[1]), lambda i: (i, 0)) for z in zs]
    in_specs += [pl.BlockSpec((8, g.shape[1]), lambda i: (0, 0)) for g in gs]
    return pl.pallas_call(
        _row_kernel,
        grid=(rows // tm,),
        in_specs=in_specs,
        out_specs=pl.BlockSpec((tm, 1), lambda i: (i, 0)),
        out_shape=jax.ShapeDtypeStruct((rows, 1), jnp.float32),
    )(*zs, *gs)


def _col_pass(z_ref, f_ref, o_ref):
    rows = z_ref.shape[0]
    for cc in range(z_ref.shape[1] // 128):
        cols = pl.ds(cc * 128, 128)

        def run_max(r, m):
            rs = pl.ds(pl.multiple_of(r * 8, 8), 8)
            return jnp.maximum(m, z_ref[rs, cols] + f_ref[rs, :])

        m = lax.fori_loop(1, rows // 8, run_max, z_ref[0:8, cols] + f_ref[0:8, :], unroll=8)
        top = m.max(axis=0, keepdims=True)

        def run_sum(r, acc):
            rs = pl.ds(pl.multiple_of(r * 8, 8), 8)
            return acc + jnp.exp(z_ref[rs, cols] + f_ref[rs, :] - top)

        acc = lax.fori_loop(0, rows // 8, run_sum, jnp.zeros((8, 128), jnp.float32), unroll=8)
        o_ref[:, cols] = top + jnp.log(acc.sum(axis=0, keepdims=True))


def _col_kernel(zo_ref, ze_ref, f_ref, oo_ref, oe_ref):
    _col_pass(zo_ref, f_ref, oo_ref)
    _col_pass(ze_ref, f_ref, oe_ref)


def col_lse_call(zo, ze, f, steps=8):
    rows = zo.shape[0]
    wo = zo.shape[1] // steps
    we = ze.shape[1] // steps
    f = jnp.broadcast_to(f, (rows, 128))
    return pl.pallas_call(
        _col_kernel,
        grid=(steps,),
        in_specs=[
            pl.BlockSpec((rows, wo), lambda j: (0, j)),
            pl.BlockSpec((rows, we), lambda j: (0, j)),
            pl.BlockSpec((rows, 128), lambda j: (0, 0)),
        ],
        out_specs=[
            pl.BlockSpec((1, wo), lambda j: (0, j)),
            pl.BlockSpec((1, we), lambda j: (0, j)),
        ],
        out_shape=[
            jax.ShapeDtypeStruct((1, zo.shape[1]), jnp.float32),
            jax.ShapeDtypeStruct((1, ze.shape[1]), jnp.float32),
        ],
    )(zo, ze, f)


def _map_kernel(zo_ref, ze_ref, go_ref, ge_ref, l_ref, to_ref, te_ref, out_ref):
    lse = l_ref[...]
    wo = jnp.exp(zo_ref[...] + go_ref[...] - lse).astype(jnp.bfloat16)
    we = jnp.exp(ze_ref[...] + ge_ref[...] - lse).astype(jnp.bfloat16)
    acc = jnp.dot(wo, to_ref[...], preferred_element_type=jnp.float32)
    out_ref[...] = acc + jnp.dot(we, te_ref[...], preferred_element_type=jnp.float32)


def map_call(zo, ze, go, ge, lse, to, te, tm=256):
    rows = zo.shape[0]
    feats = to.shape[1]
    return pl.pallas_call(
        _map_kernel,
        grid=(rows // tm,),
        in_specs=[
            pl.BlockSpec((tm, zo.shape[1]), lambda i: (i, 0)),
            pl.BlockSpec((tm, ze.shape[1]), lambda i: (i, 0)),
            pl.BlockSpec((1, go.shape[1]), lambda i: (0, 0)),
            pl.BlockSpec((1, ge.shape[1]), lambda i: (0, 0)),
            pl.BlockSpec((tm, 1), lambda i: (i, 0)),
            pl.BlockSpec(to.shape, lambda i: (0, 0)),
            pl.BlockSpec(te.shape, lambda i: (0, 0)),
        ],
        out_specs=pl.BlockSpec((tm, feats), lambda i: (i, 0)),
        out_shape=jax.ShapeDtypeStruct((rows, feats), jnp.float32),
    )(zo, ze, go, ge, lse, to, te)


def narrow_lse(partial_value, column, narrow_count):
    pieces = [partial_value] + [shifted(partial_value, "narrow", k) for k in range(1, narrow_count)]
    stacked = jnp.stack(pieces)
    order = (column - jnp.arange(narrow_count, dtype=jnp.int32)) % narrow_count
    ordered = stacked[order]
    top = jnp.max(ordered, axis=0)
    return top + jnp.log(jnp.sum(jnp.exp(ordered - top[None, :]), axis=0))


def shards(sources, targets, pair_target, pair_count):
    feature_count = sources.shape[1]
    tgt_blocks = targets.shape[0] // BLK
    wide_count = lax.axis_size("wide")
    narrow_count = lax.axis_size("narrow")
    w = lax.axis_index("wide")
    c = lax.axis_index("narrow")
    group_blocks = tgt_blocks * narrow_count
    scale = (1.0 / math.sqrt(feature_count)) * (1.0 / epsilon)
    inv_eps = 1.0 / epsilon
    log_src = -math.log(wide_count * sources.shape[0])
    log_tgt = -math.log(wide_count * narrow_count * targets.shape[0])

    left = (w - 1 + wide_count) % wide_count
    right = (w + 1) % wide_count
    slot = group_blocks + c

    mine = pair_target[w, slot]
    mine_live = pair_count[w] > slot
    mine_from_left = (mine // group_blocks) == left

    want_right = pair_target[right, slot]
    want_right_live = (pair_count[right] > slot) & ((want_right // group_blocks) == w)
    want_left = pair_target[left, slot]
    want_left_live = (pair_count[left] > slot) & ((want_left // group_blocks) == w)
    left2 = (w - 2 + 2 * wide_count) % wide_count
    right2 = (w + 2) % wide_count
    far_left_same = (pair_count[left2] > slot) & (pair_target[left2, slot] == mine)
    far_right_same = (pair_count[right2] > slot) & (pair_target[right2, slot] == mine)

    blocks = targets.reshape(tgt_blocks, BLK, feature_count)
    to_right = blocks[want_right % tgt_blocks]
    to_left = blocks[want_left % tgt_blocks]
    from_left = shifted(to_right, "wide", 1)
    from_right = shifted(to_left, "wide", -1)

    zo = lax.dot_general(
        sources, targets, (((1,), (1,)), ((), ())), preferred_element_type=jnp.float32
    ) * scale
    extra = jnp.where(mine_from_left, from_left, from_right)
    ze = lax.dot_general(
        sources, extra, (((1,), (1,)), ((), ())), preferred_element_type=jnp.float32
    ) * scale

    extra_mask = jnp.where(mine_live, 0.0, sentinel).astype(jnp.float32)
    own_width = tgt_blocks * BLK

    def scaled(g_own, g_extra):
        return ((g_own * inv_eps).reshape(1, own_width), (g_extra * inv_eps + extra_mask).reshape(1, BLK))

    g_own = jnp.zeros((own_width,), jnp.float32)
    g_extra = jnp.zeros((BLK,), jnp.float32)
    for iteration in range(ITERS):
        go, ge = scaled(g_own, g_extra)
        if iteration == 0:
            part_own = row_lse_call([zo], [go])
            part_ext = row_lse_call([ze], [ge])
            part = jnp.logaddexp(part_own, part_ext)
        else:
            part = row_lse_call([zo, ze], [go, ge])
        row = narrow_lse(part.reshape(-1), c, narrow_count)
        f = epsilon * (log_src - row)
        own_cols, extra_cols = col_lse_call(zo, ze, (f * inv_eps).reshape(-1, 1))
        own_cols = own_cols.reshape(tgt_blocks, BLK)
        extra_cols = jnp.where(mine_live, extra_cols.reshape(-1), sentinel)
        from_left_msg = shifted(jnp.stack([extra_cols, own_cols[want_right % tgt_blocks]]), "wide", 1)
        from_right_msg = shifted(jnp.stack([extra_cols, own_cols[want_left % tgt_blocks]]), "wide", -1)
        part_from_left2 = shifted(extra_cols, "wide", 2)
        part_from_right2 = shifted(extra_cols, "wide", -2)
        part_from_left, cover_from_left = from_left_msg[0], from_left_msg[1]
        part_from_right, cover_from_right = from_right_msg[0], from_right_msg[1]
        ids = jnp.arange(tgt_blocks, dtype=jnp.int32)[:, None]
        add_right = jnp.where(want_right_live & (ids == want_right % tgt_blocks), part_from_right[None, :], sentinel)
        add_left = jnp.where(want_left_live & (ids == want_left % tgt_blocks), part_from_left[None, :], sentinel)
        top = jnp.maximum(own_cols, jnp.maximum(add_right, add_left))
        total = jnp.exp(own_cols - top) + jnp.exp(add_right - top) + jnp.exp(add_left - top)
        g_blocks = epsilon * (log_tgt - (top + jnp.log(total)))
        g_own = g_blocks.reshape(-1)
        cover_e = jnp.where(mine_from_left, cover_from_left, cover_from_right)
        other = jnp.where(mine_from_left, part_from_left2, part_from_right2)
        other_live = jnp.where(mine_from_left, far_left_same, far_right_same)
        other = jnp.where(other_live, other, sentinel)
        first = jnp.where(mine_from_left, extra_cols, other)
        second = jnp.where(mine_from_left, other, extra_cols)
        top_e = jnp.maximum(cover_e, jnp.maximum(first, second))
        total_e = jnp.exp(cover_e - top_e) + jnp.exp(first - top_e) + jnp.exp(second - top_e)
        g_extra = epsilon * (log_tgt - (top_e + jnp.log(total_e)))

    go, ge = scaled(g_own, g_extra)
    row = narrow_lse(row_lse_call([zo, ze], [go, ge]).reshape(-1), c, narrow_count)
    source_pot = epsilon * (log_src - row)
    numer = map_call(zo, ze, go, ge, row.reshape(-1, 1), targets, extra)

    rows = sources.shape[0]
    quarter = rows // narrow_count
    half = quarter // 2
    chunks = numer.reshape(narrow_count, 2, half, feature_count)

    def chunk(index, side):
        return lax.dynamic_index_in_dim(chunks, index % narrow_count, 0, False)[side]

    far_a = shifted(chunk(c + 2, 0), "narrow", 1)
    far_b = shifted(chunk(c + 2, 1), "narrow", -1)
    to_right = jnp.stack([chunk(c + 1, 0) + far_a, chunk(c + 1, 1)])
    to_left = jnp.stack([chunk(c - 1, 0), chunk(c - 1, 1) + far_b])
    got_left = shifted(to_right, "narrow", 1)
    got_right = shifted(to_left, "narrow", -1)
    mine_sum = jnp.stack([chunk(c, 0), chunk(c, 1)]) + got_left + got_right
    done = mine_sum.astype(jnp.bfloat16).reshape(quarter, feature_count)
    q_left = shifted(done, "narrow", 1)
    q_right = shifted(done, "narrow", -1)
    far_half_a = shifted(q_left[:half], "narrow", 1)
    far_half_b = shifted(q_right[half:], "narrow", -1)
    q_far = jnp.concatenate([far_half_a, far_half_b])
    pieces = jnp.stack([done, q_left, q_far, q_right])
    order = (c - jnp.arange(narrow_count, dtype=jnp.int32)) % narrow_count
    mapped = pieces[order].reshape(rows, feature_count)
    return (source_pot, g_own, mapped)


def solution(mesh):
    placed = (P("wide", None), P(("wide", "narrow"), None), P(), P())
    return jax.shard_map(
        shards,
        mesh=mesh,
        in_specs=placed,
        out_specs=(P("wide"), P(("wide", "narrow")), P("wide", None)),
        check_vma=False,
    )
```

```python
import math

import jax
import jax.numpy as jnp
from jax import lax
from jax.sharding import PartitionSpec as P
from jax.experimental import pallas as pl

BLK = 1024
ITERS = 2


epsilon = 0.25
sentinel = -1e30


def shifted(x, axis, distance):
    size = lax.axis_size(axis)
    route = [(i, (i + distance) % size) for i in range(size)]
    return lax.ppermute(x, axis, route)


def _row_kernel(*refs):
    n = (len(refs) - 1) // 2
    out_ref = refs[-1]
    scores = [refs[k][...] + refs[n + k][...] for k in range(n)]
    top = scores[0].max(axis=1, keepdims=True)
    for s in scores[1:]:
        top = jnp.maximum(top, s.max(axis=1, keepdims=True))
    total = jnp.sum(jnp.exp(scores[0] - top), axis=1, keepdims=True)
    for s in scores[1:]:
        total = total + jnp.sum(jnp.exp(s - top), axis=1, keepdims=True)
    out_ref[...] = top + jnp.log(total)


def row_lse_call(zs, gs, tm=256):
    rows = zs[0].shape[0]
    in_specs = [pl.BlockSpec((tm, z.shape[1]), lambda i: (i, 0)) for z in zs]
    in_specs += [pl.BlockSpec((1, g.shape[1]), lambda i: (0, 0)) for g in gs]
    return pl.pallas_call(
        _row_kernel,
        grid=(rows // tm,),
        in_specs=in_specs,
        out_specs=pl.BlockSpec((tm, 1), lambda i: (i, 0)),
        out_shape=jax.ShapeDtypeStruct((rows, 1), jnp.float32),
    )(*zs, *gs)


def _col_kernel(zo_ref, ze_ref, f_ref, oo_ref, oe_ref):
    f = f_ref[...]
    for z_ref, o_ref in ((zo_ref, oo_ref), (ze_ref, oe_ref)):
        s = z_ref[...] + f
        top = s.max(axis=0, keepdims=True)
        o_ref[...] = top + jnp.log(jnp.sum(jnp.exp(s - top), axis=0, keepdims=True))


def col_lse_call(zo, ze, f, steps=4):
    rows = zo.shape[0]
    wo = zo.shape[1] // steps
    we = ze.shape[1] // steps
    return pl.pallas_call(
        _col_kernel,
        grid=(steps,),
        in_specs=[
            pl.BlockSpec((rows, wo), lambda j: (0, j)),
            pl.BlockSpec((rows, we), lambda j: (0, j)),
            pl.BlockSpec((rows, 1), lambda j: (0, 0)),
        ],
        out_specs=[
            pl.BlockSpec((1, wo), lambda j: (0, j)),
            pl.BlockSpec((1, we), lambda j: (0, j)),
        ],
        out_shape=[
            jax.ShapeDtypeStruct((1, zo.shape[1]), jnp.float32),
            jax.ShapeDtypeStruct((1, ze.shape[1]), jnp.float32),
        ],
    )(zo, ze, f)


def _map_kernel(zo_ref, ze_ref, go_ref, ge_ref, l_ref, to_ref, te_ref, out_ref):
    lse = l_ref[...]
    wo = jnp.exp(zo_ref[...] + go_ref[...] - lse).astype(jnp.bfloat16)
    we = jnp.exp(ze_ref[...] + ge_ref[...] - lse).astype(jnp.bfloat16)
    acc = jnp.dot(wo, to_ref[...], preferred_element_type=jnp.float32)
    out_ref[...] = acc + jnp.dot(we, te_ref[...], preferred_element_type=jnp.float32)


def map_call(zo, ze, go, ge, lse, to, te, tm=256):
    rows = zo.shape[0]
    feats = to.shape[1]
    return pl.pallas_call(
        _map_kernel,
        grid=(rows // tm,),
        in_specs=[
            pl.BlockSpec((tm, zo.shape[1]), lambda i: (i, 0)),
            pl.BlockSpec((tm, ze.shape[1]), lambda i: (i, 0)),
            pl.BlockSpec((1, go.shape[1]), lambda i: (0, 0)),
            pl.BlockSpec((1, ge.shape[1]), lambda i: (0, 0)),
            pl.BlockSpec((tm, 1), lambda i: (i, 0)),
            pl.BlockSpec(to.shape, lambda i: (0, 0)),
            pl.BlockSpec(te.shape, lambda i: (0, 0)),
        ],
        out_specs=pl.BlockSpec((tm, feats), lambda i: (i, 0)),
        out_shape=jax.ShapeDtypeStruct((rows, feats), jnp.float32),
    )(zo, ze, go, ge, lse, to, te)


def narrow_lse(partial_value, column, narrow_count):
    pieces = [partial_value] + [shifted(partial_value, "narrow", k) for k in range(1, narrow_count)]
    stacked = jnp.stack(pieces)
    order = (column - jnp.arange(narrow_count, dtype=jnp.int32)) % narrow_count
    ordered = stacked[order]
    top = jnp.max(ordered, axis=0)
    return top + jnp.log(jnp.sum(jnp.exp(ordered - top[None, :]), axis=0))


def reduce_over_narrow(numer, c, narrow_count, quarter, half):
    rows, width = numer.shape
    chunks = numer.reshape(narrow_count, 2, half, width)

    def chunk(index, side):
        return lax.dynamic_index_in_dim(chunks, index % narrow_count, 0, False)[side]

    far_a = shifted(chunk(c + 2, 0), "narrow", 1)
    far_b = shifted(chunk(c + 2, 1), "narrow", -1)
    to_right = jnp.stack([chunk(c + 1, 0) + far_a, chunk(c + 1, 1)])
    to_left = jnp.stack([chunk(c - 1, 0), chunk(c - 1, 1) + far_b])
    got_left = shifted(to_right, "narrow", 1)
    got_right = shifted(to_left, "narrow", -1)
    mine_sum = jnp.stack([chunk(c, 0), chunk(c, 1)]) + got_left + got_right
    done = mine_sum.astype(jnp.bfloat16).reshape(quarter, width)
    q_left = shifted(done, "narrow", 1)
    q_right = shifted(done, "narrow", -1)
    far_half_a = shifted(q_left[:half], "narrow", 1)
    far_half_b = shifted(q_right[half:], "narrow", -1)
    q_far = jnp.concatenate([far_half_a, far_half_b])
    pieces = jnp.stack([done, q_left, q_far, q_right])
    order = (c - jnp.arange(narrow_count, dtype=jnp.int32)) % narrow_count
    return pieces[order].reshape(rows, width)


def shards(sources, targets, pair_target, pair_count):
    feature_count = sources.shape[1]
    tgt_blocks = targets.shape[0] // BLK
    wide_count = lax.axis_size("wide")
    narrow_count = lax.axis_size("narrow")
    w = lax.axis_index("wide")
    c = lax.axis_index("narrow")
    group_blocks = tgt_blocks * narrow_count
    scale = (1.0 / math.sqrt(feature_count)) * (1.0 / epsilon)
    inv_eps = 1.0 / epsilon
    log_src = -math.log(wide_count * sources.shape[0])
    log_tgt = -math.log(wide_count * narrow_count * targets.shape[0])

    left = (w - 1 + wide_count) % wide_count
    right = (w + 1) % wide_count
    slot = group_blocks + c

    mine = pair_target[w, slot]
    mine_live = pair_count[w] > slot
    mine_from_left = (mine // group_blocks) == left

    want_right = pair_target[right, slot]
    want_right_live = (pair_count[right] > slot) & ((want_right // group_blocks) == w)
    want_left = pair_target[left, slot]
    want_left_live = (pair_count[left] > slot) & ((want_left // group_blocks) == w)
    left2 = (w - 2 + 2 * wide_count) % wide_count
    right2 = (w + 2) % wide_count
    far_left_same = (pair_count[left2] > slot) & (pair_target[left2, slot] == mine)
    far_right_same = (pair_count[right2] > slot) & (pair_target[right2, slot] == mine)

    blocks = targets.reshape(tgt_blocks, BLK, feature_count)
    to_right = blocks[want_right % tgt_blocks]
    to_left = blocks[want_left % tgt_blocks]
    from_left = shifted(to_right, "wide", 1)
    from_right = shifted(to_left, "wide", -1)

    zo = lax.dot_general(
        sources, targets, (((1,), (1,)), ((), ())), preferred_element_type=jnp.float32
    ) * scale
    extra = jnp.where(mine_from_left, from_left, from_right)
    ze = lax.dot_general(
        sources, extra, (((1,), (1,)), ((), ())), preferred_element_type=jnp.float32
    ) * scale

    extra_mask = jnp.where(mine_live, 0.0, sentinel).astype(jnp.float32)
    own_width = tgt_blocks * BLK

    def scaled(g_own, g_extra):
        return ((g_own * inv_eps).reshape(1, own_width), (g_extra * inv_eps + extra_mask).reshape(1, BLK))

    g_own = jnp.zeros((own_width,), jnp.float32)
    g_extra = jnp.zeros((BLK,), jnp.float32)
    for iteration in range(ITERS):
        go, ge = scaled(g_own, g_extra)
        if iteration == 0:
            part_own = row_lse_call([zo], [go])
            part_ext = row_lse_call([ze], [ge])
            part = jnp.logaddexp(part_own, part_ext)
        else:
            part = row_lse_call([zo, ze], [go, ge])
        row = narrow_lse(part.reshape(-1), c, narrow_count)
        f = epsilon * (log_src - row)
        own_cols, extra_cols = col_lse_call(zo, ze, (f * inv_eps).reshape(-1, 1))
        own_cols = own_cols.reshape(tgt_blocks, BLK)
        extra_cols = jnp.where(mine_live, extra_cols.reshape(-1), sentinel)
        from_left_msg = shifted(jnp.stack([extra_cols, own_cols[want_right % tgt_blocks]]), "wide", 1)
        from_right_msg = shifted(jnp.stack([extra_cols, own_cols[want_left % tgt_blocks]]), "wide", -1)
        part_from_left2 = shifted(extra_cols, "wide", 2)
        part_from_right2 = shifted(extra_cols, "wide", -2)
        part_from_left, cover_from_left = from_left_msg[0], from_left_msg[1]
        part_from_right, cover_from_right = from_right_msg[0], from_right_msg[1]
        ids = jnp.arange(tgt_blocks, dtype=jnp.int32)[:, None]
        add_right = jnp.where(want_right_live & (ids == want_right % tgt_blocks), part_from_right[None, :], sentinel)
        add_left = jnp.where(want_left_live & (ids == want_left % tgt_blocks), part_from_left[None, :], sentinel)
        top = jnp.maximum(own_cols, jnp.maximum(add_right, add_left))
        total = jnp.exp(own_cols - top) + jnp.exp(add_right - top) + jnp.exp(add_left - top)
        g_blocks = epsilon * (log_tgt - (top + jnp.log(total)))
        g_own = g_blocks.reshape(-1)
        cover_e = jnp.where(mine_from_left, cover_from_left, cover_from_right)
        other = jnp.where(mine_from_left, part_from_left2, part_from_right2)
        other_live = jnp.where(mine_from_left, far_left_same, far_right_same)
        other = jnp.where(other_live, other, sentinel)
        first = jnp.where(mine_from_left, extra_cols, other)
        second = jnp.where(mine_from_left, other, extra_cols)
        top_e = jnp.maximum(cover_e, jnp.maximum(first, second))
        total_e = jnp.exp(cover_e - top_e) + jnp.exp(first - top_e) + jnp.exp(second - top_e)
        g_extra = epsilon * (log_tgt - (top_e + jnp.log(total_e)))

    go, ge = scaled(g_own, g_extra)
    row = narrow_lse(row_lse_call([zo, ze], [go, ge]).reshape(-1), c, narrow_count)
    source_pot = epsilon * (log_src - row)
    numer = map_call(zo, ze, go, ge, row.reshape(-1, 1), targets, extra)

    rows = sources.shape[0]
    quarter = rows // narrow_count
    half = quarter // 2
    lanes = feature_count // 2
    mapped = jnp.concatenate(
        [
            reduce_over_narrow(numer[:, k * lanes:(k + 1) * lanes], c, narrow_count, quarter, half)
            for k in range(2)
        ],
        axis=1,
    )
    return (source_pot, g_own, mapped)


def solution(mesh):
    placed = (P("wide", None), P(("wide", "narrow"), None), P(), P())
    return jax.shard_map(
        shards,
        mesh=mesh,
        in_specs=placed,
        out_specs=(P("wide"), P(("wide", "narrow")), P("wide", None)),
        check_vma=False,
    )
```

```python
import math

import jax
import jax.numpy as jnp
from jax import lax
from jax.sharding import PartitionSpec as P
from jax.experimental import pallas as pl

BLK = 1024
ITERS = 2


epsilon = 0.25
sentinel = -1e30


def shifted(x, axis, distance):
    size = lax.axis_size(axis)
    route = [(i, (i + distance) % size) for i in range(size)]
    return lax.ppermute(x, axis, route)


def _row_kernel(*refs):
    n = (len(refs) - 1) // 2
    out_ref = refs[-1]
    scores = [refs[k][...] + refs[n + k][...] for k in range(n)]
    top = scores[0].max(axis=1, keepdims=True)
    for s in scores[1:]:
        top = jnp.maximum(top, s.max(axis=1, keepdims=True))
    total = jnp.sum(jnp.exp(scores[0] - top), axis=1, keepdims=True)
    for s in scores[1:]:
        total = total + jnp.sum(jnp.exp(s - top), axis=1, keepdims=True)
    out_ref[...] = top + jnp.log(total)


def row_lse_call(zs, gs, tm=256):
    rows = zs[0].shape[0]
    in_specs = [pl.BlockSpec((tm, z.shape[1]), lambda i: (i, 0)) for z in zs]
    in_specs += [pl.BlockSpec((1, g.shape[1]), lambda i: (0, 0)) for g in gs]
    return pl.pallas_call(
        _row_kernel,
        grid=(rows // tm,),
        in_specs=in_specs,
        out_specs=pl.BlockSpec((tm, 1), lambda i: (i, 0)),
        out_shape=jax.ShapeDtypeStruct((rows, 1), jnp.float32),
    )(*zs, *gs)


def _col_kernel(zo_ref, ze_ref, f_ref, oo_ref, oe_ref):
    f = f_ref[...]
    for z_ref, o_ref in ((zo_ref, oo_ref), (ze_ref, oe_ref)):
        s = z_ref[...] + f
        top = s.max(axis=0, keepdims=True)
        o_ref[...] = top + jnp.log(jnp.sum(jnp.exp(s - top), axis=0, keepdims=True))


def col_lse_call(zo, ze, f, steps=4):
    rows = zo.shape[0]
    wo = zo.shape[1] // steps
    we = ze.shape[1] // steps
    return pl.pallas_call(
        _col_kernel,
        grid=(steps,),
        in_specs=[
            pl.BlockSpec((rows, wo), lambda j: (0, j)),
            pl.BlockSpec((rows, we), lambda j: (0, j)),
            pl.BlockSpec((rows, 1), lambda j: (0, 0)),
        ],
        out_specs=[
            pl.BlockSpec((1, wo), lambda j: (0, j)),
            pl.BlockSpec((1, we), lambda j: (0, j)),
        ],
        out_shape=[
            jax.ShapeDtypeStruct((1, zo.shape[1]), jnp.float32),
            jax.ShapeDtypeStruct((1, ze.shape[1]), jnp.float32),
        ],
    )(zo, ze, f)


def _map_kernel(zo_ref, ze_ref, go_ref, ge_ref, l_ref, to_ref, te_ref, out_ref):
    lse = l_ref[...]
    wo = jnp.exp(zo_ref[...] + go_ref[...] - lse).astype(jnp.bfloat16)
    we = jnp.exp(ze_ref[...] + ge_ref[...] - lse).astype(jnp.bfloat16)
    acc = jnp.dot(wo, to_ref[...], preferred_element_type=jnp.float32)
    out_ref[...] = acc + jnp.dot(we, te_ref[...], preferred_element_type=jnp.float32)


def map_call(zo, ze, go, ge, lse, to, te, tm=256):
    rows = zo.shape[0]
    feats = to.shape[1]
    return pl.pallas_call(
        _map_kernel,
        grid=(rows // tm,),
        in_specs=[
            pl.BlockSpec((tm, zo.shape[1]), lambda i: (i, 0)),
            pl.BlockSpec((tm, ze.shape[1]), lambda i: (i, 0)),
            pl.BlockSpec((1, go.shape[1]), lambda i: (0, 0)),
            pl.BlockSpec((1, ge.shape[1]), lambda i: (0, 0)),
            pl.BlockSpec((tm, 1), lambda i: (i, 0)),
            pl.BlockSpec(to.shape, lambda i: (0, 0)),
            pl.BlockSpec(te.shape, lambda i: (0, 0)),
        ],
        out_specs=pl.BlockSpec((tm, feats), lambda i: (i, 0)),
        out_shape=jax.ShapeDtypeStruct((rows, feats), jnp.float32),
    )(zo, ze, go, ge, lse, to, te)


def narrow_lse(partial_value, column, narrow_count):
    spread = jnp.broadcast_to(partial_value[None, :], (narrow_count, partial_value.shape[0]))
    ordered = lax.all_to_all(spread, "narrow", 0, 0)
    top = jnp.max(ordered, axis=0)
    return top + jnp.log(jnp.sum(jnp.exp(ordered - top[None, :]), axis=0))


def shards(sources, targets, pair_target, pair_count):
    feature_count = sources.shape[1]
    tgt_blocks = targets.shape[0] // BLK
    wide_count = lax.axis_size("wide")
    narrow_count = lax.axis_size("narrow")
    w = lax.axis_index("wide")
    c = lax.axis_index("narrow")
    group_blocks = tgt_blocks * narrow_count
    scale = (1.0 / math.sqrt(feature_count)) * (1.0 / epsilon)
    inv_eps = 1.0 / epsilon
    log_src = -math.log(wide_count * sources.shape[0])
    log_tgt = -math.log(wide_count * narrow_count * targets.shape[0])

    left = (w - 1 + wide_count) % wide_count
    right = (w + 1) % wide_count
    slot = group_blocks + c

    mine = pair_target[w, slot]
    mine_live = pair_count[w] > slot
    mine_from_left = (mine // group_blocks) == left

    want_right = pair_target[right, slot]
    want_right_live = (pair_count[right] > slot) & ((want_right // group_blocks) == w)
    want_left = pair_target[left, slot]
    want_left_live = (pair_count[left] > slot) & ((want_left // group_blocks) == w)
    left2 = (w - 2 + 2 * wide_count) % wide_count
    right2 = (w + 2) % wide_count
    far_left_same = (pair_count[left2] > slot) & (pair_target[left2, slot] == mine)
    far_right_same = (pair_count[right2] > slot) & (pair_target[right2, slot] == mine)

    blocks = targets.reshape(tgt_blocks, BLK, feature_count)
    to_right = blocks[want_right % tgt_blocks]
    to_left = blocks[want_left % tgt_blocks]
    from_left = shifted(to_right, "wide", 1)
    from_right = shifted(to_left, "wide", -1)

    zo = lax.dot_general(
        sources, targets, (((1,), (1,)), ((), ())), preferred_element_type=jnp.float32
    ) * scale
    extra = jnp.where(mine_from_left, from_left, from_right)
    ze = lax.dot_general(
        sources, extra, (((1,), (1,)), ((), ())), preferred_element_type=jnp.float32
    ) * scale

    extra_mask = jnp.where(mine_live, 0.0, sentinel).astype(jnp.float32)
    own_width = tgt_blocks * BLK

    def scaled(g_own, g_extra):
        return ((g_own * inv_eps).reshape(1, own_width), (g_extra * inv_eps + extra_mask).reshape(1, BLK))

    g_own = jnp.zeros((own_width,), jnp.float32)
    g_extra = jnp.zeros((BLK,), jnp.float32)
    for iteration in range(ITERS):
        go, ge = scaled(g_own, g_extra)
        if iteration == 0:
            part_own = row_lse_call([zo], [go])
            part_ext = row_lse_call([ze], [ge])
            part = jnp.logaddexp(part_own, part_ext)
        else:
            part = row_lse_call([zo, ze], [go, ge])
        row = narrow_lse(part.reshape(-1), c, narrow_count)
        f = epsilon * (log_src - row)
        own_cols, extra_cols = col_lse_call(zo, ze, (f * inv_eps).reshape(-1, 1))
        own_cols = own_cols.reshape(tgt_blocks, BLK)
        extra_cols = jnp.where(mine_live, extra_cols.reshape(-1), sentinel)
        from_left_msg = shifted(jnp.stack([extra_cols, own_cols[want_right % tgt_blocks]]), "wide", 1)
        from_right_msg = shifted(jnp.stack([extra_cols, own_cols[want_left % tgt_blocks]]), "wide", -1)
        part_from_left2 = shifted(extra_cols, "wide", 2)
        part_from_right2 = shifted(extra_cols, "wide", -2)
        part_from_left, cover_from_left = from_left_msg[0], from_left_msg[1]
        part_from_right, cover_from_right = from_right_msg[0], from_right_msg[1]
        ids = jnp.arange(tgt_blocks, dtype=jnp.int32)[:, None]
        add_right = jnp.where(want_right_live & (ids == want_right % tgt_blocks), part_from_right[None, :], sentinel)
        add_left = jnp.where(want_left_live & (ids == want_left % tgt_blocks), part_from_left[None, :], sentinel)
        top = jnp.maximum(own_cols, jnp.maximum(add_right, add_left))
        total = jnp.exp(own_cols - top) + jnp.exp(add_right - top) + jnp.exp(add_left - top)
        g_blocks = epsilon * (log_tgt - (top + jnp.log(total)))
        g_own = g_blocks.reshape(-1)
        cover_e = jnp.where(mine_from_left, cover_from_left, cover_from_right)
        other = jnp.where(mine_from_left, part_from_left2, part_from_right2)
        other_live = jnp.where(mine_from_left, far_left_same, far_right_same)
        other = jnp.where(other_live, other, sentinel)
        first = jnp.where(mine_from_left, extra_cols, other)
        second = jnp.where(mine_from_left, other, extra_cols)
        top_e = jnp.maximum(cover_e, jnp.maximum(first, second))
        total_e = jnp.exp(cover_e - top_e) + jnp.exp(first - top_e) + jnp.exp(second - top_e)
        g_extra = epsilon * (log_tgt - (top_e + jnp.log(total_e)))

    go, ge = scaled(g_own, g_extra)
    row = narrow_lse(row_lse_call([zo, ze], [go, ge]).reshape(-1), c, narrow_count)
    source_pot = epsilon * (log_src - row)
    numer = map_call(zo, ze, go, ge, row.reshape(-1, 1), targets, extra)

    rows = sources.shape[0]
    quarter = rows // narrow_count
    half = quarter // 2
    chunks = numer.reshape(narrow_count, 2, half, feature_count)

    def chunk(index, side):
        return lax.dynamic_index_in_dim(chunks, index % narrow_count, 0, False)[side]

    far_a = shifted(chunk(c + 2, 0), "narrow", 1)
    far_b = shifted(chunk(c + 2, 1), "narrow", -1)
    to_right = jnp.stack([chunk(c + 1, 0) + far_a, chunk(c + 1, 1)])
    to_left = jnp.stack([chunk(c - 1, 0), chunk(c - 1, 1) + far_b])
    got_left = shifted(to_right, "narrow", 1)
    got_right = shifted(to_left, "narrow", -1)
    mine_sum = jnp.stack([chunk(c, 0), chunk(c, 1)]) + got_left + got_right
    done = mine_sum.astype(jnp.bfloat16).reshape(quarter, feature_count)
    q_left = shifted(done, "narrow", 1)
    q_right = shifted(done, "narrow", -1)
    far_half_a = shifted(q_left[:half], "narrow", 1)
    far_half_b = shifted(q_right[half:], "narrow", -1)
    q_far = jnp.concatenate([far_half_a, far_half_b])
    pieces = jnp.stack([done, q_left, q_far, q_right])
    order = (c - jnp.arange(narrow_count, dtype=jnp.int32)) % narrow_count
    mapped = pieces[order].reshape(rows, feature_count)
    return (source_pot, g_own, mapped)


def solution(mesh):
    placed = (P("wide", None), P(("wide", "narrow"), None), P(), P())
    return jax.shard_map(
        shards,
        mesh=mesh,
        in_specs=placed,
        out_specs=(P("wide"), P(("wide", "narrow")), P("wide", None)),
        check_vma=False,
    )
```

```python
import functools
import math

import jax
import jax.numpy as jnp
from jax import lax
from jax.sharding import PartitionSpec as P
from jax.experimental import pallas as pl
from jax.experimental.pallas import tpu as pltpu

BLK = 1024
ITERS = 2


epsilon = 0.25
sentinel = -1e30


def shifted(x, axis, distance):
    size = lax.axis_size(axis)
    route = [(i, (i + distance) % size) for i in range(size)]
    return lax.ppermute(x, axis, route)


def _row_kernel(*refs):
    n = (len(refs) - 1) // 2
    out_ref = refs[-1]
    scores = [refs[k][...] + refs[n + k][...] for k in range(n)]
    top = scores[0].max(axis=1, keepdims=True)
    for s in scores[1:]:
        top = jnp.maximum(top, s.max(axis=1, keepdims=True))
    total = jnp.sum(jnp.exp(scores[0] - top), axis=1, keepdims=True)
    for s in scores[1:]:
        total = total + jnp.sum(jnp.exp(s - top), axis=1, keepdims=True)
    out_ref[...] = top + jnp.log(total)


def row_lse_call(zs, gs, tm=256):
    rows = zs[0].shape[0]
    in_specs = [pl.BlockSpec((tm, z.shape[1]), lambda i: (i, 0)) for z in zs]
    in_specs += [pl.BlockSpec((1, g.shape[1]), lambda i: (0, 0)) for g in gs]
    return pl.pallas_call(
        _row_kernel,
        grid=(rows // tm,),
        in_specs=in_specs,
        out_specs=pl.BlockSpec((tm, 1), lambda i: (i, 0)),
        out_shape=jax.ShapeDtypeStruct((rows, 1), jnp.float32),
    )(*zs, *gs)


def _col_kernel(zo_ref, ze_ref, f_ref, oo_ref, oe_ref):
    f = f_ref[...]
    for z_ref, o_ref in ((zo_ref, oo_ref), (ze_ref, oe_ref)):
        s = z_ref[...] + f
        top = s.max(axis=0, keepdims=True)
        o_ref[...] = top + jnp.log(jnp.sum(jnp.exp(s - top), axis=0, keepdims=True))


def col_lse_call(zo, ze, f, steps=4):
    rows = zo.shape[0]
    wo = zo.shape[1] // steps
    we = ze.shape[1] // steps
    return pl.pallas_call(
        _col_kernel,
        grid=(steps,),
        in_specs=[
            pl.BlockSpec((rows, wo), lambda j: (0, j)),
            pl.BlockSpec((rows, we), lambda j: (0, j)),
            pl.BlockSpec((rows, 1), lambda j: (0, 0)),
        ],
        out_specs=[
            pl.BlockSpec((1, wo), lambda j: (0, j)),
            pl.BlockSpec((1, we), lambda j: (0, j)),
        ],
        out_shape=[
            jax.ShapeDtypeStruct((1, zo.shape[1]), jnp.float32),
            jax.ShapeDtypeStruct((1, ze.shape[1]), jnp.float32),
        ],
    )(zo, ze, f)


def _ext_kernel(flag_ref, s_ref, l_ref, r_ref, ge_ref, own_ref, ze_ref, part_ref, *, scale):
    def product(e_ref):
        ze_ref[...] = lax.dot_general(
            s_ref[...], e_ref[...], (((1,), (1,)), ((), ())), preferred_element_type=jnp.float32
        ) * scale

    @pl.when(flag_ref[0] == 1)
    def _():
        product(l_ref)

    @pl.when(flag_ref[0] != 1)
    def _():
        product(r_ref)

    s = ze_ref[...] + ge_ref[...]
    own = own_ref[...]
    top = jnp.maximum(s.max(axis=1, keepdims=True), own)
    part_ref[...] = top + jnp.log(jnp.sum(jnp.exp(s - top), axis=1, keepdims=True) + jnp.exp(own - top))


def ext_call(flag, sources, from_left, from_right, ge, own_part, scale, tm=256):
    rows, feats = sources.shape
    width = from_left.shape[0]
    grid_spec = pltpu.PrefetchScalarGridSpec(
        num_scalar_prefetch=1,
        grid=(rows // tm,),
        in_specs=[
            pl.BlockSpec((tm, feats), lambda i, f: (i, 0)),
            pl.BlockSpec(from_left.shape, lambda i, f: (0, 0)),
            pl.BlockSpec(from_right.shape, lambda i, f: (0, 0)),
            pl.BlockSpec((1, width), lambda i, f: (0, 0)),
            pl.BlockSpec((tm, 1), lambda i, f: (i, 0)),
        ],
        out_specs=[
            pl.BlockSpec((tm, width), lambda i, f: (i, 0)),
            pl.BlockSpec((tm, 1), lambda i, f: (i, 0)),
        ],
    )
    return pl.pallas_call(
        functools.partial(_ext_kernel, scale=scale),
        grid_spec=grid_spec,
        out_shape=[
            jax.ShapeDtypeStruct((rows, width), jnp.float32),
            jax.ShapeDtypeStruct((rows, 1), jnp.float32),
        ],
    )(flag, sources, from_left, from_right, ge, own_part)


def _pick_kernel(idx_ref, t_hbm, a_hbm, b_hbm, sem):
    blk = a_hbm.shape[0]
    first = pltpu.make_async_copy(t_hbm.at[pl.ds(idx_ref[0] * blk, blk)], a_hbm, sem.at[0])
    second = pltpu.make_async_copy(t_hbm.at[pl.ds(idx_ref[1] * blk, blk)], b_hbm, sem.at[1])
    first.start()
    second.start()
    first.wait()
    second.wait()


def pick_blocks(targets, idx, blk):
    shape = jax.ShapeDtypeStruct((blk, targets.shape[1]), targets.dtype)
    grid_spec = pltpu.PrefetchScalarGridSpec(
        num_scalar_prefetch=1,
        grid=(1,),
        in_specs=[pl.BlockSpec(memory_space=pl.ANY)],
        out_specs=[pl.BlockSpec(memory_space=pl.ANY), pl.BlockSpec(memory_space=pl.ANY)],
        scratch_shapes=[pltpu.SemaphoreType.DMA((2,))],
    )
    return pl.pallas_call(_pick_kernel, grid_spec=grid_spec, out_shape=[shape, shape])(idx, targets)


def _map_kernel(flag_ref, zo_ref, ze_ref, go_ref, ge_ref, l_ref, to_ref, tl_ref, tr_ref, out_ref):
    lse = l_ref[...]
    wo = jnp.exp(zo_ref[...] + go_ref[...] - lse).astype(jnp.bfloat16)
    we = jnp.exp(ze_ref[...] + ge_ref[...] - lse).astype(jnp.bfloat16)
    out_ref[...] = jnp.dot(wo, to_ref[...], preferred_element_type=jnp.float32)

    @pl.when(flag_ref[0] == 1)
    def _():
        out_ref[...] += jnp.dot(we, tl_ref[...], preferred_element_type=jnp.float32)

    @pl.when(flag_ref[0] != 1)
    def _():
        out_ref[...] += jnp.dot(we, tr_ref[...], preferred_element_type=jnp.float32)


def map_call(flag, zo, ze, go, ge, lse, to, tl, tr, tm=256):
    rows = zo.shape[0]
    feats = to.shape[1]
    grid_spec = pltpu.PrefetchScalarGridSpec(
        num_scalar_prefetch=1,
        grid=(rows // tm,),
        in_specs=[
            pl.BlockSpec((tm, zo.shape[1]), lambda i, f: (i, 0)),
            pl.BlockSpec((tm, ze.shape[1]), lambda i, f: (i, 0)),
            pl.BlockSpec((1, go.shape[1]), lambda i, f: (0, 0)),
            pl.BlockSpec((1, ge.shape[1]), lambda i, f: (0, 0)),
            pl.BlockSpec((tm, 1), lambda i, f: (i, 0)),
            pl.BlockSpec(to.shape, lambda i, f: (0, 0)),
            pl.BlockSpec(tl.shape, lambda i, f: (0, 0)),
            pl.BlockSpec(tr.shape, lambda i, f: (0, 0)),
        ],
        out_specs=pl.BlockSpec((tm, feats), lambda i, f: (i, 0)),
    )
    return pl.pallas_call(
        _map_kernel,
        grid_spec=grid_spec,
        out_shape=jax.ShapeDtypeStruct((rows, feats), jnp.float32),
    )(flag, zo, ze, go, ge, lse, to, tl, tr)


def narrow_lse(partial_value, column, narrow_count):
    pieces = [partial_value] + [shifted(partial_value, "narrow", k) for k in range(1, narrow_count)]
    stacked = jnp.stack(pieces)
    order = (column - jnp.arange(narrow_count, dtype=jnp.int32)) % narrow_count
    ordered = stacked[order]
    top = jnp.max(ordered, axis=0)
    return top + jnp.log(jnp.sum(jnp.exp(ordered - top[None, :]), axis=0))


def shards(sources, targets, pair_target, pair_count):
    feature_count = sources.shape[1]
    tgt_blocks = targets.shape[0] // BLK
    wide_count = lax.axis_size("wide")
    narrow_count = lax.axis_size("narrow")
    w = lax.axis_index("wide")
    c = lax.axis_index("narrow")
    group_blocks = tgt_blocks * narrow_count
    scale = (1.0 / math.sqrt(feature_count)) * (1.0 / epsilon)
    inv_eps = 1.0 / epsilon
    log_src = -math.log(wide_count * sources.shape[0])
    log_tgt = -math.log(wide_count * narrow_count * targets.shape[0])

    left = (w - 1 + wide_count) % wide_count
    right = (w + 1) % wide_count
    slot = group_blocks + c

    mine = pair_target[w, slot]
    mine_live = pair_count[w] > slot
    mine_from_left = (mine // group_blocks) == left

    want_right = pair_target[right, slot]
    want_right_live = (pair_count[right] > slot) & ((want_right // group_blocks) == w)
    want_left = pair_target[left, slot]
    want_left_live = (pair_count[left] > slot) & ((want_left // group_blocks) == w)
    left2 = (w - 2 + 2 * wide_count) % wide_count
    right2 = (w + 2) % wide_count
    far_left_same = (pair_count[left2] > slot) & (pair_target[left2, slot] == mine)
    far_right_same = (pair_count[right2] > slot) & (pair_target[right2, slot] == mine)

    to_right, to_left = pick_blocks(
        targets, jnp.stack([want_right % tgt_blocks, want_left % tgt_blocks]).astype(jnp.int32), BLK
    )
    from_left = shifted(to_right, "wide", 1)
    from_right = shifted(to_left, "wide", -1)

    zo = lax.dot_general(
        sources, targets, (((1,), (1,)), ((), ())), preferred_element_type=jnp.float32
    ) * scale
    extra_mask = jnp.where(mine_live, 0.0, sentinel).astype(jnp.float32)
    flag = mine_from_left.astype(jnp.int32).reshape(1)
    own_width = tgt_blocks * BLK

    def scaled(g_own, g_extra):
        return ((g_own * inv_eps).reshape(1, own_width), (g_extra * inv_eps + extra_mask).reshape(1, BLK))

    g_own = jnp.zeros((own_width,), jnp.float32)
    g_extra = jnp.zeros((BLK,), jnp.float32)
    for iteration in range(ITERS):
        go, ge = scaled(g_own, g_extra)
        if iteration == 0:
            ze, part = ext_call(flag, sources, from_left, from_right, ge, row_lse_call([zo], [go]), scale)
        else:
            part = row_lse_call([zo, ze], [go, ge])
        row = narrow_lse(part.reshape(-1), c, narrow_count)
        f = epsilon * (log_src - row)
        own_cols, extra_cols = col_lse_call(zo, ze, (f * inv_eps).reshape(-1, 1))
        own_cols = own_cols.reshape(tgt_blocks, BLK)
        extra_cols = jnp.where(mine_live, extra_cols.reshape(-1), sentinel)
        from_left_msg = shifted(jnp.stack([extra_cols, own_cols[want_right % tgt_blocks]]), "wide", 1)
        from_right_msg = shifted(jnp.stack([extra_cols, own_cols[want_left % tgt_blocks]]), "wide", -1)
        part_from_left2 = shifted(extra_cols, "wide", 2)
        part_from_right2 = shifted(extra_cols, "wide", -2)
        part_from_left, cover_from_left = from_left_msg[0], from_left_msg[1]
        part_from_right, cover_from_right = from_right_msg[0], from_right_msg[1]
        ids = jnp.arange(tgt_blocks, dtype=jnp.int32)[:, None]
        add_right = jnp.where(want_right_live & (ids == want_right % tgt_blocks), part_from_right[None, :], sentinel)
        add_left = jnp.where(want_left_live & (ids == want_left % tgt_blocks), part_from_left[None, :], sentinel)
        top = jnp.maximum(own_cols, jnp.maximum(add_right, add_left))
        total = jnp.exp(own_cols - top) + jnp.exp(add_right - top) + jnp.exp(add_left - top)
        g_blocks = epsilon * (log_tgt - (top + jnp.log(total)))
        g_own = g_blocks.reshape(-1)
        cover_e = jnp.where(mine_from_left, cover_from_left, cover_from_right)
        other = jnp.where(mine_from_left, part_from_left2, part_from_right2)
        other_live = jnp.where(mine_from_left, far_left_same, far_right_same)
        other = jnp.where(other_live, other, sentinel)
        first = jnp.where(mine_from_left, extra_cols, other)
        second = jnp.where(mine_from_left, other, extra_cols)
        top_e = jnp.maximum(cover_e, jnp.maximum(first, second))
        total_e = jnp.exp(cover_e - top_e) + jnp.exp(first - top_e) + jnp.exp(second - top_e)
        g_extra = epsilon * (log_tgt - (top_e + jnp.log(total_e)))

    go, ge = scaled(g_own, g_extra)
    row = narrow_lse(row_lse_call([zo, ze], [go, ge]).reshape(-1), c, narrow_count)
    source_pot = epsilon * (log_src - row)
    numer = map_call(flag, zo, ze, go, ge, row.reshape(-1, 1), targets, from_left, from_right)

    rows = sources.shape[0]
    quarter = rows // narrow_count
    half = quarter // 2
    chunks = numer.reshape(narrow_count, 2, half, feature_count)

    def chunk(index, side):
        return lax.dynamic_index_in_dim(chunks, index % narrow_count, 0, False)[side]

    far_a = shifted(chunk(c + 2, 0), "narrow", 1)
    far_b = shifted(chunk(c + 2, 1), "narrow", -1)
    to_right = jnp.stack([chunk(c + 1, 0) + far_a, chunk(c + 1, 1)])
    to_left = jnp.stack([chunk(c - 1, 0), chunk(c - 1, 1) + far_b])
    got_left = shifted(to_right, "narrow", 1)
    got_right = shifted(to_left, "narrow", -1)
    mine_sum = jnp.stack([chunk(c, 0), chunk(c, 1)]) + got_left + got_right
    done = mine_sum.astype(jnp.bfloat16).reshape(quarter, feature_count)
    q_left = shifted(done, "narrow", 1)
    q_right = shifted(done, "narrow", -1)
    far_half_a = shifted(q_left[:half], "narrow", 1)
    far_half_b = shifted(q_right[half:], "narrow", -1)
    q_far = jnp.concatenate([far_half_a, far_half_b])
    pieces = jnp.stack([done, q_left, q_far, q_right])
    order = (c - jnp.arange(narrow_count, dtype=jnp.int32)) % narrow_count
    mapped = pieces[order].reshape(rows, feature_count)
    return (source_pot, g_own, mapped)


def solution(mesh):
    placed = (P("wide", None), P(("wide", "narrow"), None), P(), P())
    return jax.shard_map(
        shards,
        mesh=mesh,
        in_specs=placed,
        out_specs=(P("wide"), P(("wide", "narrow")), P("wide", None)),
        check_vma=False,
    )
```

```python
import functools
import math

import jax
import jax.numpy as jnp
from jax import lax
from jax.sharding import PartitionSpec as P
from jax.experimental import pallas as pl
from jax.experimental.pallas import tpu as pltpu

BLK = 1024
ITERS = 2


epsilon = 0.25
sentinel = -1e30


def shifted(x, axis, distance):
    size = lax.axis_size(axis)
    route = [(i, (i + distance) % size) for i in range(size)]
    return lax.ppermute(x, axis, route)


def _row_kernel(*refs):
    n = (len(refs) - 1) // 2
    out_ref = refs[-1]
    scores = [refs[k][...] + refs[n + k][...] for k in range(n)]
    top = scores[0].max(axis=1, keepdims=True)
    for s in scores[1:]:
        top = jnp.maximum(top, s.max(axis=1, keepdims=True))
    total = jnp.sum(jnp.exp(scores[0] - top), axis=1, keepdims=True)
    for s in scores[1:]:
        total = total + jnp.sum(jnp.exp(s - top), axis=1, keepdims=True)
    out_ref[...] = top + jnp.log(total)


def row_lse_call(zs, gs, tm=256):
    rows = zs[0].shape[0]
    in_specs = [pl.BlockSpec((tm, z.shape[1]), lambda i: (i, 0)) for z in zs]
    in_specs += [pl.BlockSpec((1, g.shape[1]), lambda i: (0, 0)) for g in gs]
    return pl.pallas_call(
        _row_kernel,
        grid=(rows // tm,),
        in_specs=in_specs,
        out_specs=pl.BlockSpec((tm, 1), lambda i: (i, 0)),
        out_shape=jax.ShapeDtypeStruct((rows, 1), jnp.float32),
    )(*zs, *gs)


def _col_kernel(zo_ref, ze_ref, f_ref, oo_ref, oe_ref):
    f = f_ref[...]
    for z_ref, o_ref in ((zo_ref, oo_ref), (ze_ref, oe_ref)):
        s = z_ref[...] + f
        top = s.max(axis=0, keepdims=True)
        o_ref[...] = top + jnp.log(jnp.sum(jnp.exp(s - top), axis=0, keepdims=True))


def col_lse_call(zo, ze, f, steps=4):
    rows = zo.shape[0]
    wo = zo.shape[1] // steps
    we = ze.shape[1] // steps
    return pl.pallas_call(
        _col_kernel,
        grid=(steps,),
        in_specs=[
            pl.BlockSpec((rows, wo), lambda j: (0, j)),
            pl.BlockSpec((rows, we), lambda j: (0, j)),
            pl.BlockSpec((rows, 1), lambda j: (0, 0)),
        ],
        out_specs=[
            pl.BlockSpec((1, wo), lambda j: (0, j)),
            pl.BlockSpec((1, we), lambda j: (0, j)),
        ],
        out_shape=[
            jax.ShapeDtypeStruct((1, zo.shape[1]), jnp.float32),
            jax.ShapeDtypeStruct((1, ze.shape[1]), jnp.float32),
        ],
    )(zo, ze, f)


def _ext_kernel(flag_ref, s_ref, l_ref, r_ref, ge_ref, own_ref, ze_ref, part_ref, *, scale):
    def product(e_ref):
        ze_ref[...] = lax.dot_general(
            s_ref[...], e_ref[...], (((1,), (1,)), ((), ())), preferred_element_type=jnp.float32
        ) * scale

    @pl.when(flag_ref[0] == 1)
    def _():
        product(l_ref)

    @pl.when(flag_ref[0] != 1)
    def _():
        product(r_ref)

    s = ze_ref[...] + ge_ref[...]
    own = own_ref[...]
    top = jnp.maximum(s.max(axis=1, keepdims=True), own)
    part_ref[...] = top + jnp.log(jnp.sum(jnp.exp(s - top), axis=1, keepdims=True) + jnp.exp(own - top))


def ext_call(flag, sources, from_left, from_right, ge, own_part, scale, tm=256):
    rows, feats = sources.shape
    width = from_left.shape[0]
    grid_spec = pltpu.PrefetchScalarGridSpec(
        num_scalar_prefetch=1,
        grid=(rows // tm,),
        in_specs=[
            pl.BlockSpec((tm, feats), lambda i, f: (i, 0)),
            pl.BlockSpec(from_left.shape, lambda i, f: (0, 0)),
            pl.BlockSpec(from_right.shape, lambda i, f: (0, 0)),
            pl.BlockSpec((1, width), lambda i, f: (0, 0)),
            pl.BlockSpec((tm, 1), lambda i, f: (i, 0)),
        ],
        out_specs=[
            pl.BlockSpec((tm, width), lambda i, f: (i, 0)),
            pl.BlockSpec((tm, 1), lambda i, f: (i, 0)),
        ],
    )
    return pl.pallas_call(
        functools.partial(_ext_kernel, scale=scale),
        grid_spec=grid_spec,
        out_shape=[
            jax.ShapeDtypeStruct((rows, width), jnp.float32),
            jax.ShapeDtypeStruct((rows, 1), jnp.float32),
        ],
    )(flag, sources, from_left, from_right, ge, own_part)


def _map_kernel(flag_ref, zo_ref, ze_ref, go_ref, ge_ref, l_ref, to_ref, tl_ref, tr_ref, out_ref):
    lse = l_ref[...]
    wo = jnp.exp(zo_ref[...] + go_ref[...] - lse).astype(jnp.bfloat16)
    we = jnp.exp(ze_ref[...] + ge_ref[...] - lse).astype(jnp.bfloat16)
    out_ref[...] = jnp.dot(wo, to_ref[...], preferred_element_type=jnp.float32)

    @pl.when(flag_ref[0] == 1)
    def _():
        out_ref[...] += jnp.dot(we, tl_ref[...], preferred_element_type=jnp.float32)

    @pl.when(flag_ref[0] != 1)
    def _():
        out_ref[...] += jnp.dot(we, tr_ref[...], preferred_element_type=jnp.float32)


def map_call(flag, zo, ze, go, ge, lse, to, tl, tr, tm=256):
    rows = zo.shape[0]
    feats = to.shape[1]
    grid_spec = pltpu.PrefetchScalarGridSpec(
        num_scalar_prefetch=1,
        grid=(rows // tm,),
        in_specs=[
            pl.BlockSpec((tm, zo.shape[1]), lambda i, f: (i, 0)),
            pl.BlockSpec((tm, ze.shape[1]), lambda i, f: (i, 0)),
            pl.BlockSpec((1, go.shape[1]), lambda i, f: (0, 0)),
            pl.BlockSpec((1, ge.shape[1]), lambda i, f: (0, 0)),
            pl.BlockSpec((tm, 1), lambda i, f: (i, 0)),
            pl.BlockSpec(to.shape, lambda i, f: (0, 0)),
            pl.BlockSpec(tl.shape, lambda i, f: (0, 0)),
            pl.BlockSpec(tr.shape, lambda i, f: (0, 0)),
        ],
        out_specs=pl.BlockSpec((tm, feats), lambda i, f: (i, 0)),
    )
    return pl.pallas_call(
        _map_kernel,
        grid_spec=grid_spec,
        out_shape=jax.ShapeDtypeStruct((rows, feats), jnp.float32),
    )(flag, zo, ze, go, ge, lse, to, tl, tr)


def narrow_lse(partial_value, column, narrow_count):
    pieces = [partial_value] + [shifted(partial_value, "narrow", k) for k in range(1, narrow_count)]
    stacked = jnp.stack(pieces)
    order = (column - jnp.arange(narrow_count, dtype=jnp.int32)) % narrow_count
    ordered = stacked[order]
    top = jnp.max(ordered, axis=0)
    return top + jnp.log(jnp.sum(jnp.exp(ordered - top[None, :]), axis=0))


def shards(sources, targets, pair_target, pair_count):
    feature_count = sources.shape[1]
    tgt_blocks = targets.shape[0] // BLK
    wide_count = lax.axis_size("wide")
    narrow_count = lax.axis_size("narrow")
    w = lax.axis_index("wide")
    c = lax.axis_index("narrow")
    group_blocks = tgt_blocks * narrow_count
    scale = (1.0 / math.sqrt(feature_count)) * (1.0 / epsilon)
    inv_eps = 1.0 / epsilon
    log_src = -math.log(wide_count * sources.shape[0])
    log_tgt = -math.log(wide_count * narrow_count * targets.shape[0])

    left = (w - 1 + wide_count) % wide_count
    right = (w + 1) % wide_count
    slot = group_blocks + c

    mine = pair_target[w, slot]
    mine_live = pair_count[w] > slot
    mine_from_left = (mine // group_blocks) == left

    want_right = pair_target[right, slot]
    want_right_live = (pair_count[right] > slot) & ((want_right // group_blocks) == w)
    want_left = pair_target[left, slot]
    want_left_live = (pair_count[left] > slot) & ((want_left // group_blocks) == w)
    left2 = (w - 2 + 2 * wide_count) % wide_count
    right2 = (w + 2) % wide_count
    far_left_same = (pair_count[left2] > slot) & (pair_target[left2, slot] == mine)
    far_right_same = (pair_count[right2] > slot) & (pair_target[right2, slot] == mine)

    blocks = targets.reshape(tgt_blocks, BLK, feature_count)
    to_right = blocks[want_right % tgt_blocks]
    to_left = blocks[want_left % tgt_blocks]
    from_left = shifted(to_right, "wide", 1)
    from_right = shifted(to_left, "wide", -1)

    zo = lax.dot_general(
        sources, targets, (((1,), (1,)), ((), ())), preferred_element_type=jnp.float32
    ) * scale
    extra_mask = jnp.where(mine_live, 0.0, sentinel).astype(jnp.float32)
    flag = mine_from_left.astype(jnp.int32).reshape(1)
    own_width = tgt_blocks * BLK

    def scaled(g_own, g_extra):
        return ((g_own * inv_eps).reshape(1, own_width), (g_extra * inv_eps + extra_mask).reshape(1, BLK))

    g_own = jnp.zeros((own_width,), jnp.float32)
    g_extra = jnp.zeros((BLK,), jnp.float32)
    for iteration in range(ITERS):
        go, ge = scaled(g_own, g_extra)
        if iteration == 0:
            ze, part = ext_call(flag, sources, from_left, from_right, ge, row_lse_call([zo], [go]), scale)
        else:
            part = row_lse_call([zo, ze], [go, ge])
        row = narrow_lse(part.reshape(-1), c, narrow_count)
        f = epsilon * (log_src - row)
        own_cols, extra_cols = col_lse_call(zo, ze, (f * inv_eps).reshape(-1, 1))
        own_cols = own_cols.reshape(tgt_blocks, BLK)
        extra_cols = jnp.where(mine_live, extra_cols.reshape(-1), sentinel)
        from_left_msg = shifted(jnp.stack([extra_cols, own_cols[want_right % tgt_blocks]]), "wide", 1)
        from_right_msg = shifted(jnp.stack([extra_cols, own_cols[want_left % tgt_blocks]]), "wide", -1)
        part_from_left2 = shifted(extra_cols, "wide", 2)
        part_from_right2 = shifted(extra_cols, "wide", -2)
        part_from_left, cover_from_left = from_left_msg[0], from_left_msg[1]
        part_from_right, cover_from_right = from_right_msg[0], from_right_msg[1]
        ids = jnp.arange(tgt_blocks, dtype=jnp.int32)[:, None]
        add_right = jnp.where(want_right_live & (ids == want_right % tgt_blocks), part_from_right[None, :], sentinel)
        add_left = jnp.where(want_left_live & (ids == want_left % tgt_blocks), part_from_left[None, :], sentinel)
        top = jnp.maximum(own_cols, jnp.maximum(add_right, add_left))
        total = jnp.exp(own_cols - top) + jnp.exp(add_right - top) + jnp.exp(add_left - top)
        g_blocks = epsilon * (log_tgt - (top + jnp.log(total)))
        g_own = g_blocks.reshape(-1)
        cover_e = jnp.where(mine_from_left, cover_from_left, cover_from_right)
        other = jnp.where(mine_from_left, part_from_left2, part_from_right2)
        other_live = jnp.where(mine_from_left, far_left_same, far_right_same)
        other = jnp.where(other_live, other, sentinel)
        first = jnp.where(mine_from_left, extra_cols, other)
        second = jnp.where(mine_from_left, other, extra_cols)
        top_e = jnp.maximum(cover_e, jnp.maximum(first, second))
        total_e = jnp.exp(cover_e - top_e) + jnp.exp(first - top_e) + jnp.exp(second - top_e)
        g_extra = epsilon * (log_tgt - (top_e + jnp.log(total_e)))

    go, ge = scaled(g_own, g_extra)
    row = narrow_lse(row_lse_call([zo, ze], [go, ge]).reshape(-1), c, narrow_count)
    source_pot = epsilon * (log_src - row)
    numer = map_call(flag, zo, ze, go, ge, row.reshape(-1, 1), targets, from_left, from_right)

    rows = sources.shape[0]
    quarter = rows // narrow_count
    half = quarter // 2
    chunks = numer.reshape(narrow_count, 2, half, feature_count)

    def chunk(index, side):
        return lax.dynamic_index_in_dim(chunks, index % narrow_count, 0, False)[side]

    far_a = shifted(chunk(c + 2, 0), "narrow", 1)
    far_b = shifted(chunk(c + 2, 1), "narrow", -1)
    to_right = jnp.stack([chunk(c + 1, 0) + far_a, chunk(c + 1, 1)])
    to_left = jnp.stack([chunk(c - 1, 0), chunk(c - 1, 1) + far_b])
    got_left = shifted(to_right, "narrow", 1)
    got_right = shifted(to_left, "narrow", -1)
    mine_sum = jnp.stack([chunk(c, 0), chunk(c, 1)]) + got_left + got_right
    done = mine_sum.astype(jnp.bfloat16).reshape(quarter, feature_count)
    q_left = shifted(done, "narrow", 1)
    q_right = shifted(done, "narrow", -1)
    far_half_a = shifted(q_left[:half], "narrow", 1)
    far_half_b = shifted(q_right[half:], "narrow", -1)
    q_far = jnp.concatenate([far_half_a, far_half_b])
    pieces = jnp.stack([done, q_left, q_far, q_right])
    order = (c - jnp.arange(narrow_count, dtype=jnp.int32)) % narrow_count
    mapped = pieces[order].reshape(rows, feature_count)
    return (source_pot, g_own, mapped)


def solution(mesh):
    placed = (P("wide", None), P(("wide", "narrow"), None), P(), P())
    return jax.shard_map(
        shards,
        mesh=mesh,
        in_specs=placed,
        out_specs=(P("wide"), P(("wide", "narrow")), P("wide", None)),
        check_vma=False,
    )
```

```python
import functools
import math

import jax
import jax.numpy as jnp
from jax import lax
from jax.sharding import PartitionSpec as P
from jax.experimental import pallas as pl
from jax.experimental.pallas import tpu as pltpu

BLK = 1024
ITERS = 2


epsilon = 0.25
sentinel = -1e30


def shifted(x, axis, distance):
    size = lax.axis_size(axis)
    route = [(i, (i + distance) % size) for i in range(size)]
    return lax.ppermute(x, axis, route)


def _row_kernel(*refs):
    n = (len(refs) - 1) // 2
    out_ref = refs[-1]
    scores = [refs[k][...] + refs[n + k][...] for k in range(n)]
    top = scores[0].max(axis=1, keepdims=True)
    for s in scores[1:]:
        top = jnp.maximum(top, s.max(axis=1, keepdims=True))
    total = jnp.sum(jnp.exp(scores[0] - top), axis=1, keepdims=True)
    for s in scores[1:]:
        total = total + jnp.sum(jnp.exp(s - top), axis=1, keepdims=True)
    out_ref[...] = top + jnp.log(total)


def row_lse_call(zs, gs, tm=256):
    rows = zs[0].shape[0]
    in_specs = [pl.BlockSpec((tm, z.shape[1]), lambda i: (i, 0)) for z in zs]
    in_specs += [pl.BlockSpec((1, g.shape[1]), lambda i: (0, 0)) for g in gs]
    return pl.pallas_call(
        _row_kernel,
        grid=(rows // tm,),
        in_specs=in_specs,
        out_specs=pl.BlockSpec((tm, 1), lambda i: (i, 0)),
        out_shape=jax.ShapeDtypeStruct((rows, 1), jnp.float32),
    )(*zs, *gs)


def _row_merge_kernel(z_ref, g_ref, prior_ref, out_ref):
    s = z_ref[...] + g_ref[...]
    prior = prior_ref[...]
    top = jnp.maximum(s.max(axis=1, keepdims=True), prior)
    out_ref[...] = top + jnp.log(jnp.sum(jnp.exp(s - top), axis=1, keepdims=True) + jnp.exp(prior - top))


def row_merge_call(z, g, prior, tm=256):
    rows, width = z.shape
    return pl.pallas_call(
        _row_merge_kernel,
        grid=(rows // tm,),
        in_specs=[
            pl.BlockSpec((tm, width), lambda i: (i, 0)),
            pl.BlockSpec((1, width), lambda i: (0, 0)),
            pl.BlockSpec((tm, 1), lambda i: (i, 0)),
        ],
        out_specs=pl.BlockSpec((tm, 1), lambda i: (i, 0)),
        out_shape=jax.ShapeDtypeStruct((rows, 1), jnp.float32),
    )(z, g, prior)


def _col_one_kernel(z_ref, f_ref, o_ref):
    s = z_ref[...] + f_ref[...]
    top = s.max(axis=0, keepdims=True)
    o_ref[...] = top + jnp.log(jnp.sum(jnp.exp(s - top), axis=0, keepdims=True))


def col_one_call(z, f, tn=256):
    rows, width = z.shape
    return pl.pallas_call(
        _col_one_kernel,
        grid=(width // tn,),
        in_specs=[pl.BlockSpec((rows, tn), lambda j: (0, j)), pl.BlockSpec((rows, 1), lambda j: (0, 0))],
        out_specs=pl.BlockSpec((1, tn), lambda j: (0, j)),
        out_shape=jax.ShapeDtypeStruct((1, width), jnp.float32),
    )(z, f)


def _col_kernel(zo_ref, ze_ref, f_ref, oo_ref, oe_ref):
    f = f_ref[...]
    for z_ref, o_ref in ((zo_ref, oo_ref), (ze_ref, oe_ref)):
        s = z_ref[...] + f
        top = s.max(axis=0, keepdims=True)
        o_ref[...] = top + jnp.log(jnp.sum(jnp.exp(s - top), axis=0, keepdims=True))


def col_lse_call(zo, ze, f, steps=4):
    rows = zo.shape[0]
    wo = zo.shape[1] // steps
    we = ze.shape[1] // steps
    return pl.pallas_call(
        _col_kernel,
        grid=(steps,),
        in_specs=[
            pl.BlockSpec((rows, wo), lambda j: (0, j)),
            pl.BlockSpec((rows, we), lambda j: (0, j)),
            pl.BlockSpec((rows, 1), lambda j: (0, 0)),
        ],
        out_specs=[
            pl.BlockSpec((1, wo), lambda j: (0, j)),
            pl.BlockSpec((1, we), lambda j: (0, j)),
        ],
        out_shape=[
            jax.ShapeDtypeStruct((1, zo.shape[1]), jnp.float32),
            jax.ShapeDtypeStruct((1, ze.shape[1]), jnp.float32),
        ],
    )(zo, ze, f)


def _ext_kernel(flag_ref, s_ref, l_ref, r_ref, ge_ref, own_ref, ze_ref, part_ref, *, scale):
    def product(e_ref):
        ze_ref[...] = lax.dot_general(
            s_ref[...], e_ref[...], (((1,), (1,)), ((), ())), preferred_element_type=jnp.float32
        ) * scale

    @pl.when(flag_ref[0] == 1)
    def _():
        product(l_ref)

    @pl.when(flag_ref[0] != 1)
    def _():
        product(r_ref)

    s = ze_ref[...] + ge_ref[...]
    own = own_ref[...]
    top = jnp.maximum(s.max(axis=1, keepdims=True), own)
    part_ref[...] = top + jnp.log(jnp.sum(jnp.exp(s - top), axis=1, keepdims=True) + jnp.exp(own - top))


def ext_call(flag, sources, from_left, from_right, ge, own_part, scale, tm=256):
    rows, feats = sources.shape
    width = from_left.shape[0]
    grid_spec = pltpu.PrefetchScalarGridSpec(
        num_scalar_prefetch=1,
        grid=(rows // tm,),
        in_specs=[
            pl.BlockSpec((tm, feats), lambda i, f: (i, 0)),
            pl.BlockSpec(from_left.shape, lambda i, f: (0, 0)),
            pl.BlockSpec(from_right.shape, lambda i, f: (0, 0)),
            pl.BlockSpec((1, width), lambda i, f: (0, 0)),
            pl.BlockSpec((tm, 1), lambda i, f: (i, 0)),
        ],
        out_specs=[
            pl.BlockSpec((tm, width), lambda i, f: (i, 0)),
            pl.BlockSpec((tm, 1), lambda i, f: (i, 0)),
        ],
    )
    return pl.pallas_call(
        functools.partial(_ext_kernel, scale=scale),
        grid_spec=grid_spec,
        out_shape=[
            jax.ShapeDtypeStruct((rows, width), jnp.float32),
            jax.ShapeDtypeStruct((rows, 1), jnp.float32),
        ],
    )(flag, sources, from_left, from_right, ge, own_part)


def _map_kernel(flag_ref, zo_ref, ze_ref, go_ref, ge_ref, l_ref, to_ref, tl_ref, tr_ref, out_ref):
    lse = l_ref[...]
    wo = jnp.exp(zo_ref[...] + go_ref[...] - lse).astype(jnp.bfloat16)
    we = jnp.exp(ze_ref[...] + ge_ref[...] - lse).astype(jnp.bfloat16)
    out_ref[...] = jnp.dot(wo, to_ref[...], preferred_element_type=jnp.float32)

    @pl.when(flag_ref[0] == 1)
    def _():
        out_ref[...] += jnp.dot(we, tl_ref[...], preferred_element_type=jnp.float32)

    @pl.when(flag_ref[0] != 1)
    def _():
        out_ref[...] += jnp.dot(we, tr_ref[...], preferred_element_type=jnp.float32)


def map_call(flag, zo, ze, go, ge, lse, to, tl, tr, tm=256):
    rows = zo.shape[0]
    feats = to.shape[1]
    grid_spec = pltpu.PrefetchScalarGridSpec(
        num_scalar_prefetch=1,
        grid=(rows // tm,),
        in_specs=[
            pl.BlockSpec((tm, zo.shape[1]), lambda i, f: (i, 0)),
            pl.BlockSpec((tm, ze.shape[1]), lambda i, f: (i, 0)),
            pl.BlockSpec((1, go.shape[1]), lambda i, f: (0, 0)),
            pl.BlockSpec((1, ge.shape[1]), lambda i, f: (0, 0)),
            pl.BlockSpec((tm, 1), lambda i, f: (i, 0)),
            pl.BlockSpec(to.shape, lambda i, f: (0, 0)),
            pl.BlockSpec(tl.shape, lambda i, f: (0, 0)),
            pl.BlockSpec(tr.shape, lambda i, f: (0, 0)),
        ],
        out_specs=pl.BlockSpec((tm, feats), lambda i, f: (i, 0)),
    )
    return pl.pallas_call(
        _map_kernel,
        grid_spec=grid_spec,
        out_shape=jax.ShapeDtypeStruct((rows, feats), jnp.float32),
    )(flag, zo, ze, go, ge, lse, to, tl, tr)


def narrow_lse(partial_value, column, narrow_count):
    pieces = [partial_value] + [shifted(partial_value, "narrow", k) for k in range(1, narrow_count)]
    stacked = jnp.stack(pieces)
    order = (column - jnp.arange(narrow_count, dtype=jnp.int32)) % narrow_count
    ordered = stacked[order]
    top = jnp.max(ordered, axis=0)
    return top + jnp.log(jnp.sum(jnp.exp(ordered - top[None, :]), axis=0))


def shards(sources, targets, pair_target, pair_count):
    feature_count = sources.shape[1]
    tgt_blocks = targets.shape[0] // BLK
    wide_count = lax.axis_size("wide")
    narrow_count = lax.axis_size("narrow")
    w = lax.axis_index("wide")
    c = lax.axis_index("narrow")
    group_blocks = tgt_blocks * narrow_count
    scale = (1.0 / math.sqrt(feature_count)) * (1.0 / epsilon)
    inv_eps = 1.0 / epsilon
    log_src = -math.log(wide_count * sources.shape[0])
    log_tgt = -math.log(wide_count * narrow_count * targets.shape[0])

    left = (w - 1 + wide_count) % wide_count
    right = (w + 1) % wide_count
    slot = group_blocks + c

    mine = pair_target[w, slot]
    mine_live = pair_count[w] > slot
    mine_from_left = (mine // group_blocks) == left

    want_right = pair_target[right, slot]
    want_right_live = (pair_count[right] > slot) & ((want_right // group_blocks) == w)
    want_left = pair_target[left, slot]
    want_left_live = (pair_count[left] > slot) & ((want_left // group_blocks) == w)
    left2 = (w - 2 + 2 * wide_count) % wide_count
    right2 = (w + 2) % wide_count
    far_left_same = (pair_count[left2] > slot) & (pair_target[left2, slot] == mine)
    far_right_same = (pair_count[right2] > slot) & (pair_target[right2, slot] == mine)

    blocks = targets.reshape(tgt_blocks, BLK, feature_count)
    to_right = blocks[want_right % tgt_blocks]
    to_left = blocks[want_left % tgt_blocks]
    from_left = shifted(to_right, "wide", 1)
    from_right = shifted(to_left, "wide", -1)

    zo = lax.dot_general(
        sources, targets, (((1,), (1,)), ((), ())), preferred_element_type=jnp.float32
    ) * scale
    extra_mask = jnp.where(mine_live, 0.0, sentinel).astype(jnp.float32)
    flag = mine_from_left.astype(jnp.int32).reshape(1)
    own_width = tgt_blocks * BLK

    def scaled(g_own, g_extra):
        return ((g_own * inv_eps).reshape(1, own_width), (g_extra * inv_eps + extra_mask).reshape(1, BLK))

    g_own = jnp.zeros((own_width,), jnp.float32)
    g_extra = jnp.zeros((BLK,), jnp.float32)
    for iteration in range(ITERS):
        go, ge = scaled(g_own, g_extra)
        if iteration == 0:
            ze, part = ext_call(flag, sources, from_left, from_right, ge, row_lse_call([zo], [go]), scale)
        else:
            part = row_merge_call(ze, ge, row_lse_call([zo], [go]))
        row = narrow_lse(part.reshape(-1), c, narrow_count)
        f = epsilon * (log_src - row)
        f_col = (f * inv_eps).reshape(-1, 1)
        extra_cols = jnp.where(mine_live, col_one_call(ze, f_col).reshape(-1), sentinel)
        part_from_left2 = shifted(extra_cols, "wide", 2)
        part_from_right2 = shifted(extra_cols, "wide", -2)
        own_cols = col_one_call(zo, f_col).reshape(tgt_blocks, BLK)
        from_left_msg = shifted(jnp.stack([extra_cols, own_cols[want_right % tgt_blocks]]), "wide", 1)
        from_right_msg = shifted(jnp.stack([extra_cols, own_cols[want_left % tgt_blocks]]), "wide", -1)
        part_from_left, cover_from_left = from_left_msg[0], from_left_msg[1]
        part_from_right, cover_from_right = from_right_msg[0], from_right_msg[1]
        ids = jnp.arange(tgt_blocks, dtype=jnp.int32)[:, None]
        add_right = jnp.where(want_right_live & (ids == want_right % tgt_blocks), part_from_right[None, :], sentinel)
        add_left = jnp.where(want_left_live & (ids == want_left % tgt_blocks), part_from_left[None, :], sentinel)
        top = jnp.maximum(own_cols, jnp.maximum(add_right, add_left))
        total = jnp.exp(own_cols - top) + jnp.exp(add_right - top) + jnp.exp(add_left - top)
        g_blocks = epsilon * (log_tgt - (top + jnp.log(total)))
        g_own = g_blocks.reshape(-1)
        cover_e = jnp.where(mine_from_left, cover_from_left, cover_from_right)
        other = jnp.where(mine_from_left, part_from_left2, part_from_right2)
        other_live = jnp.where(mine_from_left, far_left_same, far_right_same)
        other = jnp.where(other_live, other, sentinel)
        first = jnp.where(mine_from_left, extra_cols, other)
        second = jnp.where(mine_from_left, other, extra_cols)
        top_e = jnp.maximum(cover_e, jnp.maximum(first, second))
        total_e = jnp.exp(cover_e - top_e) + jnp.exp(first - top_e) + jnp.exp(second - top_e)
        g_extra = epsilon * (log_tgt - (top_e + jnp.log(total_e)))

    go, ge = scaled(g_own, g_extra)
    row = narrow_lse(row_merge_call(ze, ge, row_lse_call([zo], [go])).reshape(-1), c, narrow_count)
    source_pot = epsilon * (log_src - row)
    numer = map_call(flag, zo, ze, go, ge, row.reshape(-1, 1), targets, from_left, from_right)

    rows = sources.shape[0]
    quarter = rows // narrow_count
    half = quarter // 2
    chunks = numer.reshape(narrow_count, 2, half, feature_count)

    def chunk(index, side):
        return lax.dynamic_index_in_dim(chunks, index % narrow_count, 0, False)[side]

    far_a = shifted(chunk(c + 2, 0), "narrow", 1)
    far_b = shifted(chunk(c + 2, 1), "narrow", -1)
    to_right = jnp.stack([chunk(c + 1, 0) + far_a, chunk(c + 1, 1)])
    to_left = jnp.stack([chunk(c - 1, 0), chunk(c - 1, 1) + far_b])
    got_left = shifted(to_right, "narrow", 1)
    got_right = shifted(to_left, "narrow", -1)
    mine_sum = jnp.stack([chunk(c, 0), chunk(c, 1)]) + got_left + got_right
    done = mine_sum.astype(jnp.bfloat16).reshape(quarter, feature_count)
    q_left = shifted(done, "narrow", 1)
    q_right = shifted(done, "narrow", -1)
    far_half_a = shifted(q_left[:half], "narrow", 1)
    far_half_b = shifted(q_right[half:], "narrow", -1)
    q_far = jnp.concatenate([far_half_a, far_half_b])
    pieces = jnp.stack([done, q_left, q_far, q_right])
    order = (c - jnp.arange(narrow_count, dtype=jnp.int32)) % narrow_count
    mapped = pieces[order].reshape(rows, feature_count)
    return (source_pot, g_own, mapped)


def solution(mesh):
    placed = (P("wide", None), P(("wide", "narrow"), None), P(), P())
    return jax.shard_map(
        shards,
        mesh=mesh,
        in_specs=placed,
        out_specs=(P("wide"), P(("wide", "narrow")), P("wide", None)),
        check_vma=False,
    )
```

```python
import functools
import math

import jax
import jax.numpy as jnp
from jax import lax
from jax.sharding import PartitionSpec as P
from jax.experimental import pallas as pl
from jax.experimental.pallas import tpu as pltpu

BLK = 1024
ITERS = 2


epsilon = 0.25
sentinel = -1e30


def shifted(x, axis, distance):
    size = lax.axis_size(axis)
    route = [(i, (i + distance) % size) for i in range(size)]
    return lax.ppermute(x, axis, route)


def _row_kernel(*refs):
    n = (len(refs) - 1) // 2
    out_ref = refs[-1]
    scores = [refs[k][...] + refs[n + k][...] for k in range(n)]
    top = scores[0].max(axis=1, keepdims=True)
    for s in scores[1:]:
        top = jnp.maximum(top, s.max(axis=1, keepdims=True))
    total = jnp.sum(jnp.exp(scores[0] - top), axis=1, keepdims=True)
    for s in scores[1:]:
        total = total + jnp.sum(jnp.exp(s - top), axis=1, keepdims=True)
    out_ref[...] = top + jnp.log(total)


def row_lse_call(zs, gs, tm=128):
    rows = zs[0].shape[0]
    in_specs = [pl.BlockSpec((tm, z.shape[1]), lambda i: (i, 0)) for z in zs]
    in_specs += [pl.BlockSpec((1, g.shape[1]), lambda i: (0, 0)) for g in gs]
    return pl.pallas_call(
        _row_kernel,
        grid=(rows // tm,),
        in_specs=in_specs,
        out_specs=pl.BlockSpec((tm, 1), lambda i: (i, 0)),
        out_shape=jax.ShapeDtypeStruct((rows, 1), jnp.float32),
    )(*zs, *gs)


def _col_kernel(zo_ref, ze_ref, f_ref, oo_ref, oe_ref):
    f = f_ref[...]
    for z_ref, o_ref in ((zo_ref, oo_ref), (ze_ref, oe_ref)):
        s = z_ref[...] + f
        top = s.max(axis=0, keepdims=True)
        o_ref[...] = top + jnp.log(jnp.sum(jnp.exp(s - top), axis=0, keepdims=True))


def col_lse_call(zo, ze, f, steps=8):
    rows = zo.shape[0]
    wo = zo.shape[1] // steps
    we = ze.shape[1] // steps
    return pl.pallas_call(
        _col_kernel,
        grid=(steps,),
        in_specs=[
            pl.BlockSpec((rows, wo), lambda j: (0, j)),
            pl.BlockSpec((rows, we), lambda j: (0, j)),
            pl.BlockSpec((rows, 1), lambda j: (0, 0)),
        ],
        out_specs=[
            pl.BlockSpec((1, wo), lambda j: (0, j)),
            pl.BlockSpec((1, we), lambda j: (0, j)),
        ],
        out_shape=[
            jax.ShapeDtypeStruct((1, zo.shape[1]), jnp.float32),
            jax.ShapeDtypeStruct((1, ze.shape[1]), jnp.float32),
        ],
    )(zo, ze, f)


def _ext_kernel(flag_ref, s_ref, l_ref, r_ref, ge_ref, own_ref, ze_ref, part_ref, *, scale):
    def product(e_ref):
        ze_ref[...] = lax.dot_general(
            s_ref[...], e_ref[...], (((1,), (1,)), ((), ())), preferred_element_type=jnp.float32
        ) * scale

    @pl.when(flag_ref[0] == 1)
    def _():
        product(l_ref)

    @pl.when(flag_ref[0] != 1)
    def _():
        product(r_ref)

    s = ze_ref[...] + ge_ref[...]
    own = own_ref[...]
    top = jnp.maximum(s.max(axis=1, keepdims=True), own)
    part_ref[...] = top + jnp.log(jnp.sum(jnp.exp(s - top), axis=1, keepdims=True) + jnp.exp(own - top))


def ext_call(flag, sources, from_left, from_right, ge, own_part, scale, tm=128):
    rows, feats = sources.shape
    width = from_left.shape[0]
    grid_spec = pltpu.PrefetchScalarGridSpec(
        num_scalar_prefetch=1,
        grid=(rows // tm,),
        in_specs=[
            pl.BlockSpec((tm, feats), lambda i, f: (i, 0)),
            pl.BlockSpec(from_left.shape, lambda i, f: (0, 0)),
            pl.BlockSpec(from_right.shape, lambda i, f: (0, 0)),
            pl.BlockSpec((1, width), lambda i, f: (0, 0)),
            pl.BlockSpec((tm, 1), lambda i, f: (i, 0)),
        ],
        out_specs=[
            pl.BlockSpec((tm, width), lambda i, f: (i, 0)),
            pl.BlockSpec((tm, 1), lambda i, f: (i, 0)),
        ],
    )
    return pl.pallas_call(
        functools.partial(_ext_kernel, scale=scale),
        grid_spec=grid_spec,
        out_shape=[
            jax.ShapeDtypeStruct((rows, width), jnp.float32),
            jax.ShapeDtypeStruct((rows, 1), jnp.float32),
        ],
    )(flag, sources, from_left, from_right, ge, own_part)


def _map_kernel(flag_ref, zo_ref, ze_ref, go_ref, ge_ref, l_ref, to_ref, tl_ref, tr_ref, out_ref):
    lse = l_ref[...]
    wo = jnp.exp(zo_ref[...] + go_ref[...] - lse).astype(jnp.bfloat16)
    we = jnp.exp(ze_ref[...] + ge_ref[...] - lse).astype(jnp.bfloat16)
    out_ref[...] = jnp.dot(wo, to_ref[...], preferred_element_type=jnp.float32)

    @pl.when(flag_ref[0] == 1)
    def _():
        out_ref[...] += jnp.dot(we, tl_ref[...], preferred_element_type=jnp.float32)

    @pl.when(flag_ref[0] != 1)
    def _():
        out_ref[...] += jnp.dot(we, tr_ref[...], preferred_element_type=jnp.float32)


def map_call(flag, zo, ze, go, ge, lse, to, tl, tr, tm=128):
    rows = zo.shape[0]
    feats = to.shape[1]
    grid_spec = pltpu.PrefetchScalarGridSpec(
        num_scalar_prefetch=1,
        grid=(rows // tm,),
        in_specs=[
            pl.BlockSpec((tm, zo.shape[1]), lambda i, f: (i, 0)),
            pl.BlockSpec((tm, ze.shape[1]), lambda i, f: (i, 0)),
            pl.BlockSpec((1, go.shape[1]), lambda i, f: (0, 0)),
            pl.BlockSpec((1, ge.shape[1]), lambda i, f: (0, 0)),
            pl.BlockSpec((tm, 1), lambda i, f: (i, 0)),
            pl.BlockSpec(to.shape, lambda i, f: (0, 0)),
            pl.BlockSpec(tl.shape, lambda i, f: (0, 0)),
            pl.BlockSpec(tr.shape, lambda i, f: (0, 0)),
        ],
        out_specs=pl.BlockSpec((tm, feats), lambda i, f: (i, 0)),
    )
    return pl.pallas_call(
        _map_kernel,
        grid_spec=grid_spec,
        out_shape=jax.ShapeDtypeStruct((rows, feats), jnp.float32),
    )(flag, zo, ze, go, ge, lse, to, tl, tr)


def narrow_lse(partial_value, column, narrow_count):
    pieces = [partial_value] + [shifted(partial_value, "narrow", k) for k in range(1, narrow_count)]
    stacked = jnp.stack(pieces)
    order = (column - jnp.arange(narrow_count, dtype=jnp.int32)) % narrow_count
    ordered = stacked[order]
    top = jnp.max(ordered, axis=0)
    return top + jnp.log(jnp.sum(jnp.exp(ordered - top[None, :]), axis=0))


def shards(sources, targets, pair_target, pair_count):
    feature_count = sources.shape[1]
    tgt_blocks = targets.shape[0] // BLK
    wide_count = lax.axis_size("wide")
    narrow_count = lax.axis_size("narrow")
    w = lax.axis_index("wide")
    c = lax.axis_index("narrow")
    group_blocks = tgt_blocks * narrow_count
    scale = (1.0 / math.sqrt(feature_count)) * (1.0 / epsilon)
    inv_eps = 1.0 / epsilon
    log_src = -math.log(wide_count * sources.shape[0])
    log_tgt = -math.log(wide_count * narrow_count * targets.shape[0])

    left = (w - 1 + wide_count) % wide_count
    right = (w + 1) % wide_count
    slot = group_blocks + c

    mine = pair_target[w, slot]
    mine_live = pair_count[w] > slot
    mine_from_left = (mine // group_blocks) == left

    want_right = pair_target[right, slot]
    want_right_live = (pair_count[right] > slot) & ((want_right // group_blocks) == w)
    want_left = pair_target[left, slot]
    want_left_live = (pair_count[left] > slot) & ((want_left // group_blocks) == w)
    left2 = (w - 2 + 2 * wide_count) % wide_count
    right2 = (w + 2) % wide_count
    far_left_same = (pair_count[left2] > slot) & (pair_target[left2, slot] == mine)
    far_right_same = (pair_count[right2] > slot) & (pair_target[right2, slot] == mine)

    blocks = targets.reshape(tgt_blocks, BLK, feature_count)
    to_right = blocks[want_right % tgt_blocks]
    to_left = blocks[want_left % tgt_blocks]
    from_left = shifted(to_right, "wide", 1)
    from_right = shifted(to_left, "wide", -1)

    zo = lax.dot_general(
        sources, targets, (((1,), (1,)), ((), ())), preferred_element_type=jnp.float32
    ) * scale
    extra_mask = jnp.where(mine_live, 0.0, sentinel).astype(jnp.float32)
    flag = mine_from_left.astype(jnp.int32).reshape(1)
    own_width = tgt_blocks * BLK

    def scaled(g_own, g_extra):
        return ((g_own * inv_eps).reshape(1, own_width), (g_extra * inv_eps + extra_mask).reshape(1, BLK))

    g_own = jnp.zeros((own_width,), jnp.float32)
    g_extra = jnp.zeros((BLK,), jnp.float32)
    for iteration in range(ITERS):
        go, ge = scaled(g_own, g_extra)
        if iteration == 0:
            ze, part = ext_call(flag, sources, from_left, from_right, ge, row_lse_call([zo], [go]), scale)
        else:
            part = row_lse_call([zo, ze], [go, ge])
        row = narrow_lse(part.reshape(-1), c, narrow_count)
        f = epsilon * (log_src - row)
        own_cols, extra_cols = col_lse_call(zo, ze, (f * inv_eps).reshape(-1, 1))
        own_cols = own_cols.reshape(tgt_blocks, BLK)
        extra_cols = jnp.where(mine_live, extra_cols.reshape(-1), sentinel)
        from_left_msg = shifted(jnp.stack([extra_cols, own_cols[want_right % tgt_blocks]]), "wide", 1)
        from_right_msg = shifted(jnp.stack([extra_cols, own_cols[want_left % tgt_blocks]]), "wide", -1)
        part_from_left2 = shifted(extra_cols, "wide", 2)
        part_from_right2 = shifted(extra_cols, "wide", -2)
        part_from_left, cover_from_left = from_left_msg[0], from_left_msg[1]
        part_from_right, cover_from_right = from_right_msg[0], from_right_msg[1]
        ids = jnp.arange(tgt_blocks, dtype=jnp.int32)[:, None]
        add_right = jnp.where(want_right_live & (ids == want_right % tgt_blocks), part_from_right[None, :], sentinel)
        add_left = jnp.where(want_left_live & (ids == want_left % tgt_blocks), part_from_left[None, :], sentinel)
        top = jnp.maximum(own_cols, jnp.maximum(add_right, add_left))
        total = jnp.exp(own_cols - top) + jnp.exp(add_right - top) + jnp.exp(add_left - top)
        g_blocks = epsilon * (log_tgt - (top + jnp.log(total)))
        g_own = g_blocks.reshape(-1)
        cover_e = jnp.where(mine_from_left, cover_from_left, cover_from_right)
        other = jnp.where(mine_from_left, part_from_left2, part_from_right2)
        other_live = jnp.where(mine_from_left, far_left_same, far_right_same)
        other = jnp.where(other_live, other, sentinel)
        first = jnp.where(mine_from_left, extra_cols, other)
        second = jnp.where(mine_from_left, other, extra_cols)
        top_e = jnp.maximum(cover_e, jnp.maximum(first, second))
        total_e = jnp.exp(cover_e - top_e) + jnp.exp(first - top_e) + jnp.exp(second - top_e)
        g_extra = epsilon * (log_tgt - (top_e + jnp.log(total_e)))

    go, ge = scaled(g_own, g_extra)
    row = narrow_lse(row_lse_call([zo, ze], [go, ge]).reshape(-1), c, narrow_count)
    source_pot = epsilon * (log_src - row)
    numer = map_call(flag, zo, ze, go, ge, row.reshape(-1, 1), targets, from_left, from_right)

    rows = sources.shape[0]
    quarter = rows // narrow_count
    half = quarter // 2
    chunks = numer.reshape(narrow_count, 2, half, feature_count)

    def chunk(index, side):
        return lax.dynamic_index_in_dim(chunks, index % narrow_count, 0, False)[side]

    far_a = shifted(chunk(c + 2, 0), "narrow", 1)
    far_b = shifted(chunk(c + 2, 1), "narrow", -1)
    to_right = jnp.stack([chunk(c + 1, 0) + far_a, chunk(c + 1, 1)])
    to_left = jnp.stack([chunk(c - 1, 0), chunk(c - 1, 1) + far_b])
    got_left = shifted(to_right, "narrow", 1)
    got_right = shifted(to_left, "narrow", -1)
    mine_sum = jnp.stack([chunk(c, 0), chunk(c, 1)]) + got_left + got_right
    done = mine_sum.astype(jnp.bfloat16).reshape(quarter, feature_count)
    q_left = shifted(done, "narrow", 1)
    q_right = shifted(done, "narrow", -1)
    far_half_a = shifted(q_left[:half], "narrow", 1)
    far_half_b = shifted(q_right[half:], "narrow", -1)
    q_far = jnp.concatenate([far_half_a, far_half_b])
    pieces = jnp.stack([done, q_left, q_far, q_right])
    order = (c - jnp.arange(narrow_count, dtype=jnp.int32)) % narrow_count
    mapped = pieces[order].reshape(rows, feature_count)
    return (source_pot, g_own, mapped)


def solution(mesh):
    placed = (P("wide", None), P(("wide", "narrow"), None), P(), P())
    return jax.shard_map(
        shards,
        mesh=mesh,
        in_specs=placed,
        out_specs=(P("wide"), P(("wide", "narrow")), P("wide", None)),
        check_vma=False,
    )
```

```python
import functools
import math

import jax
import jax.numpy as jnp
from jax import lax
from jax.sharding import PartitionSpec as P
from jax.experimental import pallas as pl
from jax.experimental.pallas import tpu as pltpu

BLK = 1024
ITERS = 2


epsilon = 0.25
sentinel = -1e30


def shifted(x, axis, distance):
    size = lax.axis_size(axis)
    route = [(i, (i + distance) % size) for i in range(size)]
    return lax.ppermute(x, axis, route)


def _row_kernel(*refs):
    n = (len(refs) - 1) // 2
    out_ref = refs[-1]
    scores = [refs[k][...] + refs[n + k][...] for k in range(n)]
    top = scores[0].max(axis=1, keepdims=True)
    for s in scores[1:]:
        top = jnp.maximum(top, s.max(axis=1, keepdims=True))
    total = jnp.sum(jnp.exp(scores[0] - top), axis=1, keepdims=True)
    for s in scores[1:]:
        total = total + jnp.sum(jnp.exp(s - top), axis=1, keepdims=True)
    out_ref[...] = top + jnp.log(total)


def row_lse_call(zs, gs, tm=512):
    rows = zs[0].shape[0]
    in_specs = [pl.BlockSpec((tm, z.shape[1]), lambda i: (i, 0)) for z in zs]
    in_specs += [pl.BlockSpec((1, g.shape[1]), lambda i: (0, 0)) for g in gs]
    return pl.pallas_call(
        _row_kernel,
        grid=(rows // tm,),
        in_specs=in_specs,
        out_specs=pl.BlockSpec((tm, 1), lambda i: (i, 0)),
        out_shape=jax.ShapeDtypeStruct((rows, 1), jnp.float32),
    )(*zs, *gs)


def _col_kernel(zo_ref, ze_ref, f_ref, oo_ref, oe_ref):
    f = f_ref[...]
    for z_ref, o_ref in ((zo_ref, oo_ref), (ze_ref, oe_ref)):
        s = z_ref[...] + f
        top = s.max(axis=0, keepdims=True)
        o_ref[...] = top + jnp.log(jnp.sum(jnp.exp(s - top), axis=0, keepdims=True))


def col_lse_call(zo, ze, f, steps=2):
    rows = zo.shape[0]
    wo = zo.shape[1] // steps
    we = ze.shape[1] // steps
    return pl.pallas_call(
        _col_kernel,
        grid=(steps,),
        in_specs=[
            pl.BlockSpec((rows, wo), lambda j: (0, j)),
            pl.BlockSpec((rows, we), lambda j: (0, j)),
            pl.BlockSpec((rows, 1), lambda j: (0, 0)),
        ],
        out_specs=[
            pl.BlockSpec((1, wo), lambda j: (0, j)),
            pl.BlockSpec((1, we), lambda j: (0, j)),
        ],
        out_shape=[
            jax.ShapeDtypeStruct((1, zo.shape[1]), jnp.float32),
            jax.ShapeDtypeStruct((1, ze.shape[1]), jnp.float32),
        ],
    )(zo, ze, f)


def _ext_kernel(flag_ref, s_ref, l_ref, r_ref, ge_ref, own_ref, ze_ref, part_ref, *, scale):
    def product(e_ref):
        ze_ref[...] = lax.dot_general(
            s_ref[...], e_ref[...], (((1,), (1,)), ((), ())), preferred_element_type=jnp.float32
        ) * scale

    @pl.when(flag_ref[0] == 1)
    def _():
        product(l_ref)

    @pl.when(flag_ref[0] != 1)
    def _():
        product(r_ref)

    s = ze_ref[...] + ge_ref[...]
    own = own_ref[...]
    top = jnp.maximum(s.max(axis=1, keepdims=True), own)
    part_ref[...] = top + jnp.log(jnp.sum(jnp.exp(s - top), axis=1, keepdims=True) + jnp.exp(own - top))


def ext_call(flag, sources, from_left, from_right, ge, own_part, scale, tm=512):
    rows, feats = sources.shape
    width = from_left.shape[0]
    grid_spec = pltpu.PrefetchScalarGridSpec(
        num_scalar_prefetch=1,
        grid=(rows // tm,),
        in_specs=[
            pl.BlockSpec((tm, feats), lambda i, f: (i, 0)),
            pl.BlockSpec(from_left.shape, lambda i, f: (0, 0)),
            pl.BlockSpec(from_right.shape, lambda i, f: (0, 0)),
            pl.BlockSpec((1, width), lambda i, f: (0, 0)),
            pl.BlockSpec((tm, 1), lambda i, f: (i, 0)),
        ],
        out_specs=[
            pl.BlockSpec((tm, width), lambda i, f: (i, 0)),
            pl.BlockSpec((tm, 1), lambda i, f: (i, 0)),
        ],
    )
    return pl.pallas_call(
        functools.partial(_ext_kernel, scale=scale),
        grid_spec=grid_spec,
        out_shape=[
            jax.ShapeDtypeStruct((rows, width), jnp.float32),
            jax.ShapeDtypeStruct((rows, 1), jnp.float32),
        ],
    )(flag, sources, from_left, from_right, ge, own_part)


def _map_kernel(flag_ref, zo_ref, ze_ref, go_ref, ge_ref, l_ref, to_ref, tl_ref, tr_ref, out_ref):
    lse = l_ref[...]
    wo = jnp.exp(zo_ref[...] + go_ref[...] - lse).astype(jnp.bfloat16)
    we = jnp.exp(ze_ref[...] + ge_ref[...] - lse).astype(jnp.bfloat16)
    out_ref[...] = jnp.dot(wo, to_ref[...], preferred_element_type=jnp.float32)

    @pl.when(flag_ref[0] == 1)
    def _():
        out_ref[...] += jnp.dot(we, tl_ref[...], preferred_element_type=jnp.float32)

    @pl.when(flag_ref[0] != 1)
    def _():
        out_ref[...] += jnp.dot(we, tr_ref[...], preferred_element_type=jnp.float32)


def map_call(flag, zo, ze, go, ge, lse, to, tl, tr, tm=256):
    rows = zo.shape[0]
    feats = to.shape[1]
    grid_spec = pltpu.PrefetchScalarGridSpec(
        num_scalar_prefetch=1,
        grid=(rows // tm,),
        in_specs=[
            pl.BlockSpec((tm, zo.shape[1]), lambda i, f: (i, 0)),
            pl.BlockSpec((tm, ze.shape[1]), lambda i, f: (i, 0)),
            pl.BlockSpec((1, go.shape[1]), lambda i, f: (0, 0)),
            pl.BlockSpec((1, ge.shape[1]), lambda i, f: (0, 0)),
            pl.BlockSpec((tm, 1), lambda i, f: (i, 0)),
            pl.BlockSpec(to.shape, lambda i, f: (0, 0)),
            pl.BlockSpec(tl.shape, lambda i, f: (0, 0)),
            pl.BlockSpec(tr.shape, lambda i, f: (0, 0)),
        ],
        out_specs=pl.BlockSpec((tm, feats), lambda i, f: (i, 0)),
    )
    return pl.pallas_call(
        _map_kernel,
        grid_spec=grid_spec,
        out_shape=jax.ShapeDtypeStruct((rows, feats), jnp.float32),
    )(flag, zo, ze, go, ge, lse, to, tl, tr)


def narrow_lse(partial_value, column, narrow_count):
    pieces = [partial_value] + [shifted(partial_value, "narrow", k) for k in range(1, narrow_count)]
    stacked = jnp.stack(pieces)
    order = (column - jnp.arange(narrow_count, dtype=jnp.int32)) % narrow_count
    ordered = stacked[order]
    top = jnp.max(ordered, axis=0)
    return top + jnp.log(jnp.sum(jnp.exp(ordered - top[None, :]), axis=0))


def shards(sources, targets, pair_target, pair_count):
    feature_count = sources.shape[1]
    tgt_blocks = targets.shape[0] // BLK
    wide_count = lax.axis_size("wide")
    narrow_count = lax.axis_size("narrow")
    w = lax.axis_index("wide")
    c = lax.axis_index("narrow")
    group_blocks = tgt_blocks * narrow_count
    scale = (1.0 / math.sqrt(feature_count)) * (1.0 / epsilon)
    inv_eps = 1.0 / epsilon
    log_src = -math.log(wide_count * sources.shape[0])
    log_tgt = -math.log(wide_count * narrow_count * targets.shape[0])

    left = (w - 1 + wide_count) % wide_count
    right = (w + 1) % wide_count
    slot = group_blocks + c

    mine = pair_target[w, slot]
    mine_live = pair_count[w] > slot
    mine_from_left = (mine // group_blocks) == left

    want_right = pair_target[right, slot]
    want_right_live = (pair_count[right] > slot) & ((want_right // group_blocks) == w)
    want_left = pair_target[left, slot]
    want_left_live = (pair_count[left] > slot) & ((want_left // group_blocks) == w)
    left2 = (w - 2 + 2 * wide_count) % wide_count
    right2 = (w + 2) % wide_count
    far_left_same = (pair_count[left2] > slot) & (pair_target[left2, slot] == mine)
    far_right_same = (pair_count[right2] > slot) & (pair_target[right2, slot] == mine)

    blocks = targets.reshape(tgt_blocks, BLK, feature_count)
    to_right = blocks[want_right % tgt_blocks]
    to_left = blocks[want_left % tgt_blocks]
    from_left = shifted(to_right, "wide", 1)
    from_right = shifted(to_left, "wide", -1)

    zo = lax.dot_general(
        sources, targets, (((1,), (1,)), ((), ())), preferred_element_type=jnp.float32
    ) * scale
    extra_mask = jnp.where(mine_live, 0.0, sentinel).astype(jnp.float32)
    flag = mine_from_left.astype(jnp.int32).reshape(1)
    own_width = tgt_blocks * BLK

    def scaled(g_own, g_extra):
        return ((g_own * inv_eps).reshape(1, own_width), (g_extra * inv_eps + extra_mask).reshape(1, BLK))

    g_own = jnp.zeros((own_width,), jnp.float32)
    g_extra = jnp.zeros((BLK,), jnp.float32)
    for iteration in range(ITERS):
        go, ge = scaled(g_own, g_extra)
        if iteration == 0:
            ze, part = ext_call(flag, sources, from_left, from_right, ge, row_lse_call([zo], [go]), scale)
        else:
            part = row_lse_call([zo, ze], [go, ge])
        row = narrow_lse(part.reshape(-1), c, narrow_count)
        f = epsilon * (log_src - row)
        own_cols, extra_cols = col_lse_call(zo, ze, (f * inv_eps).reshape(-1, 1))
        own_cols = own_cols.reshape(tgt_blocks, BLK)
        extra_cols = jnp.where(mine_live, extra_cols.reshape(-1), sentinel)
        from_left_msg = shifted(jnp.stack([extra_cols, own_cols[want_right % tgt_blocks]]), "wide", 1)
        from_right_msg = shifted(jnp.stack([extra_cols, own_cols[want_left % tgt_blocks]]), "wide", -1)
        part_from_left2 = shifted(extra_cols, "wide", 2)
        part_from_right2 = shifted(extra_cols, "wide", -2)
        part_from_left, cover_from_left = from_left_msg[0], from_left_msg[1]
        part_from_right, cover_from_right = from_right_msg[0], from_right_msg[1]
        ids = jnp.arange(tgt_blocks, dtype=jnp.int32)[:, None]
        add_right = jnp.where(want_right_live & (ids == want_right % tgt_blocks), part_from_right[None, :], sentinel)
        add_left = jnp.where(want_left_live & (ids == want_left % tgt_blocks), part_from_left[None, :], sentinel)
        top = jnp.maximum(own_cols, jnp.maximum(add_right, add_left))
        total = jnp.exp(own_cols - top) + jnp.exp(add_right - top) + jnp.exp(add_left - top)
        g_blocks = epsilon * (log_tgt - (top + jnp.log(total)))
        g_own = g_blocks.reshape(-1)
        cover_e = jnp.where(mine_from_left, cover_from_left, cover_from_right)
        other = jnp.where(mine_from_left, part_from_left2, part_from_right2)
        other_live = jnp.where(mine_from_left, far_left_same, far_right_same)
        other = jnp.where(other_live, other, sentinel)
        first = jnp.where(mine_from_left, extra_cols, other)
        second = jnp.where(mine_from_left, other, extra_cols)
        top_e = jnp.maximum(cover_e, jnp.maximum(first, second))
        total_e = jnp.exp(cover_e - top_e) + jnp.exp(first - top_e) + jnp.exp(second - top_e)
        g_extra = epsilon * (log_tgt - (top_e + jnp.log(total_e)))

    go, ge = scaled(g_own, g_extra)
    row = narrow_lse(row_lse_call([zo, ze], [go, ge]).reshape(-1), c, narrow_count)
    source_pot = epsilon * (log_src - row)
    numer = map_call(flag, zo, ze, go, ge, row.reshape(-1, 1), targets, from_left, from_right)

    rows = sources.shape[0]
    quarter = rows // narrow_count
    half = quarter // 2
    chunks = numer.reshape(narrow_count, 2, half, feature_count)

    def chunk(index, side):
        return lax.dynamic_index_in_dim(chunks, index % narrow_count, 0, False)[side]

    far_a = shifted(chunk(c + 2, 0), "narrow", 1)
    far_b = shifted(chunk(c + 2, 1), "narrow", -1)
    to_right = jnp.stack([chunk(c + 1, 0) + far_a, chunk(c + 1, 1)])
    to_left = jnp.stack([chunk(c - 1, 0), chunk(c - 1, 1) + far_b])
    got_left = shifted(to_right, "narrow", 1)
    got_right = shifted(to_left, "narrow", -1)
    mine_sum = jnp.stack([chunk(c, 0), chunk(c, 1)]) + got_left + got_right
    done = mine_sum.astype(jnp.bfloat16).reshape(quarter, feature_count)
    q_left = shifted(done, "narrow", 1)
    q_right = shifted(done, "narrow", -1)
    far_half_a = shifted(q_left[:half], "narrow", 1)
    far_half_b = shifted(q_right[half:], "narrow", -1)
    q_far = jnp.concatenate([far_half_a, far_half_b])
    pieces = jnp.stack([done, q_left, q_far, q_right])
    order = (c - jnp.arange(narrow_count, dtype=jnp.int32)) % narrow_count
    mapped = pieces[order].reshape(rows, feature_count)
    return (source_pot, g_own, mapped)


def solution(mesh):
    placed = (P("wide", None), P(("wide", "narrow"), None), P(), P())
    return jax.shard_map(
        shards,
        mesh=mesh,
        in_specs=placed,
        out_specs=(P("wide"), P(("wide", "narrow")), P("wide", None)),
        check_vma=False,
    )
```

```python
import functools
import math

import jax
import jax.numpy as jnp
from jax import lax
from jax.sharding import PartitionSpec as P
from jax.experimental import pallas as pl
from jax.experimental.pallas import tpu as pltpu

BLK = 1024
ITERS = 2


epsilon = 0.25
sentinel = -1e30


def shifted(x, axis, distance):
    size = lax.axis_size(axis)
    route = [(i, (i + distance) % size) for i in range(size)]
    return lax.ppermute(x, axis, route)


def _row_kernel(*refs):
    n = (len(refs) - 1) // 2
    out_ref = refs[-1]
    scores = [refs[k][...] + refs[n + k][...] for k in range(n)]
    top = scores[0].max(axis=1, keepdims=True)
    for s in scores[1:]:
        top = jnp.maximum(top, s.max(axis=1, keepdims=True))
    total = jnp.sum(jnp.exp(scores[0] - top), axis=1, keepdims=True)
    for s in scores[1:]:
        total = total + jnp.sum(jnp.exp(s - top), axis=1, keepdims=True)
    out_ref[...] = top + jnp.log(total)


def row_lse_call(zs, gs, tm=512):
    rows = zs[0].shape[0]
    in_specs = [pl.BlockSpec((tm, z.shape[1]), lambda i: (i, 0)) for z in zs]
    in_specs += [pl.BlockSpec((1, g.shape[1]), lambda i: (0, 0)) for g in gs]
    return pl.pallas_call(
        _row_kernel,
        grid=(rows // tm,),
        in_specs=in_specs,
        out_specs=pl.BlockSpec((tm, 1), lambda i: (i, 0)),
        out_shape=jax.ShapeDtypeStruct((rows, 1), jnp.float32),
    )(*zs, *gs)


def _col_kernel(zo_ref, ze_ref, f_ref, oo_ref, oe_ref):
    f = f_ref[...]
    for z_ref, o_ref in ((zo_ref, oo_ref), (ze_ref, oe_ref)):
        s = z_ref[...] + f
        top = s.max(axis=0, keepdims=True)
        o_ref[...] = top + jnp.log(jnp.sum(jnp.exp(s - top), axis=0, keepdims=True))


def col_lse_call(zo, ze, f, steps=2):
    rows = zo.shape[0]
    wo = zo.shape[1] // steps
    we = ze.shape[1] // steps
    return pl.pallas_call(
        _col_kernel,
        grid=(steps,),
        in_specs=[
            pl.BlockSpec((rows, wo), lambda j: (0, j)),
            pl.BlockSpec((rows, we), lambda j: (0, j)),
            pl.BlockSpec((rows, 1), lambda j: (0, 0)),
        ],
        out_specs=[
            pl.BlockSpec((1, wo), lambda j: (0, j)),
            pl.BlockSpec((1, we), lambda j: (0, j)),
        ],
        out_shape=[
            jax.ShapeDtypeStruct((1, zo.shape[1]), jnp.float32),
            jax.ShapeDtypeStruct((1, ze.shape[1]), jnp.float32),
        ],
    )(zo, ze, f)


def _ext_kernel(flag_ref, s_ref, l_ref, r_ref, ge_ref, own_ref, ze_ref, part_ref, *, scale):
    def product(e_ref):
        ze_ref[...] = lax.dot_general(
            s_ref[...], e_ref[...], (((1,), (1,)), ((), ())), preferred_element_type=jnp.float32
        ) * scale

    @pl.when(flag_ref[0] == 1)
    def _():
        product(l_ref)

    @pl.when(flag_ref[0] != 1)
    def _():
        product(r_ref)

    s = ze_ref[...] + ge_ref[...]
    own = own_ref[...]
    top = jnp.maximum(s.max(axis=1, keepdims=True), own)
    part_ref[...] = top + jnp.log(jnp.sum(jnp.exp(s - top), axis=1, keepdims=True) + jnp.exp(own - top))


def ext_call(flag, sources, from_left, from_right, ge, own_part, scale, tm=512):
    rows, feats = sources.shape
    width = from_left.shape[0]
    grid_spec = pltpu.PrefetchScalarGridSpec(
        num_scalar_prefetch=1,
        grid=(rows // tm,),
        in_specs=[
            pl.BlockSpec((tm, feats), lambda i, f: (i, 0)),
            pl.BlockSpec(from_left.shape, lambda i, f: (0, 0)),
            pl.BlockSpec(from_right.shape, lambda i, f: (0, 0)),
            pl.BlockSpec((1, width), lambda i, f: (0, 0)),
            pl.BlockSpec((tm, 1), lambda i, f: (i, 0)),
        ],
        out_specs=[
            pl.BlockSpec((tm, width), lambda i, f: (i, 0)),
            pl.BlockSpec((tm, 1), lambda i, f: (i, 0)),
        ],
    )
    return pl.pallas_call(
        functools.partial(_ext_kernel, scale=scale),
        grid_spec=grid_spec,
        out_shape=[
            jax.ShapeDtypeStruct((rows, width), jnp.float32),
            jax.ShapeDtypeStruct((rows, 1), jnp.float32),
        ],
    )(flag, sources, from_left, from_right, ge, own_part)


def _map_kernel(flag_ref, zo_ref, ze_ref, go_ref, ge_ref, l_ref, to_ref, tl_ref, tr_ref, out_ref):
    lse = l_ref[...]
    wo = jnp.exp(zo_ref[...] + go_ref[...] - lse).astype(jnp.bfloat16)
    we = jnp.exp(ze_ref[...] + ge_ref[...] - lse).astype(jnp.bfloat16)
    out_ref[...] = jnp.dot(wo, to_ref[...], preferred_element_type=jnp.float32)

    @pl.when(flag_ref[0] == 1)
    def _():
        out_ref[...] += jnp.dot(we, tl_ref[...], preferred_element_type=jnp.float32)

    @pl.when(flag_ref[0] != 1)
    def _():
        out_ref[...] += jnp.dot(we, tr_ref[...], preferred_element_type=jnp.float32)


def map_call(flag, zo, ze, go, ge, lse, to, tl, tr, tm=512):
    rows = zo.shape[0]
    feats = to.shape[1]
    grid_spec = pltpu.PrefetchScalarGridSpec(
        num_scalar_prefetch=1,
        grid=(rows // tm,),
        in_specs=[
            pl.BlockSpec((tm, zo.shape[1]), lambda i, f: (i, 0)),
            pl.BlockSpec((tm, ze.shape[1]), lambda i, f: (i, 0)),
            pl.BlockSpec((1, go.shape[1]), lambda i, f: (0, 0)),
            pl.BlockSpec((1, ge.shape[1]), lambda i, f: (0, 0)),
            pl.BlockSpec((tm, 1), lambda i, f: (i, 0)),
            pl.BlockSpec(to.shape, lambda i, f: (0, 0)),
            pl.BlockSpec(tl.shape, lambda i, f: (0, 0)),
            pl.BlockSpec(tr.shape, lambda i, f: (0, 0)),
        ],
        out_specs=pl.BlockSpec((tm, feats), lambda i, f: (i, 0)),
    )
    return pl.pallas_call(
        _map_kernel,
        grid_spec=grid_spec,
        out_shape=jax.ShapeDtypeStruct((rows, feats), jnp.float32),
    )(flag, zo, ze, go, ge, lse, to, tl, tr)


def narrow_lse(partial_value, column, narrow_count):
    pieces = [partial_value] + [shifted(partial_value, "narrow", k) for k in range(1, narrow_count)]
    stacked = jnp.stack(pieces)
    order = (column - jnp.arange(narrow_count, dtype=jnp.int32)) % narrow_count
    ordered = stacked[order]
    top = jnp.max(ordered, axis=0)
    return top + jnp.log(jnp.sum(jnp.exp(ordered - top[None, :]), axis=0))


def shards(sources, targets, pair_target, pair_count):
    feature_count = sources.shape[1]
    tgt_blocks = targets.shape[0] // BLK
    wide_count = lax.axis_size("wide")
    narrow_count = lax.axis_size("narrow")
    w = lax.axis_index("wide")
    c = lax.axis_index("narrow")
    group_blocks = tgt_blocks * narrow_count
    scale = (1.0 / math.sqrt(feature_count)) * (1.0 / epsilon)
    inv_eps = 1.0 / epsilon
    log_src = -math.log(wide_count * sources.shape[0])
    log_tgt = -math.log(wide_count * narrow_count * targets.shape[0])

    left = (w - 1 + wide_count) % wide_count
    right = (w + 1) % wide_count
    slot = group_blocks + c

    mine = pair_target[w, slot]
    mine_live = pair_count[w] > slot
    mine_from_left = (mine // group_blocks) == left

    want_right = pair_target[right, slot]
    want_right_live = (pair_count[right] > slot) & ((want_right // group_blocks) == w)
    want_left = pair_target[left, slot]
    want_left_live = (pair_count[left] > slot) & ((want_left // group_blocks) == w)
    left2 = (w - 2 + 2 * wide_count) % wide_count
    right2 = (w + 2) % wide_count
    far_left_same = (pair_count[left2] > slot) & (pair_target[left2, slot] == mine)
    far_right_same = (pair_count[right2] > slot) & (pair_target[right2, slot] == mine)

    blocks = targets.reshape(tgt_blocks, BLK, feature_count)
    to_right = blocks[want_right % tgt_blocks]
    to_left = blocks[want_left % tgt_blocks]
    from_left = shifted(to_right, "wide", 1)
    from_right = shifted(to_left, "wide", -1)

    zo = lax.dot_general(
        sources, targets, (((1,), (1,)), ((), ())), preferred_element_type=jnp.float32
    ) * scale
    extra_mask = jnp.where(mine_live, 0.0, sentinel).astype(jnp.float32)
    flag = mine_from_left.astype(jnp.int32).reshape(1)
    own_width = tgt_blocks * BLK

    def scaled(g_own, g_extra):
        return ((g_own * inv_eps).reshape(1, own_width), (g_extra * inv_eps + extra_mask).reshape(1, BLK))

    g_own = jnp.zeros((own_width,), jnp.float32)
    g_extra = jnp.zeros((BLK,), jnp.float32)
    for iteration in range(ITERS):
        go, ge = scaled(g_own, g_extra)
        if iteration == 0:
            ze, part = ext_call(flag, sources, from_left, from_right, ge, row_lse_call([zo], [go]), scale)
        else:
            part = row_lse_call([zo, ze], [go, ge])
        row = narrow_lse(part.reshape(-1), c, narrow_count)
        f = epsilon * (log_src - row)
        own_cols, extra_cols = col_lse_call(zo, ze, (f * inv_eps).reshape(-1, 1))
        own_cols = own_cols.reshape(tgt_blocks, BLK)
        extra_cols = jnp.where(mine_live, extra_cols.reshape(-1), sentinel)
        from_left_msg = shifted(jnp.stack([extra_cols, own_cols[want_right % tgt_blocks]]), "wide", 1)
        from_right_msg = shifted(jnp.stack([extra_cols, own_cols[want_left % tgt_blocks]]), "wide", -1)
        part_from_left2 = shifted(extra_cols, "wide", 2)
        part_from_right2 = shifted(extra_cols, "wide", -2)
        part_from_left, cover_from_left = from_left_msg[0], from_left_msg[1]
        part_from_right, cover_from_right = from_right_msg[0], from_right_msg[1]
        ids = jnp.arange(tgt_blocks, dtype=jnp.int32)[:, None]
        add_right = jnp.where(want_right_live & (ids == want_right % tgt_blocks), part_from_right[None, :], sentinel)
        add_left = jnp.where(want_left_live & (ids == want_left % tgt_blocks), part_from_left[None, :], sentinel)
        top = jnp.maximum(own_cols, jnp.maximum(add_right, add_left))
        total = jnp.exp(own_cols - top) + jnp.exp(add_right - top) + jnp.exp(add_left - top)
        g_blocks = epsilon * (log_tgt - (top + jnp.log(total)))
        g_own = g_blocks.reshape(-1)
        cover_e = jnp.where(mine_from_left, cover_from_left, cover_from_right)
        other = jnp.where(mine_from_left, part_from_left2, part_from_right2)
        other_live = jnp.where(mine_from_left, far_left_same, far_right_same)
        other = jnp.where(other_live, other, sentinel)
        first = jnp.where(mine_from_left, extra_cols, other)
        second = jnp.where(mine_from_left, other, extra_cols)
        top_e = jnp.maximum(cover_e, jnp.maximum(first, second))
        total_e = jnp.exp(cover_e - top_e) + jnp.exp(first - top_e) + jnp.exp(second - top_e)
        g_extra = epsilon * (log_tgt - (top_e + jnp.log(total_e)))

    go, ge = scaled(g_own, g_extra)
    row = narrow_lse(row_lse_call([zo, ze], [go, ge]).reshape(-1), c, narrow_count)
    source_pot = epsilon * (log_src - row)
    numer = map_call(flag, zo, ze, go, ge, row.reshape(-1, 1), targets, from_left, from_right)

    rows = sources.shape[0]
    quarter = rows // narrow_count
    half = quarter // 2
    chunks = numer.reshape(narrow_count, 2, half, feature_count)

    def chunk(index, side):
        return lax.dynamic_index_in_dim(chunks, index % narrow_count, 0, False)[side]

    far_a = shifted(chunk(c + 2, 0), "narrow", 1)
    far_b = shifted(chunk(c + 2, 1), "narrow", -1)
    to_right = jnp.stack([chunk(c + 1, 0) + far_a, chunk(c + 1, 1)])
    to_left = jnp.stack([chunk(c - 1, 0), chunk(c - 1, 1) + far_b])
    got_left = shifted(to_right, "narrow", 1)
    got_right = shifted(to_left, "narrow", -1)
    mine_sum = jnp.stack([chunk(c, 0), chunk(c, 1)]) + got_left + got_right
    done = mine_sum.astype(jnp.bfloat16).reshape(quarter, feature_count)
    q_left = shifted(done, "narrow", 1)
    q_right = shifted(done, "narrow", -1)
    far_half_a = shifted(q_left[:half], "narrow", 1)
    far_half_b = shifted(q_right[half:], "narrow", -1)
    q_far = jnp.concatenate([far_half_a, far_half_b])
    mapped = jnp.zeros((rows, feature_count), jnp.bfloat16)
    for k, piece in enumerate((done, q_left, q_far, q_right)):
        mapped = lax.dynamic_update_slice_in_dim(mapped, piece, ((c - k) % narrow_count) * quarter, 0)
    return (source_pot, g_own, mapped)


def solution(mesh):
    placed = (P("wide", None), P(("wide", "narrow"), None), P(), P())
    return jax.shard_map(
        shards,
        mesh=mesh,
        in_specs=placed,
        out_specs=(P("wide"), P(("wide", "narrow")), P("wide", None)),
        check_vma=False,
    )
```

```python
import functools
import math

import jax
import jax.numpy as jnp
from jax import lax
from jax.sharding import PartitionSpec as P
from jax.experimental import pallas as pl
from jax.experimental.pallas import tpu as pltpu

BLK = 1024
ITERS = 2


epsilon = 0.25
sentinel = -1e30


def shifted(x, axis, distance):
    size = lax.axis_size(axis)
    route = [(i, (i + distance) % size) for i in range(size)]
    return lax.ppermute(x, axis, route)


def _row_kernel(*refs):
    n = (len(refs) - 1) // 2
    out_ref = refs[-1]
    scores = [refs[k][...] + refs[n + k][...] for k in range(n)]
    top = scores[0].max(axis=1, keepdims=True)
    for s in scores[1:]:
        top = jnp.maximum(top, s.max(axis=1, keepdims=True))
    total = jnp.sum(jnp.exp(scores[0] - top), axis=1, keepdims=True)
    for s in scores[1:]:
        total = total + jnp.sum(jnp.exp(s - top), axis=1, keepdims=True)
    out_ref[...] = top + jnp.log(total)


def row_lse_call(zs, gs, tm=512):
    rows = zs[0].shape[0]
    in_specs = [pl.BlockSpec((tm, z.shape[1]), lambda i: (i, 0)) for z in zs]
    in_specs += [pl.BlockSpec((1, g.shape[1]), lambda i: (0, 0)) for g in gs]
    return pl.pallas_call(
        _row_kernel,
        grid=(rows // tm,),
        in_specs=in_specs,
        out_specs=pl.BlockSpec((tm, 1), lambda i: (i, 0)),
        out_shape=jax.ShapeDtypeStruct((rows, 1), jnp.float32),
    )(*zs, *gs)


def _col_kernel(zo_ref, ze_ref, f_ref, oo_ref, oe_ref):
    f = f_ref[...]
    for z_ref, o_ref in ((zo_ref, oo_ref), (ze_ref, oe_ref)):
        s = z_ref[...] + f
        top = s.max(axis=0, keepdims=True)
        o_ref[...] = top + jnp.log(jnp.sum(jnp.exp(s - top), axis=0, keepdims=True))


def col_lse_call(zo, ze, f, steps=2):
    rows = zo.shape[0]
    wo = zo.shape[1] // steps
    we = ze.shape[1] // steps
    return pl.pallas_call(
        _col_kernel,
        grid=(steps,),
        in_specs=[
            pl.BlockSpec((rows, wo), lambda j: (0, j)),
            pl.BlockSpec((rows, we), lambda j: (0, j)),
            pl.BlockSpec((rows, 1), lambda j: (0, 0)),
        ],
        out_specs=[
            pl.BlockSpec((1, wo), lambda j: (0, j)),
            pl.BlockSpec((1, we), lambda j: (0, j)),
        ],
        out_shape=[
            jax.ShapeDtypeStruct((1, zo.shape[1]), jnp.float32),
            jax.ShapeDtypeStruct((1, ze.shape[1]), jnp.float32),
        ],
    )(zo, ze, f)


def _ext_kernel(flag_ref, s_ref, l_ref, r_ref, ge_ref, own_ref, ze_ref, part_ref, *, scale):
    def product(e_ref):
        ze_ref[...] = lax.dot_general(
            s_ref[...], e_ref[...], (((1,), (1,)), ((), ())), preferred_element_type=jnp.float32
        ) * scale

    @pl.when(flag_ref[0] == 1)
    def _():
        product(l_ref)

    @pl.when(flag_ref[0] != 1)
    def _():
        product(r_ref)

    s = ze_ref[...] + ge_ref[...]
    own = own_ref[...]
    top = jnp.maximum(s.max(axis=1, keepdims=True), own)
    part_ref[...] = top + jnp.log(jnp.sum(jnp.exp(s - top), axis=1, keepdims=True) + jnp.exp(own - top))


def ext_call(flag, sources, from_left, from_right, ge, own_part, scale, tm=512):
    rows, feats = sources.shape
    width = from_left.shape[0]
    grid_spec = pltpu.PrefetchScalarGridSpec(
        num_scalar_prefetch=1,
        grid=(rows // tm,),
        in_specs=[
            pl.BlockSpec((tm, feats), lambda i, f: (i, 0)),
            pl.BlockSpec(from_left.shape, lambda i, f: (0, 0)),
            pl.BlockSpec(from_right.shape, lambda i, f: (0, 0)),
            pl.BlockSpec((1, width), lambda i, f: (0, 0)),
            pl.BlockSpec((tm, 1), lambda i, f: (i, 0)),
        ],
        out_specs=[
            pl.BlockSpec((tm, width), lambda i, f: (i, 0)),
            pl.BlockSpec((tm, 1), lambda i, f: (i, 0)),
        ],
    )
    return pl.pallas_call(
        functools.partial(_ext_kernel, scale=scale),
        grid_spec=grid_spec,
        out_shape=[
            jax.ShapeDtypeStruct((rows, width), jnp.float32),
            jax.ShapeDtypeStruct((rows, 1), jnp.float32),
        ],
    )(flag, sources, from_left, from_right, ge, own_part)


def _map_kernel(flag_ref, pos_ref, zo_ref, ze_ref, go_ref, ge_ref, l_ref, to_ref, tl_ref, tr_ref, out_ref):
    lse = l_ref[...]
    wo = jnp.exp(zo_ref[...] + go_ref[...] - lse).astype(jnp.bfloat16)
    we = jnp.exp(ze_ref[...] + ge_ref[...] - lse).astype(jnp.bfloat16)
    out_ref[...] = jnp.dot(wo, to_ref[...], preferred_element_type=jnp.float32)

    @pl.when(flag_ref[0] == 1)
    def _():
        out_ref[...] += jnp.dot(we, tl_ref[...], preferred_element_type=jnp.float32)

    @pl.when(flag_ref[0] != 1)
    def _():
        out_ref[...] += jnp.dot(we, tr_ref[...], preferred_element_type=jnp.float32)


def map_call(flag, pos, zo, ze, go, ge, lse, to, tl, tr, tm=256):
    rows = zo.shape[0]
    feats = to.shape[1]
    grid_spec = pltpu.PrefetchScalarGridSpec(
        num_scalar_prefetch=2,
        grid=(rows // tm,),
        in_specs=[
            pl.BlockSpec((tm, zo.shape[1]), lambda i, f, p: (i, 0)),
            pl.BlockSpec((tm, ze.shape[1]), lambda i, f, p: (i, 0)),
            pl.BlockSpec((1, go.shape[1]), lambda i, f, p: (0, 0)),
            pl.BlockSpec((1, ge.shape[1]), lambda i, f, p: (0, 0)),
            pl.BlockSpec((tm, 1), lambda i, f, p: (i, 0)),
            pl.BlockSpec(to.shape, lambda i, f, p: (0, 0)),
            pl.BlockSpec(tl.shape, lambda i, f, p: (0, 0)),
            pl.BlockSpec(tr.shape, lambda i, f, p: (0, 0)),
        ],
        out_specs=pl.BlockSpec((tm, feats), lambda i, f, p: (p[i], 0)),
    )
    return pl.pallas_call(
        _map_kernel,
        grid_spec=grid_spec,
        out_shape=jax.ShapeDtypeStruct((rows, feats), jnp.float32),
    )(flag, pos, zo, ze, go, ge, lse, to, tl, tr)


def narrow_lse(partial_value, column, narrow_count):
    pieces = [partial_value] + [shifted(partial_value, "narrow", k) for k in range(1, narrow_count)]
    stacked = jnp.stack(pieces)
    order = (column - jnp.arange(narrow_count, dtype=jnp.int32)) % narrow_count
    ordered = stacked[order]
    top = jnp.max(ordered, axis=0)
    return top + jnp.log(jnp.sum(jnp.exp(ordered - top[None, :]), axis=0))


def shards(sources, targets, pair_target, pair_count):
    feature_count = sources.shape[1]
    tgt_blocks = targets.shape[0] // BLK
    wide_count = lax.axis_size("wide")
    narrow_count = lax.axis_size("narrow")
    w = lax.axis_index("wide")
    c = lax.axis_index("narrow")
    group_blocks = tgt_blocks * narrow_count
    scale = (1.0 / math.sqrt(feature_count)) * (1.0 / epsilon)
    inv_eps = 1.0 / epsilon
    log_src = -math.log(wide_count * sources.shape[0])
    log_tgt = -math.log(wide_count * narrow_count * targets.shape[0])

    left = (w - 1 + wide_count) % wide_count
    right = (w + 1) % wide_count
    slot = group_blocks + c

    mine = pair_target[w, slot]
    mine_live = pair_count[w] > slot
    mine_from_left = (mine // group_blocks) == left

    want_right = pair_target[right, slot]
    want_right_live = (pair_count[right] > slot) & ((want_right // group_blocks) == w)
    want_left = pair_target[left, slot]
    want_left_live = (pair_count[left] > slot) & ((want_left // group_blocks) == w)
    left2 = (w - 2 + 2 * wide_count) % wide_count
    right2 = (w + 2) % wide_count
    far_left_same = (pair_count[left2] > slot) & (pair_target[left2, slot] == mine)
    far_right_same = (pair_count[right2] > slot) & (pair_target[right2, slot] == mine)

    blocks = targets.reshape(tgt_blocks, BLK, feature_count)
    to_right = blocks[want_right % tgt_blocks]
    to_left = blocks[want_left % tgt_blocks]
    from_left = shifted(to_right, "wide", 1)
    from_right = shifted(to_left, "wide", -1)

    zo = lax.dot_general(
        sources, targets, (((1,), (1,)), ((), ())), preferred_element_type=jnp.float32
    ) * scale
    extra_mask = jnp.where(mine_live, 0.0, sentinel).astype(jnp.float32)
    flag = mine_from_left.astype(jnp.int32).reshape(1)
    own_width = tgt_blocks * BLK

    def scaled(g_own, g_extra):
        return ((g_own * inv_eps).reshape(1, own_width), (g_extra * inv_eps + extra_mask).reshape(1, BLK))

    g_own = jnp.zeros((own_width,), jnp.float32)
    g_extra = jnp.zeros((BLK,), jnp.float32)
    for iteration in range(ITERS):
        go, ge = scaled(g_own, g_extra)
        if iteration == 0:
            ze, part = ext_call(flag, sources, from_left, from_right, ge, row_lse_call([zo], [go]), scale)
        else:
            part = row_lse_call([zo, ze], [go, ge])
        row = narrow_lse(part.reshape(-1), c, narrow_count)
        f = epsilon * (log_src - row)
        own_cols, extra_cols = col_lse_call(zo, ze, (f * inv_eps).reshape(-1, 1))
        own_cols = own_cols.reshape(tgt_blocks, BLK)
        extra_cols = jnp.where(mine_live, extra_cols.reshape(-1), sentinel)
        from_left_msg = shifted(jnp.stack([extra_cols, own_cols[want_right % tgt_blocks]]), "wide", 1)
        from_right_msg = shifted(jnp.stack([extra_cols, own_cols[want_left % tgt_blocks]]), "wide", -1)
        part_from_left2 = shifted(extra_cols, "wide", 2)
        part_from_right2 = shifted(extra_cols, "wide", -2)
        part_from_left, cover_from_left = from_left_msg[0], from_left_msg[1]
        part_from_right, cover_from_right = from_right_msg[0], from_right_msg[1]
        ids = jnp.arange(tgt_blocks, dtype=jnp.int32)[:, None]
        add_right = jnp.where(want_right_live & (ids == want_right % tgt_blocks), part_from_right[None, :], sentinel)
        add_left = jnp.where(want_left_live & (ids == want_left % tgt_blocks), part_from_left[None, :], sentinel)
        top = jnp.maximum(own_cols, jnp.maximum(add_right, add_left))
        total = jnp.exp(own_cols - top) + jnp.exp(add_right - top) + jnp.exp(add_left - top)
        g_blocks = epsilon * (log_tgt - (top + jnp.log(total)))
        g_own = g_blocks.reshape(-1)
        cover_e = jnp.where(mine_from_left, cover_from_left, cover_from_right)
        other = jnp.where(mine_from_left, part_from_left2, part_from_right2)
        other_live = jnp.where(mine_from_left, far_left_same, far_right_same)
        other = jnp.where(other_live, other, sentinel)
        first = jnp.where(mine_from_left, extra_cols, other)
        second = jnp.where(mine_from_left, other, extra_cols)
        top_e = jnp.maximum(cover_e, jnp.maximum(first, second))
        total_e = jnp.exp(cover_e - top_e) + jnp.exp(first - top_e) + jnp.exp(second - top_e)
        g_extra = epsilon * (log_tgt - (top_e + jnp.log(total_e)))

    go, ge = scaled(g_own, g_extra)
    row = narrow_lse(row_lse_call([zo, ze], [go, ge]).reshape(-1), c, narrow_count)
    source_pot = epsilon * (log_src - row)
    place = jnp.array([3, 1, 0, 2], jnp.int32)
    pos = place[(jnp.arange(narrow_count, dtype=jnp.int32) - c) % narrow_count]
    numer = map_call(flag, pos, zo, ze, go, ge, row.reshape(-1, 1), targets, from_left, from_right,
                     tm=sources.shape[0] // narrow_count)

    rows = sources.shape[0]
    quarter = rows // narrow_count
    half = quarter // 2
    chunks = numer.reshape(narrow_count, 2, half, feature_count)
    slot_of = {2: 0, 1: 1, -1: 2, 0: 3}

    def chunk(offset, side):
        return chunks[slot_of[offset], side]

    far_a = shifted(chunk(2, 0), "narrow", 1)
    far_b = shifted(chunk(2, 1), "narrow", -1)
    to_right = jnp.stack([chunk(1, 0) + far_a, chunk(1, 1)])
    to_left = jnp.stack([chunk(-1, 0), chunk(-1, 1) + far_b])
    got_left = shifted(to_right, "narrow", 1)
    got_right = shifted(to_left, "narrow", -1)
    mine_sum = jnp.stack([chunk(0, 0), chunk(0, 1)]) + got_left + got_right
    done = mine_sum.astype(jnp.bfloat16).reshape(quarter, feature_count)
    q_left = shifted(done, "narrow", 1)
    q_right = shifted(done, "narrow", -1)
    far_half_a = shifted(q_left[:half], "narrow", 1)
    far_half_b = shifted(q_right[half:], "narrow", -1)
    q_far = jnp.concatenate([far_half_a, far_half_b])
    mapped = jnp.zeros((rows, feature_count), jnp.bfloat16)
    for k, piece in enumerate((done, q_left, q_far, q_right)):
        mapped = lax.dynamic_update_slice_in_dim(mapped, piece, ((c - k) % narrow_count) * quarter, 0)
    return (source_pot, g_own, mapped)


def solution(mesh):
    placed = (P("wide", None), P(("wide", "narrow"), None), P(), P())
    return jax.shard_map(
        shards,
        mesh=mesh,
        in_specs=placed,
        out_specs=(P("wide"), P(("wide", "narrow")), P("wide", None)),
        check_vma=False,
    )
```

```python
import functools
import math

import jax
import jax.numpy as jnp
from jax import lax
from jax.sharding import PartitionSpec as P
from jax.experimental import pallas as pl
from jax.experimental.pallas import tpu as pltpu

BLK = 1024
ITERS = 2


epsilon = 0.25
sentinel = -1e30


def shifted(x, axis, distance):
    size = lax.axis_size(axis)
    route = [(i, (i + distance) % size) for i in range(size)]
    return lax.ppermute(x, axis, route)


def _row_kernel(*refs):
    n = (len(refs) - 1) // 2
    out_ref = refs[-1]
    scores = [refs[k][...] + refs[n + k][...] for k in range(n)]
    top = scores[0].max(axis=1, keepdims=True)
    for s in scores[1:]:
        top = jnp.maximum(top, s.max(axis=1, keepdims=True))
    total = jnp.sum(jnp.exp(scores[0] - top), axis=1, keepdims=True)
    for s in scores[1:]:
        total = total + jnp.sum(jnp.exp(s - top), axis=1, keepdims=True)
    out_ref[...] = top + jnp.log(total)


def row_lse_call(zs, gs, tm=512):
    rows = zs[0].shape[0]
    in_specs = [pl.BlockSpec((tm, z.shape[1]), lambda i: (i, 0)) for z in zs]
    in_specs += [pl.BlockSpec((1, g.shape[1]), lambda i: (0, 0)) for g in gs]
    return pl.pallas_call(
        _row_kernel,
        grid=(rows // tm,),
        in_specs=in_specs,
        out_specs=pl.BlockSpec((tm, 1), lambda i: (i, 0)),
        out_shape=jax.ShapeDtypeStruct((rows, 1), jnp.float32),
    )(*zs, *gs)


def _col_kernel(zo_ref, ze_ref, f_ref, oo_ref, oe_ref):
    f = f_ref[...]
    for z_ref, o_ref in ((zo_ref, oo_ref), (ze_ref, oe_ref)):
        s = z_ref[...] + f
        top = s.max(axis=0, keepdims=True)
        o_ref[...] = top + jnp.log(jnp.sum(jnp.exp(s - top), axis=0, keepdims=True))


def col_lse_call(zo, ze, f, steps=2):
    rows = zo.shape[0]
    wo = zo.shape[1] // steps
    we = ze.shape[1] // steps
    return pl.pallas_call(
        _col_kernel,
        grid=(steps,),
        in_specs=[
            pl.BlockSpec((rows, wo), lambda j: (0, j)),
            pl.BlockSpec((rows, we), lambda j: (0, j)),
            pl.BlockSpec((rows, 1), lambda j: (0, 0)),
        ],
        out_specs=[
            pl.BlockSpec((1, wo), lambda j: (0, j)),
            pl.BlockSpec((1, we), lambda j: (0, j)),
        ],
        out_shape=[
            jax.ShapeDtypeStruct((1, zo.shape[1]), jnp.float32),
            jax.ShapeDtypeStruct((1, ze.shape[1]), jnp.float32),
        ],
    )(zo, ze, f)


def _ext_kernel(flag_ref, s_ref, l_ref, r_ref, ge_ref, zo_ref, go_ref, ze_ref, part_ref, *, scale):
    def product(e_ref):
        ze_ref[...] = lax.dot_general(
            s_ref[...], e_ref[...], (((1,), (1,)), ((), ())), preferred_element_type=jnp.float32
        ) * scale

    @pl.when(flag_ref[0] == 1)
    def _():
        product(l_ref)

    @pl.when(flag_ref[0] != 1)
    def _():
        product(r_ref)

    s = ze_ref[...] + ge_ref[...]
    so = zo_ref[...] + go_ref[...]
    top = jnp.maximum(s.max(axis=1, keepdims=True), so.max(axis=1, keepdims=True))
    total = jnp.sum(jnp.exp(s - top), axis=1, keepdims=True) + jnp.sum(jnp.exp(so - top), axis=1, keepdims=True)
    part_ref[...] = top + jnp.log(total)


def ext_call(flag, sources, from_left, from_right, ge, zo, go, scale, tm=512):
    rows, feats = sources.shape
    width = from_left.shape[0]
    grid_spec = pltpu.PrefetchScalarGridSpec(
        num_scalar_prefetch=1,
        grid=(rows // tm,),
        in_specs=[
            pl.BlockSpec((tm, feats), lambda i, f: (i, 0)),
            pl.BlockSpec(from_left.shape, lambda i, f: (0, 0)),
            pl.BlockSpec(from_right.shape, lambda i, f: (0, 0)),
            pl.BlockSpec((1, width), lambda i, f: (0, 0)),
            pl.BlockSpec((tm, zo.shape[1]), lambda i, f: (i, 0)),
            pl.BlockSpec((1, go.shape[1]), lambda i, f: (0, 0)),
        ],
        out_specs=[
            pl.BlockSpec((tm, width), lambda i, f: (i, 0)),
            pl.BlockSpec((tm, 1), lambda i, f: (i, 0)),
        ],
    )
    return pl.pallas_call(
        functools.partial(_ext_kernel, scale=scale),
        grid_spec=grid_spec,
        out_shape=[
            jax.ShapeDtypeStruct((rows, width), jnp.float32),
            jax.ShapeDtypeStruct((rows, 1), jnp.float32),
        ],
    )(flag, sources, from_left, from_right, ge, zo, go)


def _map_kernel(flag_ref, pos_ref, zo_ref, ze_ref, go_ref, ge_ref, l_ref, to_ref, tl_ref, tr_ref, out_ref):
    lse = l_ref[...]
    wo = jnp.exp(zo_ref[...] + go_ref[...] - lse).astype(jnp.bfloat16)
    we = jnp.exp(ze_ref[...] + ge_ref[...] - lse).astype(jnp.bfloat16)
    out_ref[...] = jnp.dot(wo, to_ref[...], preferred_element_type=jnp.float32)

    @pl.when(flag_ref[0] == 1)
    def _():
        out_ref[...] += jnp.dot(we, tl_ref[...], preferred_element_type=jnp.float32)

    @pl.when(flag_ref[0] != 1)
    def _():
        out_ref[...] += jnp.dot(we, tr_ref[...], preferred_element_type=jnp.float32)


def map_call(flag, pos, zo, ze, go, ge, lse, to, tl, tr, tm=256):
    rows = zo.shape[0]
    feats = to.shape[1]
    grid_spec = pltpu.PrefetchScalarGridSpec(
        num_scalar_prefetch=2,
        grid=(rows // tm,),
        in_specs=[
            pl.BlockSpec((tm, zo.shape[1]), lambda i, f, p: (i, 0)),
            pl.BlockSpec((tm, ze.shape[1]), lambda i, f, p: (i, 0)),
            pl.BlockSpec((1, go.shape[1]), lambda i, f, p: (0, 0)),
            pl.BlockSpec((1, ge.shape[1]), lambda i, f, p: (0, 0)),
            pl.BlockSpec((tm, 1), lambda i, f, p: (i, 0)),
            pl.BlockSpec(to.shape, lambda i, f, p: (0, 0)),
            pl.BlockSpec(tl.shape, lambda i, f, p: (0, 0)),
            pl.BlockSpec(tr.shape, lambda i, f, p: (0, 0)),
        ],
        out_specs=pl.BlockSpec((tm, feats), lambda i, f, p: (p[i], 0)),
    )
    return pl.pallas_call(
        _map_kernel,
        grid_spec=grid_spec,
        out_shape=jax.ShapeDtypeStruct((rows, feats), jnp.float32),
    )(flag, pos, zo, ze, go, ge, lse, to, tl, tr)


def narrow_lse(partial_value, column, narrow_count):
    pieces = [partial_value] + [shifted(partial_value, "narrow", k) for k in range(1, narrow_count)]
    stacked = jnp.stack(pieces)
    order = (column - jnp.arange(narrow_count, dtype=jnp.int32)) % narrow_count
    ordered = stacked[order]
    top = jnp.max(ordered, axis=0)
    return top + jnp.log(jnp.sum(jnp.exp(ordered - top[None, :]), axis=0))


def shards(sources, targets, pair_target, pair_count):
    feature_count = sources.shape[1]
    tgt_blocks = targets.shape[0] // BLK
    wide_count = lax.axis_size("wide")
    narrow_count = lax.axis_size("narrow")
    w = lax.axis_index("wide")
    c = lax.axis_index("narrow")
    group_blocks = tgt_blocks * narrow_count
    scale = (1.0 / math.sqrt(feature_count)) * (1.0 / epsilon)
    inv_eps = 1.0 / epsilon
    log_src = -math.log(wide_count * sources.shape[0])
    log_tgt = -math.log(wide_count * narrow_count * targets.shape[0])

    left = (w - 1 + wide_count) % wide_count
    right = (w + 1) % wide_count
    slot = group_blocks + c

    mine = pair_target[w, slot]
    mine_live = pair_count[w] > slot
    mine_from_left = (mine // group_blocks) == left

    want_right = pair_target[right, slot]
    want_right_live = (pair_count[right] > slot) & ((want_right // group_blocks) == w)
    want_left = pair_target[left, slot]
    want_left_live = (pair_count[left] > slot) & ((want_left // group_blocks) == w)
    left2 = (w - 2 + 2 * wide_count) % wide_count
    right2 = (w + 2) % wide_count
    far_left_same = (pair_count[left2] > slot) & (pair_target[left2, slot] == mine)
    far_right_same = (pair_count[right2] > slot) & (pair_target[right2, slot] == mine)

    blocks = targets.reshape(tgt_blocks, BLK, feature_count)
    to_right = blocks[want_right % tgt_blocks]
    to_left = blocks[want_left % tgt_blocks]
    from_left = shifted(to_right, "wide", 1)
    from_right = shifted(to_left, "wide", -1)

    zo = lax.dot_general(
        sources, targets, (((1,), (1,)), ((), ())), preferred_element_type=jnp.float32
    ) * scale
    extra_mask = jnp.where(mine_live, 0.0, sentinel).astype(jnp.float32)
    flag = mine_from_left.astype(jnp.int32).reshape(1)
    own_width = tgt_blocks * BLK

    def scaled(g_own, g_extra):
        return ((g_own * inv_eps).reshape(1, own_width), (g_extra * inv_eps + extra_mask).reshape(1, BLK))

    g_own = jnp.zeros((own_width,), jnp.float32)
    g_extra = jnp.zeros((BLK,), jnp.float32)
    for iteration in range(ITERS):
        go, ge = scaled(g_own, g_extra)
        if iteration == 0:
            ze, part = ext_call(flag, sources, from_left, from_right, ge, zo, go, scale)
        else:
            part = row_lse_call([zo, ze], [go, ge])
        row = narrow_lse(part.reshape(-1), c, narrow_count)
        f = epsilon * (log_src - row)
        own_cols, extra_cols = col_lse_call(zo, ze, (f * inv_eps).reshape(-1, 1))
        own_cols = own_cols.reshape(tgt_blocks, BLK)
        extra_cols = jnp.where(mine_live, extra_cols.reshape(-1), sentinel)
        from_left_msg = shifted(jnp.stack([extra_cols, own_cols[want_right % tgt_blocks]]), "wide", 1)
        from_right_msg = shifted(jnp.stack([extra_cols, own_cols[want_left % tgt_blocks]]), "wide", -1)
        part_from_left2 = shifted(extra_cols, "wide", 2)
        part_from_right2 = shifted(extra_cols, "wide", -2)
        part_from_left, cover_from_left = from_left_msg[0], from_left_msg[1]
        part_from_right, cover_from_right = from_right_msg[0], from_right_msg[1]
        ids = jnp.arange(tgt_blocks, dtype=jnp.int32)[:, None]
        add_right = jnp.where(want_right_live & (ids == want_right % tgt_blocks), part_from_right[None, :], sentinel)
        add_left = jnp.where(want_left_live & (ids == want_left % tgt_blocks), part_from_left[None, :], sentinel)
        top = jnp.maximum(own_cols, jnp.maximum(add_right, add_left))
        total = jnp.exp(own_cols - top) + jnp.exp(add_right - top) + jnp.exp(add_left - top)
        g_blocks = epsilon * (log_tgt - (top + jnp.log(total)))
        g_own = g_blocks.reshape(-1)
        cover_e = jnp.where(mine_from_left, cover_from_left, cover_from_right)
        other = jnp.where(mine_from_left, part_from_left2, part_from_right2)
        other_live = jnp.where(mine_from_left, far_left_same, far_right_same)
        other = jnp.where(other_live, other, sentinel)
        first = jnp.where(mine_from_left, extra_cols, other)
        second = jnp.where(mine_from_left, other, extra_cols)
        top_e = jnp.maximum(cover_e, jnp.maximum(first, second))
        total_e = jnp.exp(cover_e - top_e) + jnp.exp(first - top_e) + jnp.exp(second - top_e)
        g_extra = epsilon * (log_tgt - (top_e + jnp.log(total_e)))

    go, ge = scaled(g_own, g_extra)
    row = narrow_lse(row_lse_call([zo, ze], [go, ge]).reshape(-1), c, narrow_count)
    source_pot = epsilon * (log_src - row)
    place = jnp.array([3, 1, 0, 2], jnp.int32)
    pos = place[(jnp.arange(narrow_count, dtype=jnp.int32) - c) % narrow_count]
    numer = map_call(flag, pos, zo, ze, go, ge, row.reshape(-1, 1), targets, from_left, from_right,
                     tm=sources.shape[0] // narrow_count)

    rows = sources.shape[0]
    quarter = rows // narrow_count
    half = quarter // 2
    chunks = numer.reshape(narrow_count, 2, half, feature_count)
    slot_of = {2: 0, 1: 1, -1: 2, 0: 3}

    def chunk(offset, side):
        return chunks[slot_of[offset], side]

    far_a = shifted(chunk(2, 0), "narrow", 1)
    far_b = shifted(chunk(2, 1), "narrow", -1)
    to_right = jnp.stack([chunk(1, 0) + far_a, chunk(1, 1)])
    to_left = jnp.stack([chunk(-1, 0), chunk(-1, 1) + far_b])
    got_left = shifted(to_right, "narrow", 1)
    got_right = shifted(to_left, "narrow", -1)
    mine_sum = jnp.stack([chunk(0, 0), chunk(0, 1)]) + got_left + got_right
    done = mine_sum.astype(jnp.bfloat16).reshape(quarter, feature_count)
    q_left = shifted(done, "narrow", 1)
    q_right = shifted(done, "narrow", -1)
    far_half_a = shifted(q_left[:half], "narrow", 1)
    far_half_b = shifted(q_right[half:], "narrow", -1)
    q_far = jnp.concatenate([far_half_a, far_half_b])
    mapped = jnp.zeros((rows, feature_count), jnp.bfloat16)
    for k, piece in enumerate((done, q_left, q_far, q_right)):
        mapped = lax.dynamic_update_slice_in_dim(mapped, piece, ((c - k) % narrow_count) * quarter, 0)
    return (source_pot, g_own, mapped)


def solution(mesh):
    placed = (P("wide", None), P(("wide", "narrow"), None), P(), P())
    return jax.shard_map(
        shards,
        mesh=mesh,
        in_specs=placed,
        out_specs=(P("wide"), P(("wide", "narrow")), P("wide", None)),
        check_vma=False,
    )
```

```python
import functools
import math

import jax
import jax.numpy as jnp
from jax import lax
from jax.sharding import PartitionSpec as P
from jax.experimental import pallas as pl
from jax.experimental.pallas import tpu as pltpu

BLK = 1024
ITERS = 2


epsilon = 0.25
sentinel = -1e30


def shifted(x, axis, distance):
    size = lax.axis_size(axis)
    route = [(i, (i + distance) % size) for i in range(size)]
    return lax.ppermute(x, axis, route)


def _row_kernel(*refs):
    n = (len(refs) - 1) // 2
    out_ref = refs[-1]
    scores = [refs[k][...] + refs[n + k][...] for k in range(n)]
    top = scores[0].max(axis=1, keepdims=True)
    for s in scores[1:]:
        top = jnp.maximum(top, s.max(axis=1, keepdims=True))
    total = jnp.sum(jnp.exp(scores[0] - top), axis=1, keepdims=True)
    for s in scores[1:]:
        total = total + jnp.sum(jnp.exp(s - top), axis=1, keepdims=True)
    out_ref[...] = top + jnp.log(total)


def row_lse_call(zs, gs, tm=512):
    rows = zs[0].shape[0]
    in_specs = [pl.BlockSpec((tm, z.shape[1]), lambda i: (i, 0)) for z in zs]
    in_specs += [pl.BlockSpec((1, g.shape[1]), lambda i: (0, 0)) for g in gs]
    return pl.pallas_call(
        _row_kernel,
        grid=(rows // tm,),
        in_specs=in_specs,
        out_specs=pl.BlockSpec((tm, 1), lambda i: (i, 0)),
        out_shape=jax.ShapeDtypeStruct((rows, 1), jnp.float32),
    )(*zs, *gs)


def _col_kernel(zo_ref, ze_ref, f_ref, oo_ref, oe_ref):
    f = f_ref[...]
    for z_ref, o_ref in ((zo_ref, oo_ref), (ze_ref, oe_ref)):
        s = z_ref[...] + f
        top = s.max(axis=0, keepdims=True)
        o_ref[...] = top + jnp.log(jnp.sum(jnp.exp(s - top), axis=0, keepdims=True))


def col_lse_call(zo, ze, f, steps=2):
    rows = zo.shape[0]
    wo = zo.shape[1] // steps
    we = ze.shape[1] // steps
    return pl.pallas_call(
        _col_kernel,
        grid=(steps,),
        in_specs=[
            pl.BlockSpec((rows, wo), lambda j: (0, j)),
            pl.BlockSpec((rows, we), lambda j: (0, j)),
            pl.BlockSpec((rows, 1), lambda j: (0, 0)),
        ],
        out_specs=[
            pl.BlockSpec((1, wo), lambda j: (0, j)),
            pl.BlockSpec((1, we), lambda j: (0, j)),
        ],
        out_shape=[
            jax.ShapeDtypeStruct((1, zo.shape[1]), jnp.float32),
            jax.ShapeDtypeStruct((1, ze.shape[1]), jnp.float32),
        ],
    )(zo, ze, f)


def _ext_kernel(flag_ref, s_ref, l_ref, r_ref, ge_ref, own_ref, ze_ref, part_ref, *, scale):
    def product(e_ref):
        ze_ref[...] = lax.dot_general(
            s_ref[...], e_ref[...], (((1,), (1,)), ((), ())), preferred_element_type=jnp.float32
        ) * scale

    @pl.when(flag_ref[0] == 1)
    def _():
        product(l_ref)

    @pl.when(flag_ref[0] != 1)
    def _():
        product(r_ref)

    s = ze_ref[...] + ge_ref[...]
    own = own_ref[...]
    top = jnp.maximum(s.max(axis=1, keepdims=True), own)
    part_ref[...] = top + jnp.log(jnp.sum(jnp.exp(s - top), axis=1, keepdims=True) + jnp.exp(own - top))


def ext_call(flag, sources, from_left, from_right, ge, own_part, scale, tm=512):
    rows, feats = sources.shape
    width = from_left.shape[0]
    grid_spec = pltpu.PrefetchScalarGridSpec(
        num_scalar_prefetch=1,
        grid=(rows // tm,),
        in_specs=[
            pl.BlockSpec((tm, feats), lambda i, f: (i, 0)),
            pl.BlockSpec(from_left.shape, lambda i, f: (0, 0)),
            pl.BlockSpec(from_right.shape, lambda i, f: (0, 0)),
            pl.BlockSpec((1, width), lambda i, f: (0, 0)),
            pl.BlockSpec((tm, 1), lambda i, f: (i, 0)),
        ],
        out_specs=[
            pl.BlockSpec((tm, width), lambda i, f: (i, 0)),
            pl.BlockSpec((tm, 1), lambda i, f: (i, 0)),
        ],
    )
    return pl.pallas_call(
        functools.partial(_ext_kernel, scale=scale),
        grid_spec=grid_spec,
        out_shape=[
            jax.ShapeDtypeStruct((rows, width), jnp.float32),
            jax.ShapeDtypeStruct((rows, 1), jnp.float32),
        ],
    )(flag, sources, from_left, from_right, ge, own_part)


def _map_kernel(flag_ref, pos_ref, zo_ref, ze_ref, go_ref, ge_ref, l_ref, to_ref, tl_ref, tr_ref, out_ref):
    lse = l_ref[...]
    wo = jnp.exp(zo_ref[...] + go_ref[...] - lse).astype(jnp.bfloat16)
    we = jnp.exp(ze_ref[...] + ge_ref[...] - lse).astype(jnp.bfloat16)
    out_ref[...] = jnp.dot(wo, to_ref[...], preferred_element_type=jnp.float32)

    @pl.when(flag_ref[0] == 1)
    def _():
        out_ref[...] += jnp.dot(we, tl_ref[...], preferred_element_type=jnp.float32)

    @pl.when(flag_ref[0] != 1)
    def _():
        out_ref[...] += jnp.dot(we, tr_ref[...], preferred_element_type=jnp.float32)


def map_call(flag, pos, zo, ze, go, ge, lse, to, tl, tr, tm=256):
    rows = zo.shape[0]
    feats = to.shape[1]
    grid_spec = pltpu.PrefetchScalarGridSpec(
        num_scalar_prefetch=2,
        grid=(rows // tm,),
        in_specs=[
            pl.BlockSpec((tm, zo.shape[1]), lambda i, f, p: (i, 0)),
            pl.BlockSpec((tm, ze.shape[1]), lambda i, f, p: (i, 0)),
            pl.BlockSpec((1, go.shape[1]), lambda i, f, p: (0, 0)),
            pl.BlockSpec((1, ge.shape[1]), lambda i, f, p: (0, 0)),
            pl.BlockSpec((tm, 1), lambda i, f, p: (i, 0)),
            pl.BlockSpec(to.shape, lambda i, f, p: (0, 0)),
            pl.BlockSpec(tl.shape, lambda i, f, p: (0, 0)),
            pl.BlockSpec(tr.shape, lambda i, f, p: (0, 0)),
        ],
        out_specs=pl.BlockSpec((tm, feats), lambda i, f, p: (p[i], 0)),
    )
    return pl.pallas_call(
        _map_kernel,
        grid_spec=grid_spec,
        out_shape=jax.ShapeDtypeStruct((rows, feats), jnp.float32),
    )(flag, pos, zo, ze, go, ge, lse, to, tl, tr)


def narrow_lse(partial_value, column, narrow_count):
    pieces = [partial_value] + [shifted(partial_value, "narrow", k) for k in range(1, narrow_count)]
    stacked = jnp.stack(pieces)
    order = (column - jnp.arange(narrow_count, dtype=jnp.int32)) % narrow_count
    ordered = stacked[order]
    top = jnp.max(ordered, axis=0)
    return top + jnp.log(jnp.sum(jnp.exp(ordered - top[None, :]), axis=0))


def shards(sources, targets, pair_target, pair_count):
    feature_count = sources.shape[1]
    tgt_blocks = targets.shape[0] // BLK
    wide_count = lax.axis_size("wide")
    narrow_count = lax.axis_size("narrow")
    w = lax.axis_index("wide")
    c = lax.axis_index("narrow")
    group_blocks = tgt_blocks * narrow_count
    scale = (1.0 / math.sqrt(feature_count)) * (1.0 / epsilon)
    inv_eps = 1.0 / epsilon
    log_src = -math.log(wide_count * sources.shape[0])
    log_tgt = -math.log(wide_count * narrow_count * targets.shape[0])

    left = (w - 1 + wide_count) % wide_count
    right = (w + 1) % wide_count
    slot = group_blocks + c

    mine = pair_target[w, slot]
    mine_live = pair_count[w] > slot
    mine_from_left = (mine // group_blocks) == left

    want_right = pair_target[right, slot]
    want_right_live = (pair_count[right] > slot) & ((want_right // group_blocks) == w)
    want_left = pair_target[left, slot]
    want_left_live = (pair_count[left] > slot) & ((want_left // group_blocks) == w)
    left2 = (w - 2 + 2 * wide_count) % wide_count
    right2 = (w + 2) % wide_count
    far_left_same = (pair_count[left2] > slot) & (pair_target[left2, slot] == mine)
    far_right_same = (pair_count[right2] > slot) & (pair_target[right2, slot] == mine)

    blocks = targets.reshape(tgt_blocks, BLK, feature_count)
    to_right = blocks[want_right % tgt_blocks]
    to_left = blocks[want_left % tgt_blocks]
    cut = BLK // 2
    from_left = jnp.concatenate([shifted(to_right[:cut], "wide", 1), shifted(to_right[cut:], "wide", 1)])
    from_right = jnp.concatenate([shifted(to_left[:cut], "wide", -1), shifted(to_left[cut:], "wide", -1)])

    zo = lax.dot_general(
        sources, targets, (((1,), (1,)), ((), ())), preferred_element_type=jnp.float32
    ) * scale
    extra_mask = jnp.where(mine_live, 0.0, sentinel).astype(jnp.float32)
    flag = mine_from_left.astype(jnp.int32).reshape(1)
    own_width = tgt_blocks * BLK

    def scaled(g_own, g_extra):
        return ((g_own * inv_eps).reshape(1, own_width), (g_extra * inv_eps + extra_mask).reshape(1, BLK))

    g_own = jnp.zeros((own_width,), jnp.float32)
    g_extra = jnp.zeros((BLK,), jnp.float32)
    for iteration in range(ITERS):
        go, ge = scaled(g_own, g_extra)
        if iteration == 0:
            ze, part = ext_call(flag, sources, from_left, from_right, ge, row_lse_call([zo], [go]), scale)
        else:
            part = row_lse_call([zo, ze], [go, ge])
        row = narrow_lse(part.reshape(-1), c, narrow_count)
        f = epsilon * (log_src - row)
        own_cols, extra_cols = col_lse_call(zo, ze, (f * inv_eps).reshape(-1, 1))
        own_cols = own_cols.reshape(tgt_blocks, BLK)
        extra_cols = jnp.where(mine_live, extra_cols.reshape(-1), sentinel)
        from_left_msg = shifted(jnp.stack([extra_cols, own_cols[want_right % tgt_blocks]]), "wide", 1)
        from_right_msg = shifted(jnp.stack([extra_cols, own_cols[want_left % tgt_blocks]]), "wide", -1)
        part_from_left2 = shifted(extra_cols, "wide", 2)
        part_from_right2 = shifted(extra_cols, "wide", -2)
        part_from_left, cover_from_left = from_left_msg[0], from_left_msg[1]
        part_from_right, cover_from_right = from_right_msg[0], from_right_msg[1]
        ids = jnp.arange(tgt_blocks, dtype=jnp.int32)[:, None]
        add_right = jnp.where(want_right_live & (ids == want_right % tgt_blocks), part_from_right[None, :], sentinel)
        add_left = jnp.where(want_left_live & (ids == want_left % tgt_blocks), part_from_left[None, :], sentinel)
        top = jnp.maximum(own_cols, jnp.maximum(add_right, add_left))
        total = jnp.exp(own_cols - top) + jnp.exp(add_right - top) + jnp.exp(add_left - top)
        g_blocks = epsilon * (log_tgt - (top + jnp.log(total)))
        g_own = g_blocks.reshape(-1)
        cover_e = jnp.where(mine_from_left, cover_from_left, cover_from_right)
        other = jnp.where(mine_from_left, part_from_left2, part_from_right2)
        other_live = jnp.where(mine_from_left, far_left_same, far_right_same)
        other = jnp.where(other_live, other, sentinel)
        first = jnp.where(mine_from_left, extra_cols, other)
        second = jnp.where(mine_from_left, other, extra_cols)
        top_e = jnp.maximum(cover_e, jnp.maximum(first, second))
        total_e = jnp.exp(cover_e - top_e) + jnp.exp(first - top_e) + jnp.exp(second - top_e)
        g_extra = epsilon * (log_tgt - (top_e + jnp.log(total_e)))

    go, ge = scaled(g_own, g_extra)
    row = narrow_lse(row_lse_call([zo, ze], [go, ge]).reshape(-1), c, narrow_count)
    source_pot = epsilon * (log_src - row)
    place = jnp.array([3, 1, 0, 2], jnp.int32)
    pos = place[(jnp.arange(narrow_count, dtype=jnp.int32) - c) % narrow_count]
    numer = map_call(flag, pos, zo, ze, go, ge, row.reshape(-1, 1), targets, from_left, from_right,
                     tm=sources.shape[0] // narrow_count)

    rows = sources.shape[0]
    quarter = rows // narrow_count
    half = quarter // 2
    chunks = numer.reshape(narrow_count, 2, half, feature_count)
    slot_of = {2: 0, 1: 1, -1: 2, 0: 3}

    def chunk(offset, side):
        return chunks[slot_of[offset], side]

    far_a = shifted(chunk(2, 0), "narrow", 1)
    far_b = shifted(chunk(2, 1), "narrow", -1)
    to_right = jnp.stack([chunk(1, 0) + far_a, chunk(1, 1)])
    to_left = jnp.stack([chunk(-1, 0), chunk(-1, 1) + far_b])
    got_left = shifted(to_right, "narrow", 1)
    got_right = shifted(to_left, "narrow", -1)
    mine_sum = jnp.stack([chunk(0, 0), chunk(0, 1)]) + got_left + got_right
    done = mine_sum.astype(jnp.bfloat16).reshape(quarter, feature_count)
    q_left = shifted(done, "narrow", 1)
    q_right = shifted(done, "narrow", -1)
    far_half_a = shifted(q_left[:half], "narrow", 1)
    far_half_b = shifted(q_right[half:], "narrow", -1)
    q_far = jnp.concatenate([far_half_a, far_half_b])
    mapped = jnp.zeros((rows, feature_count), jnp.bfloat16)
    for k, piece in enumerate((done, q_left, q_far, q_right)):
        mapped = lax.dynamic_update_slice_in_dim(mapped, piece, ((c - k) % narrow_count) * quarter, 0)
    return (source_pot, g_own, mapped)


def solution(mesh):
    placed = (P("wide", None), P(("wide", "narrow"), None), P(), P())
    return jax.shard_map(
        shards,
        mesh=mesh,
        in_specs=placed,
        out_specs=(P("wide"), P(("wide", "narrow")), P("wide", None)),
        check_vma=False,
    )
```

```python
import functools
import math

import jax
import jax.numpy as jnp
from jax import lax
from jax.sharding import PartitionSpec as P
from jax.experimental import pallas as pl
from jax.experimental.pallas import tpu as pltpu

BLK = 1024
ITERS = 2


epsilon = 0.25
sentinel = -1e30


def shifted(x, axis, distance):
    size = lax.axis_size(axis)
    route = [(i, (i + distance) % size) for i in range(size)]
    return lax.ppermute(x, axis, route)


def _row_kernel(*refs):
    n = (len(refs) - 1) // 2
    out_ref = refs[-1]
    scores = [refs[k][...] + refs[n + k][...] for k in range(n)]
    top = scores[0].max(axis=1, keepdims=True)
    for s in scores[1:]:
        top = jnp.maximum(top, s.max(axis=1, keepdims=True))
    total = jnp.sum(jnp.exp(scores[0] - top), axis=1, keepdims=True)
    for s in scores[1:]:
        total = total + jnp.sum(jnp.exp(s - top), axis=1, keepdims=True)
    out_ref[...] = top + jnp.log(total)


def row_lse_call(zs, gs, tm=512):
    rows = zs[0].shape[0]
    in_specs = [pl.BlockSpec((tm, z.shape[1]), lambda i: (i, 0)) for z in zs]
    in_specs += [pl.BlockSpec((1, g.shape[1]), lambda i: (0, 0)) for g in gs]
    return pl.pallas_call(
        _row_kernel,
        grid=(rows // tm,),
        in_specs=in_specs,
        out_specs=pl.BlockSpec((tm, 1), lambda i: (i, 0)),
        out_shape=jax.ShapeDtypeStruct((rows, 1), jnp.float32),
    )(*zs, *gs)


def _col_kernel(zo_ref, ze_ref, f_ref, oo_ref, oe_ref):
    f = f_ref[...]
    for z_ref, o_ref in ((zo_ref, oo_ref), (ze_ref, oe_ref)):
        s = z_ref[...] + f
        top = s.max(axis=0, keepdims=True)
        o_ref[...] = top + jnp.log(jnp.sum(jnp.exp(s - top), axis=0, keepdims=True))


def col_lse_call(zo, ze, f, steps=2):
    rows = zo.shape[0]
    wo = zo.shape[1] // steps
    we = ze.shape[1] // steps
    return pl.pallas_call(
        _col_kernel,
        grid=(steps,),
        in_specs=[
            pl.BlockSpec((rows, wo), lambda j: (0, j)),
            pl.BlockSpec((rows, we), lambda j: (0, j)),
            pl.BlockSpec((rows, 1), lambda j: (0, 0)),
        ],
        out_specs=[
            pl.BlockSpec((1, wo), lambda j: (0, j)),
            pl.BlockSpec((1, we), lambda j: (0, j)),
        ],
        out_shape=[
            jax.ShapeDtypeStruct((1, zo.shape[1]), jnp.float32),
            jax.ShapeDtypeStruct((1, ze.shape[1]), jnp.float32),
        ],
    )(zo, ze, f)


def _ext_kernel(flag_ref, s_ref, l_ref, r_ref, ge_ref, own_ref, ze_ref, part_ref, *, scale):
    def product(e_ref):
        ze_ref[...] = lax.dot_general(
            s_ref[...], e_ref[...], (((1,), (1,)), ((), ())), preferred_element_type=jnp.float32
        ) * scale

    @pl.when(flag_ref[0] == 1)
    def _():
        product(l_ref)

    @pl.when(flag_ref[0] != 1)
    def _():
        product(r_ref)

    s = ze_ref[...] + ge_ref[...]
    own = own_ref[...]
    top = jnp.maximum(s.max(axis=1, keepdims=True), own)
    part_ref[...] = top + jnp.log(jnp.sum(jnp.exp(s - top), axis=1, keepdims=True) + jnp.exp(own - top))


def ext_call(flag, sources, from_left, from_right, ge, own_part, scale, tm=512):
    rows, feats = sources.shape
    width = from_left.shape[0]
    grid_spec = pltpu.PrefetchScalarGridSpec(
        num_scalar_prefetch=1,
        grid=(rows // tm,),
        in_specs=[
            pl.BlockSpec((tm, feats), lambda i, f: (i, 0)),
            pl.BlockSpec(from_left.shape, lambda i, f: (0, 0)),
            pl.BlockSpec(from_right.shape, lambda i, f: (0, 0)),
            pl.BlockSpec((1, width), lambda i, f: (0, 0)),
            pl.BlockSpec((tm, 1), lambda i, f: (i, 0)),
        ],
        out_specs=[
            pl.BlockSpec((tm, width), lambda i, f: (i, 0)),
            pl.BlockSpec((tm, 1), lambda i, f: (i, 0)),
        ],
    )
    return pl.pallas_call(
        functools.partial(_ext_kernel, scale=scale),
        grid_spec=grid_spec,
        out_shape=[
            jax.ShapeDtypeStruct((rows, width), jnp.float32),
            jax.ShapeDtypeStruct((rows, 1), jnp.float32),
        ],
    )(flag, sources, from_left, from_right, ge, own_part)


def _map_kernel(flag_ref, pos_ref, zo_ref, ze_ref, go_ref, ge_ref, l_ref, to_ref, tl_ref, tr_ref, out_ref):
    lse = l_ref[...]
    wo = jnp.exp(zo_ref[...] + go_ref[...] - lse).astype(jnp.bfloat16)
    we = jnp.exp(ze_ref[...] + ge_ref[...] - lse).astype(jnp.bfloat16)
    out_ref[...] = jnp.dot(wo, to_ref[...], preferred_element_type=jnp.float32)

    @pl.when(flag_ref[0] == 1)
    def _():
        out_ref[...] += jnp.dot(we, tl_ref[...], preferred_element_type=jnp.float32)

    @pl.when(flag_ref[0] != 1)
    def _():
        out_ref[...] += jnp.dot(we, tr_ref[...], preferred_element_type=jnp.float32)


def map_call(flag, pos, zo, ze, go, ge, lse, to, tl, tr, tm=256):
    rows = zo.shape[0]
    feats = to.shape[1]
    grid_spec = pltpu.PrefetchScalarGridSpec(
        num_scalar_prefetch=2,
        grid=(rows // tm,),
        in_specs=[
            pl.BlockSpec((tm, zo.shape[1]), lambda i, f, p: (i, 0)),
            pl.BlockSpec((tm, ze.shape[1]), lambda i, f, p: (i, 0)),
            pl.BlockSpec((1, go.shape[1]), lambda i, f, p: (0, 0)),
            pl.BlockSpec((1, ge.shape[1]), lambda i, f, p: (0, 0)),
            pl.BlockSpec((tm, 1), lambda i, f, p: (i, 0)),
            pl.BlockSpec(to.shape, lambda i, f, p: (0, 0)),
            pl.BlockSpec(tl.shape, lambda i, f, p: (0, 0)),
            pl.BlockSpec(tr.shape, lambda i, f, p: (0, 0)),
        ],
        out_specs=pl.BlockSpec((tm, feats), lambda i, f, p: (p[i], 0)),
    )
    return pl.pallas_call(
        _map_kernel,
        grid_spec=grid_spec,
        out_shape=jax.ShapeDtypeStruct((rows, feats), jnp.float32),
    )(flag, pos, zo, ze, go, ge, lse, to, tl, tr)


def narrow_lse(partial_value, column, narrow_count):
    pieces = [partial_value] + [shifted(partial_value, "narrow", k) for k in range(1, narrow_count)]
    stacked = jnp.stack(pieces)
    order = (column - jnp.arange(narrow_count, dtype=jnp.int32)) % narrow_count
    ordered = stacked[order]
    top = jnp.max(ordered, axis=0)
    return top + jnp.log(jnp.sum(jnp.exp(ordered - top[None, :]), axis=0))


def shards(sources, targets, pair_target, pair_count):
    feature_count = sources.shape[1]
    tgt_blocks = targets.shape[0] // BLK
    wide_count = lax.axis_size("wide")
    narrow_count = lax.axis_size("narrow")
    w = lax.axis_index("wide")
    c = lax.axis_index("narrow")
    group_blocks = tgt_blocks * narrow_count
    scale = (1.0 / math.sqrt(feature_count)) * (1.0 / epsilon)
    inv_eps = 1.0 / epsilon
    log_src = -math.log(wide_count * sources.shape[0])
    log_tgt = -math.log(wide_count * narrow_count * targets.shape[0])

    left = (w - 1 + wide_count) % wide_count
    right = (w + 1) % wide_count
    slot = group_blocks + c

    mine = pair_target[w, slot]
    mine_live = pair_count[w] > slot
    mine_from_left = (mine // group_blocks) == left

    want_right = pair_target[right, slot]
    want_right_live = (pair_count[right] > slot) & ((want_right // group_blocks) == w)
    want_left = pair_target[left, slot]
    want_left_live = (pair_count[left] > slot) & ((want_left // group_blocks) == w)
    left2 = (w - 2 + 2 * wide_count) % wide_count
    right2 = (w + 2) % wide_count
    far_left_same = (pair_count[left2] > slot) & (pair_target[left2, slot] == mine)
    far_right_same = (pair_count[right2] > slot) & (pair_target[right2, slot] == mine)

    blocks = targets.reshape(tgt_blocks, BLK, feature_count)
    to_right = blocks[want_right % tgt_blocks]
    to_left = blocks[want_left % tgt_blocks]
    from_left = shifted(to_right, "wide", 1)
    from_right = shifted(to_left, "wide", -1)

    zo = lax.dot_general(
        sources, targets, (((1,), (1,)), ((), ())), preferred_element_type=jnp.float32
    ) * scale
    extra_mask = jnp.where(mine_live, 0.0, sentinel).astype(jnp.float32)
    flag = mine_from_left.astype(jnp.int32).reshape(1)
    own_width = tgt_blocks * BLK

    def scaled(g_own, g_extra):
        return (g_own * inv_eps, g_extra * inv_eps + extra_mask)

    g_own = jnp.zeros((1, own_width), jnp.float32)
    g_extra = jnp.zeros((1, BLK), jnp.float32)
    lane_block = (jnp.arange(own_width, dtype=jnp.int32) // BLK)[None, :]

    def own_block(row_value, index):
        return lax.dynamic_slice_in_dim(row_value, index * BLK, BLK, 1)
    for iteration in range(ITERS):
        go, ge = scaled(g_own, g_extra)
        if iteration == 0:
            ze, part = ext_call(flag, sources, from_left, from_right, ge, row_lse_call([zo], [go]), scale)
        else:
            part = row_lse_call([zo, ze], [go, ge])
        row = narrow_lse(part.reshape(-1), c, narrow_count)
        f = epsilon * (log_src - row)
        own_cols, extra_cols = col_lse_call(zo, ze, (f * inv_eps).reshape(-1, 1))
        extra_cols = jnp.where(mine_live, extra_cols, sentinel)
        from_left_msg = shifted(
            jnp.concatenate([extra_cols, own_block(own_cols, want_right % tgt_blocks)]), "wide", 1)
        from_right_msg = shifted(
            jnp.concatenate([extra_cols, own_block(own_cols, want_left % tgt_blocks)]), "wide", -1)
        part_from_left2 = shifted(extra_cols, "wide", 2)
        part_from_right2 = shifted(extra_cols, "wide", -2)
        part_from_left, cover_from_left = from_left_msg[0:1], from_left_msg[1:2]
        part_from_right, cover_from_right = from_right_msg[0:1], from_right_msg[1:2]
        add_right = jnp.where(want_right_live & (lane_block == want_right % tgt_blocks),
                              jnp.tile(part_from_right, (1, tgt_blocks)), sentinel)
        add_left = jnp.where(want_left_live & (lane_block == want_left % tgt_blocks),
                             jnp.tile(part_from_left, (1, tgt_blocks)), sentinel)
        top = jnp.maximum(own_cols, jnp.maximum(add_right, add_left))
        total = jnp.exp(own_cols - top) + jnp.exp(add_right - top) + jnp.exp(add_left - top)
        g_own = epsilon * (log_tgt - (top + jnp.log(total)))
        cover_e = jnp.where(mine_from_left, cover_from_left, cover_from_right)
        other = jnp.where(mine_from_left, part_from_left2, part_from_right2)
        other_live = jnp.where(mine_from_left, far_left_same, far_right_same)
        other = jnp.where(other_live, other, sentinel)
        first = jnp.where(mine_from_left, extra_cols, other)
        second = jnp.where(mine_from_left, other, extra_cols)
        top_e = jnp.maximum(cover_e, jnp.maximum(first, second))
        total_e = jnp.exp(cover_e - top_e) + jnp.exp(first - top_e) + jnp.exp(second - top_e)
        g_extra = epsilon * (log_tgt - (top_e + jnp.log(total_e)))

    go, ge = scaled(g_own, g_extra)
    row = narrow_lse(row_lse_call([zo, ze], [go, ge]).reshape(-1), c, narrow_count)
    source_pot = epsilon * (log_src - row)
    place = jnp.array([3, 1, 0, 2], jnp.int32)
    pos = place[(jnp.arange(narrow_count, dtype=jnp.int32) - c) % narrow_count]
    numer = map_call(flag, pos, zo, ze, go, ge, row.reshape(-1, 1), targets, from_left, from_right,
                     tm=sources.shape[0] // narrow_count)

    rows = sources.shape[0]
    quarter = rows // narrow_count
    half = quarter // 2
    chunks = numer.reshape(narrow_count, 2, half, feature_count)
    slot_of = {2: 0, 1: 1, -1: 2, 0: 3}

    def chunk(offset, side):
        return chunks[slot_of[offset], side]

    far_a = shifted(chunk(2, 0), "narrow", 1)
    far_b = shifted(chunk(2, 1), "narrow", -1)
    to_right = jnp.stack([chunk(1, 0) + far_a, chunk(1, 1)])
    to_left = jnp.stack([chunk(-1, 0), chunk(-1, 1) + far_b])
    got_left = shifted(to_right, "narrow", 1)
    got_right = shifted(to_left, "narrow", -1)
    mine_sum = jnp.stack([chunk(0, 0), chunk(0, 1)]) + got_left + got_right
    done = mine_sum.astype(jnp.bfloat16).reshape(quarter, feature_count)
    q_left = shifted(done, "narrow", 1)
    q_right = shifted(done, "narrow", -1)
    far_half_a = shifted(q_left[:half], "narrow", 1)
    far_half_b = shifted(q_right[half:], "narrow", -1)
    q_far = jnp.concatenate([far_half_a, far_half_b])
    mapped = jnp.zeros((rows, feature_count), jnp.bfloat16)
    for k, piece in enumerate((done, q_left, q_far, q_right)):
        mapped = lax.dynamic_update_slice_in_dim(mapped, piece, ((c - k) % narrow_count) * quarter, 0)
    return (source_pot, g_own.reshape(-1), mapped)


def solution(mesh):
    placed = (P("wide", None), P(("wide", "narrow"), None), P(), P())
    return jax.shard_map(
        shards,
        mesh=mesh,
        in_specs=placed,
        out_specs=(P("wide"), P(("wide", "narrow")), P("wide", None)),
        check_vma=False,
    )
```

```python
import functools
import math

import jax
import jax.numpy as jnp
from jax import lax
from jax.sharding import PartitionSpec as P
from jax.experimental import pallas as pl
from jax.experimental.pallas import tpu as pltpu

BLK = 1024
ITERS = 2


epsilon = 0.25
sentinel = -1e30


def shifted(x, axis, distance):
    size = lax.axis_size(axis)
    route = [(i, (i + distance) % size) for i in range(size)]
    return lax.ppermute(x, axis, route)


def _row_kernel(*refs):
    n = (len(refs) - 1) // 2
    out_ref = refs[-1]
    scores = [refs[k][...] + refs[n + k][...] for k in range(n)]
    top = scores[0].max(axis=1, keepdims=True)
    for s in scores[1:]:
        top = jnp.maximum(top, s.max(axis=1, keepdims=True))
    total = jnp.sum(jnp.exp(scores[0] - top), axis=1, keepdims=True)
    for s in scores[1:]:
        total = total + jnp.sum(jnp.exp(s - top), axis=1, keepdims=True)
    out_ref[...] = top + jnp.log(total)


def row_lse_call(zs, gs, tm=1024):
    rows = zs[0].shape[0]
    in_specs = [pl.BlockSpec((tm, z.shape[1]), lambda i: (i, 0)) for z in zs]
    in_specs += [pl.BlockSpec((1, g.shape[1]), lambda i: (0, 0)) for g in gs]
    return pl.pallas_call(
        _row_kernel,
        grid=(rows // tm,),
        in_specs=in_specs,
        out_specs=pl.BlockSpec((tm, 1), lambda i: (i, 0)),
        out_shape=jax.ShapeDtypeStruct((rows, 1), jnp.float32),
    )(*zs, *gs)


def _col_kernel(zo_ref, ze_ref, f_ref, oo_ref, oe_ref):
    f = f_ref[...]
    for z_ref, o_ref in ((zo_ref, oo_ref), (ze_ref, oe_ref)):
        s = z_ref[...] + f
        top = s.max(axis=0, keepdims=True)
        o_ref[...] = top + jnp.log(jnp.sum(jnp.exp(s - top), axis=0, keepdims=True))


def col_lse_call(zo, ze, f, steps=1):
    rows = zo.shape[0]
    wo = zo.shape[1] // steps
    we = ze.shape[1] // steps
    return pl.pallas_call(
        _col_kernel,
        grid=(steps,),
        in_specs=[
            pl.BlockSpec((rows, wo), lambda j: (0, j)),
            pl.BlockSpec((rows, we), lambda j: (0, j)),
            pl.BlockSpec((rows, 1), lambda j: (0, 0)),
        ],
        out_specs=[
            pl.BlockSpec((1, wo), lambda j: (0, j)),
            pl.BlockSpec((1, we), lambda j: (0, j)),
        ],
        out_shape=[
            jax.ShapeDtypeStruct((1, zo.shape[1]), jnp.float32),
            jax.ShapeDtypeStruct((1, ze.shape[1]), jnp.float32),
        ],
    )(zo, ze, f)


def _ext_kernel(flag_ref, s_ref, l_ref, r_ref, ge_ref, own_ref, ze_ref, part_ref, *, scale):
    def product(e_ref):
        ze_ref[...] = lax.dot_general(
            s_ref[...], e_ref[...], (((1,), (1,)), ((), ())), preferred_element_type=jnp.float32
        ) * scale

    @pl.when(flag_ref[0] == 1)
    def _():
        product(l_ref)

    @pl.when(flag_ref[0] != 1)
    def _():
        product(r_ref)

    s = ze_ref[...] + ge_ref[...]
    own = own_ref[...]
    top = jnp.maximum(s.max(axis=1, keepdims=True), own)
    part_ref[...] = top + jnp.log(jnp.sum(jnp.exp(s - top), axis=1, keepdims=True) + jnp.exp(own - top))


def ext_call(flag, sources, from_left, from_right, ge, own_part, scale, tm=512):
    rows, feats = sources.shape
    width = from_left.shape[0]
    grid_spec = pltpu.PrefetchScalarGridSpec(
        num_scalar_prefetch=1,
        grid=(rows // tm,),
        in_specs=[
            pl.BlockSpec((tm, feats), lambda i, f: (i, 0)),
            pl.BlockSpec(from_left.shape, lambda i, f: (0, 0)),
            pl.BlockSpec(from_right.shape, lambda i, f: (0, 0)),
            pl.BlockSpec((1, width), lambda i, f: (0, 0)),
            pl.BlockSpec((tm, 1), lambda i, f: (i, 0)),
        ],
        out_specs=[
            pl.BlockSpec((tm, width), lambda i, f: (i, 0)),
            pl.BlockSpec((tm, 1), lambda i, f: (i, 0)),
        ],
    )
    return pl.pallas_call(
        functools.partial(_ext_kernel, scale=scale),
        grid_spec=grid_spec,
        out_shape=[
            jax.ShapeDtypeStruct((rows, width), jnp.float32),
            jax.ShapeDtypeStruct((rows, 1), jnp.float32),
        ],
    )(flag, sources, from_left, from_right, ge, own_part)


def _map_kernel(flag_ref, pos_ref, zo_ref, ze_ref, go_ref, ge_ref, l_ref, to_ref, tl_ref, tr_ref, out_ref):
    lse = l_ref[...]
    wo = jnp.exp(zo_ref[...] + go_ref[...] - lse).astype(jnp.bfloat16)
    we = jnp.exp(ze_ref[...] + ge_ref[...] - lse).astype(jnp.bfloat16)
    out_ref[...] = jnp.dot(wo, to_ref[...], preferred_element_type=jnp.float32)

    @pl.when(flag_ref[0] == 1)
    def _():
        out_ref[...] += jnp.dot(we, tl_ref[...], preferred_element_type=jnp.float32)

    @pl.when(flag_ref[0] != 1)
    def _():
        out_ref[...] += jnp.dot(we, tr_ref[...], preferred_element_type=jnp.float32)


def map_call(flag, pos, zo, ze, go, ge, lse, to, tl, tr, tm=256):
    rows = zo.shape[0]
    feats = to.shape[1]
    grid_spec = pltpu.PrefetchScalarGridSpec(
        num_scalar_prefetch=2,
        grid=(rows // tm,),
        in_specs=[
            pl.BlockSpec((tm, zo.shape[1]), lambda i, f, p: (i, 0)),
            pl.BlockSpec((tm, ze.shape[1]), lambda i, f, p: (i, 0)),
            pl.BlockSpec((1, go.shape[1]), lambda i, f, p: (0, 0)),
            pl.BlockSpec((1, ge.shape[1]), lambda i, f, p: (0, 0)),
            pl.BlockSpec((tm, 1), lambda i, f, p: (i, 0)),
            pl.BlockSpec(to.shape, lambda i, f, p: (0, 0)),
            pl.BlockSpec(tl.shape, lambda i, f, p: (0, 0)),
            pl.BlockSpec(tr.shape, lambda i, f, p: (0, 0)),
        ],
        out_specs=pl.BlockSpec((tm, feats), lambda i, f, p: (p[i], 0)),
    )
    return pl.pallas_call(
        _map_kernel,
        grid_spec=grid_spec,
        out_shape=jax.ShapeDtypeStruct((rows, feats), jnp.float32),
    )(flag, pos, zo, ze, go, ge, lse, to, tl, tr)


def narrow_lse(partial_value, column, narrow_count):
    pieces = [partial_value] + [shifted(partial_value, "narrow", k) for k in range(1, narrow_count)]
    stacked = jnp.stack(pieces)
    order = (column - jnp.arange(narrow_count, dtype=jnp.int32)) % narrow_count
    ordered = stacked[order]
    top = jnp.max(ordered, axis=0)
    return top + jnp.log(jnp.sum(jnp.exp(ordered - top[None, :]), axis=0))


def shards(sources, targets, pair_target, pair_count):
    feature_count = sources.shape[1]
    tgt_blocks = targets.shape[0] // BLK
    wide_count = lax.axis_size("wide")
    narrow_count = lax.axis_size("narrow")
    w = lax.axis_index("wide")
    c = lax.axis_index("narrow")
    group_blocks = tgt_blocks * narrow_count
    scale = (1.0 / math.sqrt(feature_count)) * (1.0 / epsilon)
    inv_eps = 1.0 / epsilon
    log_src = -math.log(wide_count * sources.shape[0])
    log_tgt = -math.log(wide_count * narrow_count * targets.shape[0])

    left = (w - 1 + wide_count) % wide_count
    right = (w + 1) % wide_count
    slot = group_blocks + c

    mine = pair_target[w, slot]
    mine_live = pair_count[w] > slot
    mine_from_left = (mine // group_blocks) == left

    want_right = pair_target[right, slot]
    want_right_live = (pair_count[right] > slot) & ((want_right // group_blocks) == w)
    want_left = pair_target[left, slot]
    want_left_live = (pair_count[left] > slot) & ((want_left // group_blocks) == w)
    left2 = (w - 2 + 2 * wide_count) % wide_count
    right2 = (w + 2) % wide_count
    far_left_same = (pair_count[left2] > slot) & (pair_target[left2, slot] == mine)
    far_right_same = (pair_count[right2] > slot) & (pair_target[right2, slot] == mine)

    blocks = targets.reshape(tgt_blocks, BLK, feature_count)
    to_right = blocks[want_right % tgt_blocks]
    to_left = blocks[want_left % tgt_blocks]
    from_left = shifted(to_right, "wide", 1)
    from_right = shifted(to_left, "wide", -1)

    zo = lax.dot_general(
        sources, targets, (((1,), (1,)), ((), ())), preferred_element_type=jnp.float32
    ) * scale
    extra_mask = jnp.where(mine_live, 0.0, sentinel).astype(jnp.float32)
    flag = mine_from_left.astype(jnp.int32).reshape(1)
    own_width = tgt_blocks * BLK

    def scaled(g_own, g_extra):
        return ((g_own * inv_eps).reshape(1, own_width), (g_extra * inv_eps + extra_mask).reshape(1, BLK))

    g_own = jnp.zeros((own_width,), jnp.float32)
    g_extra = jnp.zeros((BLK,), jnp.float32)
    for iteration in range(ITERS):
        go, ge = scaled(g_own, g_extra)
        if iteration == 0:
            ze, part = ext_call(flag, sources, from_left, from_right, ge, row_lse_call([zo], [go]), scale)
        else:
            part = row_lse_call([zo, ze], [go, ge])
        row = narrow_lse(part.reshape(-1), c, narrow_count)
        f = epsilon * (log_src - row)
        own_cols, extra_cols = col_lse_call(zo, ze, (f * inv_eps).reshape(-1, 1))
        own_cols = own_cols.reshape(tgt_blocks, BLK)
        extra_cols = jnp.where(mine_live, extra_cols.reshape(-1), sentinel)
        from_left_msg = shifted(jnp.stack([extra_cols, own_cols[want_right % tgt_blocks]]), "wide", 1)
        from_right_msg = shifted(jnp.stack([extra_cols, own_cols[want_left % tgt_blocks]]), "wide", -1)
        part_from_left2 = shifted(extra_cols, "wide", 2)
        part_from_right2 = shifted(extra_cols, "wide", -2)
        part_from_left, cover_from_left = from_left_msg[0], from_left_msg[1]
        part_from_right, cover_from_right = from_right_msg[0], from_right_msg[1]
        ids = jnp.arange(tgt_blocks, dtype=jnp.int32)[:, None]
        add_right = jnp.where(want_right_live & (ids == want_right % tgt_blocks), part_from_right[None, :], sentinel)
        add_left = jnp.where(want_left_live & (ids == want_left % tgt_blocks), part_from_left[None, :], sentinel)
        top = jnp.maximum(own_cols, jnp.maximum(add_right, add_left))
        total = jnp.exp(own_cols - top) + jnp.exp(add_right - top) + jnp.exp(add_left - top)
        g_blocks = epsilon * (log_tgt - (top + jnp.log(total)))
        g_own = g_blocks.reshape(-1)
        cover_e = jnp.where(mine_from_left, cover_from_left, cover_from_right)
        other = jnp.where(mine_from_left, part_from_left2, part_from_right2)
        other_live = jnp.where(mine_from_left, far_left_same, far_right_same)
        other = jnp.where(other_live, other, sentinel)
        first = jnp.where(mine_from_left, extra_cols, other)
        second = jnp.where(mine_from_left, other, extra_cols)
        top_e = jnp.maximum(cover_e, jnp.maximum(first, second))
        total_e = jnp.exp(cover_e - top_e) + jnp.exp(first - top_e) + jnp.exp(second - top_e)
        g_extra = epsilon * (log_tgt - (top_e + jnp.log(total_e)))

    go, ge = scaled(g_own, g_extra)
    row = narrow_lse(row_lse_call([zo, ze], [go, ge]).reshape(-1), c, narrow_count)
    source_pot = epsilon * (log_src - row)
    place = jnp.array([3, 1, 0, 2], jnp.int32)
    pos = place[(jnp.arange(narrow_count, dtype=jnp.int32) - c) % narrow_count]
    numer = map_call(flag, pos, zo, ze, go, ge, row.reshape(-1, 1), targets, from_left, from_right,
                     tm=sources.shape[0] // narrow_count)

    rows = sources.shape[0]
    quarter = rows // narrow_count
    half = quarter // 2
    chunks = numer.reshape(narrow_count, 2, half, feature_count)
    slot_of = {2: 0, 1: 1, -1: 2, 0: 3}

    def chunk(offset, side):
        return chunks[slot_of[offset], side]

    far_a = shifted(chunk(2, 0), "narrow", 1)
    far_b = shifted(chunk(2, 1), "narrow", -1)
    to_right = jnp.stack([chunk(1, 0) + far_a, chunk(1, 1)])
    to_left = jnp.stack([chunk(-1, 0), chunk(-1, 1) + far_b])
    got_left = shifted(to_right, "narrow", 1)
    got_right = shifted(to_left, "narrow", -1)
    mine_sum = jnp.stack([chunk(0, 0), chunk(0, 1)]) + got_left + got_right
    done = mine_sum.astype(jnp.bfloat16).reshape(quarter, feature_count)
    q_left = shifted(done, "narrow", 1)
    q_right = shifted(done, "narrow", -1)
    far_half_a = shifted(q_left[:half], "narrow", 1)
    far_half_b = shifted(q_right[half:], "narrow", -1)
    q_far = jnp.concatenate([far_half_a, far_half_b])
    mapped = jnp.zeros((rows, feature_count), jnp.bfloat16)
    for k, piece in enumerate((done, q_left, q_far, q_right)):
        mapped = lax.dynamic_update_slice_in_dim(mapped, piece, ((c - k) % narrow_count) * quarter, 0)
    return (source_pot, g_own, mapped)


def solution(mesh):
    placed = (P("wide", None), P(("wide", "narrow"), None), P(), P())
    return jax.shard_map(
        shards,
        mesh=mesh,
        in_specs=placed,
        out_specs=(P("wide"), P(("wide", "narrow")), P("wide", None)),
        check_vma=False,
    )
```

```python
import functools
import math

import jax
import jax.numpy as jnp
from jax import lax
from jax.sharding import PartitionSpec as P
from jax.experimental import pallas as pl
from jax.experimental.pallas import tpu as pltpu

BLK = 1024
ITERS = 2


epsilon = 0.25
sentinel = -1e30


def shifted(x, axis, distance):
    size = lax.axis_size(axis)
    route = [(i, (i + distance) % size) for i in range(size)]
    return lax.ppermute(x, axis, route)


def _row_kernel(*refs):
    n = (len(refs) - 1) // 2
    out_ref = refs[-1]
    scores = [refs[k][...] + refs[n + k][...] for k in range(n)]
    top = scores[0].max(axis=1, keepdims=True)
    for s in scores[1:]:
        top = jnp.maximum(top, s.max(axis=1, keepdims=True))
    total = jnp.sum(jnp.exp(scores[0] - top), axis=1, keepdims=True)
    for s in scores[1:]:
        total = total + jnp.sum(jnp.exp(s - top), axis=1, keepdims=True)
    out_ref[...] = top + jnp.log(total)


def row_lse_call(zs, gs, tm=1024):
    rows = zs[0].shape[0]
    in_specs = [pl.BlockSpec((tm, z.shape[1]), lambda i: (i, 0)) for z in zs]
    in_specs += [pl.BlockSpec((1, g.shape[1]), lambda i: (0, 0)) for g in gs]
    return pl.pallas_call(
        _row_kernel,
        grid=(rows // tm,),
        in_specs=in_specs,
        out_specs=pl.BlockSpec((tm, 1), lambda i: (i, 0)),
        out_shape=jax.ShapeDtypeStruct((rows, 1), jnp.float32),
    )(*zs, *gs)


def _col_kernel(zo_ref, ze_ref, f_ref, oo_ref, oe_ref):
    f = f_ref[...]
    for z_ref, o_ref in ((zo_ref, oo_ref), (ze_ref, oe_ref)):
        s = z_ref[...] + f
        top = s.max(axis=0, keepdims=True)
        o_ref[...] = top + jnp.log(jnp.sum(jnp.exp(s - top), axis=0, keepdims=True))


def col_lse_call(zo, ze, f, steps=2):
    rows = zo.shape[0]
    wo = zo.shape[1] // steps
    we = ze.shape[1] // steps
    return pl.pallas_call(
        _col_kernel,
        grid=(steps,),
        in_specs=[
            pl.BlockSpec((rows, wo), lambda j: (0, j)),
            pl.BlockSpec((rows, we), lambda j: (0, j)),
            pl.BlockSpec((rows, 1), lambda j: (0, 0)),
        ],
        out_specs=[
            pl.BlockSpec((1, wo), lambda j: (0, j)),
            pl.BlockSpec((1, we), lambda j: (0, j)),
        ],
        out_shape=[
            jax.ShapeDtypeStruct((1, zo.shape[1]), jnp.float32),
            jax.ShapeDtypeStruct((1, ze.shape[1]), jnp.float32),
        ],
    )(zo, ze, f)


def _ext_kernel(flag_ref, s_ref, l_ref, r_ref, ge_ref, own_ref, ze_ref, part_ref, *, scale):
    def product(e_ref):
        ze_ref[...] = lax.dot_general(
            s_ref[...], e_ref[...], (((1,), (1,)), ((), ())), preferred_element_type=jnp.float32
        ) * scale

    @pl.when(flag_ref[0] == 1)
    def _():
        product(l_ref)

    @pl.when(flag_ref[0] != 1)
    def _():
        product(r_ref)

    s = ze_ref[...] + ge_ref[...]
    own = own_ref[...]
    top = jnp.maximum(s.max(axis=1, keepdims=True), own)
    part_ref[...] = top + jnp.log(jnp.sum(jnp.exp(s - top), axis=1, keepdims=True) + jnp.exp(own - top))


def ext_call(flag, sources, from_left, from_right, ge, own_part, scale, tm=512):
    rows, feats = sources.shape
    width = from_left.shape[0]
    grid_spec = pltpu.PrefetchScalarGridSpec(
        num_scalar_prefetch=1,
        grid=(rows // tm,),
        in_specs=[
            pl.BlockSpec((tm, feats), lambda i, f: (i, 0)),
            pl.BlockSpec(from_left.shape, lambda i, f: (0, 0)),
            pl.BlockSpec(from_right.shape, lambda i, f: (0, 0)),
            pl.BlockSpec((1, width), lambda i, f: (0, 0)),
            pl.BlockSpec((tm, 1), lambda i, f: (i, 0)),
        ],
        out_specs=[
            pl.BlockSpec((tm, width), lambda i, f: (i, 0)),
            pl.BlockSpec((tm, 1), lambda i, f: (i, 0)),
        ],
    )
    return pl.pallas_call(
        functools.partial(_ext_kernel, scale=scale),
        grid_spec=grid_spec,
        out_shape=[
            jax.ShapeDtypeStruct((rows, width), jnp.float32),
            jax.ShapeDtypeStruct((rows, 1), jnp.float32),
        ],
    )(flag, sources, from_left, from_right, ge, own_part)


def _map_kernel(flag_ref, pos_ref, zo_ref, ze_ref, go_ref, ge_ref, l_ref, to_ref, tl_ref, tr_ref, out_ref):
    lse = l_ref[...]
    wo = jnp.exp(zo_ref[...] + go_ref[...] - lse).astype(jnp.bfloat16)
    we = jnp.exp(ze_ref[...] + ge_ref[...] - lse).astype(jnp.bfloat16)
    out_ref[...] = jnp.dot(wo, to_ref[...], preferred_element_type=jnp.float32)

    @pl.when(flag_ref[0] == 1)
    def _():
        out_ref[...] += jnp.dot(we, tl_ref[...], preferred_element_type=jnp.float32)

    @pl.when(flag_ref[0] != 1)
    def _():
        out_ref[...] += jnp.dot(we, tr_ref[...], preferred_element_type=jnp.float32)


def map_call(flag, pos, zo, ze, go, ge, lse, to, tl, tr, tm=256):
    rows = zo.shape[0]
    feats = to.shape[1]
    grid_spec = pltpu.PrefetchScalarGridSpec(
        num_scalar_prefetch=2,
        grid=(rows // tm,),
        in_specs=[
            pl.BlockSpec((tm, zo.shape[1]), lambda i, f, p: (i, 0)),
            pl.BlockSpec((tm, ze.shape[1]), lambda i, f, p: (i, 0)),
            pl.BlockSpec((1, go.shape[1]), lambda i, f, p: (0, 0)),
            pl.BlockSpec((1, ge.shape[1]), lambda i, f, p: (0, 0)),
            pl.BlockSpec((tm, 1), lambda i, f, p: (i, 0)),
            pl.BlockSpec(to.shape, lambda i, f, p: (0, 0)),
            pl.BlockSpec(tl.shape, lambda i, f, p: (0, 0)),
            pl.BlockSpec(tr.shape, lambda i, f, p: (0, 0)),
        ],
        out_specs=pl.BlockSpec((tm, feats), lambda i, f, p: (p[i], 0)),
    )
    return pl.pallas_call(
        _map_kernel,
        grid_spec=grid_spec,
        out_shape=jax.ShapeDtypeStruct((rows, feats), jnp.float32),
    )(flag, pos, zo, ze, go, ge, lse, to, tl, tr)


def narrow_lse(partial_value, column, narrow_count):
    pieces = [partial_value] + [shifted(partial_value, "narrow", k) for k in range(1, narrow_count)]
    stacked = jnp.stack(pieces)
    order = (column - jnp.arange(narrow_count, dtype=jnp.int32)) % narrow_count
    ordered = stacked[order]
    top = jnp.max(ordered, axis=0)
    return top + jnp.log(jnp.sum(jnp.exp(ordered - top[None, :]), axis=0))


def shards(sources, targets, pair_target, pair_count):
    feature_count = sources.shape[1]
    tgt_blocks = targets.shape[0] // BLK
    wide_count = lax.axis_size("wide")
    narrow_count = lax.axis_size("narrow")
    w = lax.axis_index("wide")
    c = lax.axis_index("narrow")
    group_blocks = tgt_blocks * narrow_count
    scale = (1.0 / math.sqrt(feature_count)) * (1.0 / epsilon)
    inv_eps = 1.0 / epsilon
    log_src = -math.log(wide_count * sources.shape[0])
    log_tgt = -math.log(wide_count * narrow_count * targets.shape[0])

    left = (w - 1 + wide_count) % wide_count
    right = (w + 1) % wide_count
    slot = group_blocks + c

    mine = pair_target[w, slot]
    mine_live = pair_count[w] > slot
    mine_from_left = (mine // group_blocks) == left

    want_right = pair_target[right, slot]
    want_right_live = (pair_count[right] > slot) & ((want_right // group_blocks) == w)
    want_left = pair_target[left, slot]
    want_left_live = (pair_count[left] > slot) & ((want_left // group_blocks) == w)
    left2 = (w - 2 + 2 * wide_count) % wide_count
    right2 = (w + 2) % wide_count
    far_left_same = (pair_count[left2] > slot) & (pair_target[left2, slot] == mine)
    far_right_same = (pair_count[right2] > slot) & (pair_target[right2, slot] == mine)

    blocks = targets.reshape(tgt_blocks, BLK, feature_count)
    to_right = blocks[want_right % tgt_blocks]
    to_left = blocks[want_left % tgt_blocks]
    from_left = shifted(to_right, "wide", 1)
    from_right = shifted(to_left, "wide", -1)

    zo = lax.dot_general(
        sources, targets, (((1,), (1,)), ((), ())), preferred_element_type=jnp.float32
    ) * scale
    extra_mask = jnp.where(mine_live, 0.0, sentinel).astype(jnp.float32)
    flag = mine_from_left.astype(jnp.int32).reshape(1)
    own_width = tgt_blocks * BLK

    def scaled(g_own, g_extra):
        return ((g_own * inv_eps).reshape(1, own_width), (g_extra * inv_eps + extra_mask).reshape(1, BLK))

    g_own = jnp.zeros((own_width,), jnp.float32)
    g_extra = jnp.zeros((BLK,), jnp.float32)
    for iteration in range(ITERS):
        go, ge = scaled(g_own, g_extra)
        if iteration == 0:
            ze, part = ext_call(flag, sources, from_left, from_right, ge, row_lse_call([zo], [go]), scale)
        else:
            part = row_lse_call([zo, ze], [go, ge])
        row = narrow_lse(part.reshape(-1), c, narrow_count)
        f = epsilon * (log_src - row)
        own_cols, extra_cols = col_lse_call(zo, ze, (f * inv_eps).reshape(-1, 1))
        own_cols = own_cols.reshape(tgt_blocks, BLK)
        extra_cols = jnp.where(mine_live, extra_cols.reshape(-1), sentinel)
        from_left_msg = shifted(jnp.stack([extra_cols, own_cols[want_right % tgt_blocks]]), "wide", 1)
        from_right_msg = shifted(jnp.stack([extra_cols, own_cols[want_left % tgt_blocks]]), "wide", -1)
        part_from_left2 = shifted(extra_cols, "wide", 2)
        part_from_right2 = shifted(extra_cols, "wide", -2)
        part_from_left, cover_from_left = from_left_msg[0], from_left_msg[1]
        part_from_right, cover_from_right = from_right_msg[0], from_right_msg[1]
        ids = jnp.arange(tgt_blocks, dtype=jnp.int32)[:, None]
        add_right = jnp.where(want_right_live & (ids == want_right % tgt_blocks), part_from_right[None, :], sentinel)
        add_left = jnp.where(want_left_live & (ids == want_left % tgt_blocks), part_from_left[None, :], sentinel)
        top = jnp.maximum(own_cols, jnp.maximum(add_right, add_left))
        total = jnp.exp(own_cols - top) + jnp.exp(add_right - top) + jnp.exp(add_left - top)
        g_blocks = epsilon * (log_tgt - (top + jnp.log(total)))
        g_own = g_blocks.reshape(-1)
        cover_e = jnp.where(mine_from_left, cover_from_left, cover_from_right)
        other = jnp.where(mine_from_left, part_from_left2, part_from_right2)
        other_live = jnp.where(mine_from_left, far_left_same, far_right_same)
        other = jnp.where(other_live, other, sentinel)
        first = jnp.where(mine_from_left, extra_cols, other)
        second = jnp.where(mine_from_left, other, extra_cols)
        top_e = jnp.maximum(cover_e, jnp.maximum(first, second))
        total_e = jnp.exp(cover_e - top_e) + jnp.exp(first - top_e) + jnp.exp(second - top_e)
        g_extra = epsilon * (log_tgt - (top_e + jnp.log(total_e)))

    go, ge = scaled(g_own, g_extra)
    row = narrow_lse(row_lse_call([zo, ze], [go, ge]).reshape(-1), c, narrow_count)
    source_pot = epsilon * (log_src - row)
    place = jnp.array([3, 1, 0, 2], jnp.int32)
    pos = place[(jnp.arange(narrow_count, dtype=jnp.int32) - c) % narrow_count]
    numer = map_call(flag, pos, zo, ze, go, ge, row.reshape(-1, 1), targets, from_left, from_right,
                     tm=sources.shape[0] // narrow_count)

    rows = sources.shape[0]
    quarter = rows // narrow_count
    half = quarter // 2
    chunks = numer.reshape(narrow_count, 2, half, feature_count)
    slot_of = {2: 0, 1: 1, -1: 2, 0: 3}

    def chunk(offset, side):
        return chunks[slot_of[offset], side]

    far_a = shifted(chunk(2, 0), "narrow", 1)
    far_b = shifted(chunk(2, 1), "narrow", -1)
    to_right = jnp.stack([chunk(1, 0) + far_a, chunk(1, 1)])
    to_left = jnp.stack([chunk(-1, 0), chunk(-1, 1) + far_b])
    got_left = shifted(to_right, "narrow", 1)
    got_right = shifted(to_left, "narrow", -1)
    mine_sum = jnp.stack([chunk(0, 0), chunk(0, 1)]) + got_left + got_right
    done = mine_sum.astype(jnp.bfloat16).reshape(quarter, feature_count)
    q_left = shifted(done, "narrow", 1)
    q_right = shifted(done, "narrow", -1)
    far_half_a = shifted(q_left[:half], "narrow", 1)
    far_half_b = shifted(q_right[half:], "narrow", -1)
    q_far = jnp.concatenate([far_half_a, far_half_b])
    mapped = jnp.zeros((rows, feature_count), jnp.bfloat16)
    for k, piece in enumerate((done, q_left, q_far, q_right)):
        mapped = lax.dynamic_update_slice_in_dim(mapped, piece, ((c - k) % narrow_count) * quarter, 0)
    return (source_pot, g_own, mapped)


def solution(mesh):
    placed = (P("wide", None), P(("wide", "narrow"), None), P(), P())
    return jax.shard_map(
        shards,
        mesh=mesh,
        in_specs=placed,
        out_specs=(P("wide"), P(("wide", "narrow")), P("wide", None)),
        check_vma=False,
    )
```
